32 devices in a mesh: ctx: 16 (over z, y, core), grp: 2 (over x).
Axes of the slice: x: 2, y: 2, z: 4, core: 2. Of those that a mesh axis runs over, the one named last changes fastest.
Arguments:
- projected: bfloat16 [4096, 6144], P(('ctx', 'grp')), may hold values from -6 to 6
- conv_weight: float32 [3, 6144], replicated, may hold values from -2.5 to 2.5
- skip_gain: float32 [2048], replicated, may hold values from 0.5 to 1.5
- spectrum_real: bfloat16 [32, 256, 2048], P('ctx', None, 'grp'), may hold values from -6 to 6
- spectrum_imag: bfloat16 [32, 256, 2048], P('ctx', None, 'grp'), may hold values from -6 to 6
Outputs:
- mixer_out: bfloat16 [4096, 2048], P(('ctx', 'grp'))
The draws below stay inside these ranges and needn't reach their ends.
All inputs are finite; a program needn't handle non-finite values.
Results may differ from the reference program's by a relative error of at most 0.0065.
Values may be sent and summed in bfloat16 or wider, within the bound.
No kernel may reach another device: no remote copies, remote signals or barrier semaphores. Data moves between devices by JAX's collectives and lax.ppermute only.
A program may use at most 64 MiB of HBM per device.

```python
import math
import jax
import jax.numpy as jnp
from jax import lax

D = 2048
KS = 3
BLOCKS = 16
BLOCK = 256
SEQ = 4096
FFT_LEN = 8192


def block_levels(rng, shape, shards, low, largest):
    loudness, own = 1.0, jax.random.fold_in(rng, 6)
    for position, parts in shards:
        heights = jnp.exp(jax.random.uniform(jax.random.fold_in(own, position), (parts,), jnp.float32, low / len(shards), largest / len(shards)))
        loudness = loudness * jnp.repeat(heights, shape[position] // parts).reshape([-1 if axis == position else 1 for axis in range(len(shape))])
    return loudness


def noise(rng, dims, width, bound, cuts=(), held_as=jnp.bfloat16):
    values = width * jax.random.normal(rng, dims, jnp.float32)
    if cuts:
        values = values * block_levels(rng, dims, cuts, -0.22, 0.18)
    return jnp.clip(values, -bound, bound).astype(held_as)


def setup_inputs(seed: int = 0) -> dict:
    keys = jax.random.split(jax.random.key(seed), 6)
    projected = noise(keys[0], (SEQ, 3 * D), 1.0, 6.0, ((0, 32),))
    conv_weight = noise(keys[1], (KS, 3 * D), 0.4, 2.5, (), jnp.float32)
    skip_gain = jnp.clip(jax.random.uniform(keys[2], (D,), jnp.float32, 0.5, 1.5), 0.5, 1.5)
    spectrum_real = noise(keys[3], (2 * BLOCKS, BLOCK, D), 1.0, 6.0, ((0, 16), (2, 2)))
    spectrum_imag = noise(keys[4], (2 * BLOCKS, BLOCK, D), 1.0, 6.0, ((0, 16), (2, 2)))
    return dict(projected=projected, conv_weight=conv_weight, skip_gain=skip_gain, spectrum_real=spectrum_real, spectrum_imag=spectrum_imag)


def reference(projected, conv_weight, skip_gain, spectrum_real, spectrum_imag):
    slab_width = math.gcd(D, 128)
    slab_count = D // slab_width
    rim_rows = KS - 1
    stacked = projected.reshape(SEQ, 3, slab_count, slab_width).transpose(2, 0, 1, 3)
    weights = conv_weight.reshape(KS, 3, slab_count, slab_width).transpose(2, 0, 1, 3)
    gains = skip_gain.reshape(slab_count, slab_width)

    def arrange(spectrum):
        flat = spectrum.transpose(1, 0, 2).reshape(FFT_LEN, slab_count, slab_width)
        return flat.transpose(1, 0, 2)

    def one_slab(operands):
        tokens, kernel, gain, filter_real, filter_imag = operands
        padded = jnp.pad(tokens.astype(jnp.float32), ((rim_rows, 0), (0, 0), (0, 0)))
        short = jnp.zeros((SEQ, 3, slab_width), jnp.float32)
        for offset in range(KS):
            short = short + kernel[offset] * padded[rim_rows - offset:rim_rows - offset + SEQ]
        short = lax.optimization_barrier(short.astype(jnp.bfloat16)).astype(jnp.float32)
        query = short[:, 0]
        gated = short[:, 1] * short[:, 2]
        transformed = jnp.fft.fft(gated, n=FFT_LEN, axis=0)
        response = lax.complex(filter_real.astype(jnp.float32), filter_imag.astype(jnp.float32))
        long_part = jnp.real(jnp.fft.ifft(response * transformed, axis=0))[:SEQ]
        return (query * (long_part + gain * gated)).astype(jnp.bfloat16)

    slabs = lax.map(one_slab, (stacked, weights, gains, arrange(spectrum_real), arrange(spectrum_imag)))
    return slabs.transpose(1, 0, 2).reshape(SEQ, D)
```

```python
import math

import jax
import jax.numpy as jnp
from jax import lax
from jax.sharding import PartitionSpec as P

TWO_PI = 2.0 * math.pi


def shifted(shard, axis, by):
    devices = lax.axis_size(axis)
    pairs = [(i, i + by) for i in range(devices) if 0 <= i + by < devices]
    return lax.ppermute(shard, axis, pairs)


def rotation(rows_index, cols_index, length, direction):
    product = rows_index[:, None] * cols_index[None, :] % length
    angles = product.astype(jnp.float32) * (TWO_PI / length)
    return (jnp.cos(angles), direction * jnp.sin(angles))


def complex_table(cos_part, sin_part):
    return jnp.stack([jnp.stack([cos_part, -sin_part]), jnp.stack([sin_part, cos_part])])


def contract(form, table, data):
    return jnp.einsum(
        form, table, data, precision=lax.Precision.HIGHEST, preferred_element_type=jnp.float32
    )


def twist(data, turn_real, turn_imag):
    return jnp.stack(
        [data[0] * turn_real - data[1] * turn_imag, data[0] * turn_imag + data[1] * turn_real]
    )


def across_forward(blocks, token_index, fft_len):
    block_count = blocks.shape[0]
    frequency = jnp.arange(2 * block_count, dtype=jnp.int32)
    block_order = jnp.arange(block_count, dtype=jnp.int32)
    cos_table, sin_table = rotation(frequency, block_order, 2 * block_count, -1.0)
    accum = contract("pkj,jbc->pkbc", jnp.stack([cos_table, sin_table]), blocks)
    turn_real, turn_imag = rotation(frequency, token_index, fft_len, -1.0)
    return twist(accum, turn_real[:, :, None], turn_imag[:, :, None])


def within_block(data, direction):
    leading, length, lane_count = (data.shape[1], data.shape[2], data.shape[3])
    first_len = math.gcd(length, 256)
    second_len = length // first_len
    data = data.reshape(2, leading, second_len, first_len, lane_count)
    outer_index = jnp.arange(second_len, dtype=jnp.int32)
    inner_index = jnp.arange(first_len, dtype=jnp.int32)
    table_real, table_imag = rotation(outer_index, outer_index, second_len, direction)
    section = contract("pqkj,qxjbc->pxkbc", complex_table(table_real, table_imag), data)
    turn_real, turn_imag = rotation(outer_index, inner_index, length, direction)
    twisted = twist(section, turn_real[None, :, :, None], turn_imag[None, :, :, None])
    last_real, last_imag = rotation(inner_index, inner_index, first_len, direction)
    result = contract("pqgb,qxkbc->pxgkc", complex_table(last_real, last_imag), twisted)
    return result.reshape(2, leading, length, lane_count)


def across_inverse(data, fft_len):
    block_count = data.shape[1] // 2
    block_order = jnp.arange(block_count, dtype=jnp.int32)
    frequency = jnp.arange(2 * block_count, dtype=jnp.int32)
    cos_table, sin_table = rotation(block_order, frequency, 2 * block_count, 1.0)
    summed = contract("qjk,qkbc->jbc", jnp.stack([cos_table, -sin_table]), data)
    return summed * (1.0 / fft_len)


def per_device(projected, conv_weight, skip_gain, spectrum_real, spectrum_imag):
    channels = conv_weight.shape[1] // 3
    rim_rows = conv_weight.shape[0] - 1
    row_count = projected.shape[0]
    rim = shifted(projected[row_count - rim_rows :], ("ctx", "grp"), 1)
    extended = jnp.concatenate([rim, projected], axis=0)
    short = jnp.zeros((row_count, 3 * channels), jnp.float32)
    for offset in range(rim_rows + 1):
        short = short + conv_weight[offset] * extended[
            rim_rows - offset : rim_rows - offset + row_count
        ].astype(jnp.float32)
    short = short.astype(jnp.bfloat16)
    query = short[:, :channels]
    gated = short[:, channels : 2 * channels].astype(jnp.float32) * short[:, 2 * channels :].astype(
        jnp.float32
    )
    block_count = lax.axis_size("ctx")
    group_count = lax.axis_size("grp")
    block_len = row_count * group_count
    fft_len = 2 * block_len * block_count
    block_index = lax.axis_index("ctx")
    sliver = lax.all_to_all(gated, "grp", split_axis=1, concat_axis=0, tiled=True)
    piece_len = block_len // block_count
    token_index = block_index * piece_len + jnp.arange(piece_len, dtype=jnp.int32)
    front = across_forward(
        lax.all_to_all(sliver[None], "ctx", split_axis=1, concat_axis=0, tiled=True),
        token_index,
        fft_len,
    )
    spectra = within_block(
        lax.all_to_all(front, "ctx", split_axis=1, concat_axis=2, tiled=True), -1.0
    )
    filtered = twist(spectra, spectrum_real.astype(jnp.float32), spectrum_imag.astype(jnp.float32))
    restored = within_block(filtered, 1.0)
    local_freq = spectra.shape[1]
    frequency = block_index * local_freq + jnp.arange(local_freq, dtype=jnp.int32)
    turn_real, turn_imag = rotation(frequency, jnp.arange(block_len, dtype=jnp.int32), fft_len, 1.0)
    restored = twist(restored, turn_real[:, :, None], turn_imag[:, :, None])
    long_blocks = across_inverse(
        lax.all_to_all(restored, "ctx", split_axis=2, concat_axis=1, tiled=True), fft_len
    )
    long_sliver = lax.all_to_all(long_blocks, "ctx", split_axis=0, concat_axis=1, tiled=True)[0]
    long_tokens = lax.all_to_all(long_sliver, "grp", split_axis=0, concat_axis=1, tiled=True)
    mixed = query.astype(jnp.float32) * (long_tokens + skip_gain * gated)
    return mixed.astype(jnp.bfloat16)


def short_convolution(projected, conv_weight):
    channels = conv_weight.shape[1] // 3
    rim_rows = conv_weight.shape[0] - 1
    row_count = projected.shape[0]
    rim = shifted(projected[row_count - rim_rows :], ("ctx", "grp"), 1)
    extended = jnp.concatenate([rim, projected], axis=0)
    short = jnp.zeros((row_count, 3 * channels), jnp.float32)
    for offset in range(rim_rows + 1):
        short = short + conv_weight[offset] * extended[
            rim_rows - offset : rim_rows - offset + row_count
        ].astype(jnp.float32)
    short = short.astype(jnp.bfloat16)
    query = short[:, :channels]
    gated = short[:, channels : 2 * channels].astype(jnp.float32) * short[:, 2 * channels :].astype(
        jnp.float32
    )
    return query, gated


def angle_table(rows_index, cols_index, length):
    product = rows_index[:, None] * cols_index[None, :] % length
    angles = product.astype(jnp.float32) * (TWO_PI / length)
    return jnp.cos(angles), jnp.sin(angles)


def channel_parallel(projected, conv_weight, skip_gain, spectrum_real, spectrum_imag):
    query, gated = short_convolution(projected, conv_weight)
    row_count, channels = gated.shape
    block_count = lax.axis_size("ctx")
    group_count = lax.axis_size("grp")
    devices = block_count * group_count
    block_len = row_count * group_count
    residues = 2 * block_count
    fft_len = residues * block_len
    width = channels // devices
    everyone = ("ctx", "grp")

    outgoing = gated.reshape(row_count, group_count, block_count, width).transpose(0, 2, 1, 3)
    outgoing = outgoing.reshape(row_count, devices, width)
    tokens = lax.all_to_all(outgoing, everyone, split_axis=1, concat_axis=0, tiled=True)
    tokens = tokens.reshape(block_count, block_len, width)

    def gather_spectrum(spectrum):
        local = lax.all_to_all(spectrum, "ctx", split_axis=2, concat_axis=0, tiled=True)
        return local.transpose(1, 2, 0).astype(jnp.float32)

    filter_real = gather_spectrum(spectrum_real)
    filter_imag = gather_spectrum(spectrum_imag)

    residue = jnp.arange(residues, dtype=jnp.int32)
    block_order = jnp.arange(block_count, dtype=jnp.int32)
    position = jnp.arange(block_len, dtype=jnp.int32)

    across_cos, across_sin = angle_table(block_order, residue, residues)
    folded_real = contract("jpc,ja->pca", tokens, across_cos)
    folded_imag = -contract("jpc,ja->pca", tokens, across_sin)
    turn_cos, turn_sin = angle_table(position, residue, fft_len)
    turn_cos, turn_sin = turn_cos[:, None, :], turn_sin[:, None, :]
    twisted_real = folded_real * turn_cos + folded_imag * turn_sin
    twisted_imag = folded_imag * turn_cos - folded_real * turn_sin

    within_cos, within_sin = angle_table(position, position, block_len)
    table = jnp.concatenate(
        [
            jnp.concatenate([within_cos, within_sin], axis=1),
            jnp.concatenate([-within_sin, within_cos], axis=1),
        ],
        axis=0,
    )
    lanes = width * residues
    stacked = jnp.concatenate(
        [twisted_real.reshape(block_len, lanes), twisted_imag.reshape(block_len, lanes)], axis=0
    )
    spectra = jnp.dot(table, stacked, precision=lax.Precision.HIGH, preferred_element_type=jnp.float32)
    spectra_real = spectra[:block_len].reshape(block_len, width, residues)
    spectra_imag = spectra[block_len:].reshape(block_len, width, residues)
    product_real = spectra_real * filter_real - spectra_imag * filter_imag
    product_imag = spectra_real * filter_imag + spectra_imag * filter_real
    stacked = jnp.concatenate(
        [product_real.reshape(block_len, lanes), product_imag.reshape(block_len, lanes)], axis=0
    )
    restored = lax.dot_general(
        table,
        stacked,
        (((0,), (0,)), ((), ())),
        precision=lax.Precision.HIGH,
        preferred_element_type=jnp.float32,
    )
    restored_real = restored[:block_len].reshape(block_len, width, residues)
    restored_imag = restored[block_len:].reshape(block_len, width, residues)
    unturned_real = restored_real * turn_cos - restored_imag * turn_sin
    unturned_imag = restored_real * turn_sin + restored_imag * turn_cos
    long_blocks = contract("ja,pca->jpc", across_cos, unturned_real) - contract(
        "ja,pca->jpc", across_sin, unturned_imag
    )
    long_blocks = (long_blocks * (1.0 / fft_len)).reshape(devices, row_count, width)
    returned = lax.all_to_all(long_blocks, everyone, split_axis=0, concat_axis=0, tiled=True)
    returned = returned.reshape(block_count, group_count, row_count, width).transpose(2, 1, 0, 3)
    long_tokens = returned.reshape(row_count, channels)
    mixed = query.astype(jnp.float32) * (long_tokens + skip_gain * gated)
    return mixed.astype(jnp.bfloat16)


def solution(mesh):
    in_specs = (P(("ctx", "grp"), None), P(), P(), P("ctx", None, "grp"), P("ctx", None, "grp"))
    out_specs = P(("ctx", "grp"), None)
    devices = mesh.shape["ctx"] * mesh.shape["grp"]

    def run(projected, conv_weight, skip_gain, spectrum_real, spectrum_imag):
        channels = conv_weight.shape[1] // 3
        wide = channels % devices == 0 and channels // devices >= 32
        body = channel_parallel if wide else per_device
        return jax.shard_map(
            body, mesh=mesh, in_specs=in_specs, out_specs=out_specs, check_vma=False
        )(projected, conv_weight, skip_gain, spectrum_real, spectrum_imag)

    return run
```

```python
import math

import jax
import jax.numpy as jnp
from jax import lax
from jax.sharding import PartitionSpec as P

TWO_PI = 2.0 * math.pi


def shifted(shard, axis, by):
    devices = lax.axis_size(axis)
    pairs = [(i, i + by) for i in range(devices) if 0 <= i + by < devices]
    return lax.ppermute(shard, axis, pairs)


def rotation(rows_index, cols_index, length, direction):
    product = rows_index[:, None] * cols_index[None, :] % length
    angles = product.astype(jnp.float32) * (TWO_PI / length)
    return (jnp.cos(angles), direction * jnp.sin(angles))


def complex_table(cos_part, sin_part):
    return jnp.stack([jnp.stack([cos_part, -sin_part]), jnp.stack([sin_part, cos_part])])


def contract(form, table, data):
    return jnp.einsum(
        form, table, data, precision=lax.Precision.HIGHEST, preferred_element_type=jnp.float32
    )


def twist(data, turn_real, turn_imag):
    return jnp.stack(
        [data[0] * turn_real - data[1] * turn_imag, data[0] * turn_imag + data[1] * turn_real]
    )


def across_forward(blocks, token_index, fft_len):
    block_count = blocks.shape[0]
    frequency = jnp.arange(2 * block_count, dtype=jnp.int32)
    block_order = jnp.arange(block_count, dtype=jnp.int32)
    cos_table, sin_table = rotation(frequency, block_order, 2 * block_count, -1.0)
    accum = contract("pkj,jbc->pkbc", jnp.stack([cos_table, sin_table]), blocks)
    turn_real, turn_imag = rotation(frequency, token_index, fft_len, -1.0)
    return twist(accum, turn_real[:, :, None], turn_imag[:, :, None])


def within_block(data, direction):
    leading, length, lane_count = (data.shape[1], data.shape[2], data.shape[3])
    first_len = math.gcd(length, 256)
    second_len = length // first_len
    data = data.reshape(2, leading, second_len, first_len, lane_count)
    outer_index = jnp.arange(second_len, dtype=jnp.int32)
    inner_index = jnp.arange(first_len, dtype=jnp.int32)
    table_real, table_imag = rotation(outer_index, outer_index, second_len, direction)
    section = contract("pqkj,qxjbc->pxkbc", complex_table(table_real, table_imag), data)
    turn_real, turn_imag = rotation(outer_index, inner_index, length, direction)
    twisted = twist(section, turn_real[None, :, :, None], turn_imag[None, :, :, None])
    last_real, last_imag = rotation(inner_index, inner_index, first_len, direction)
    result = contract("pqgb,qxkbc->pxgkc", complex_table(last_real, last_imag), twisted)
    return result.reshape(2, leading, length, lane_count)


def across_inverse(data, fft_len):
    block_count = data.shape[1] // 2
    block_order = jnp.arange(block_count, dtype=jnp.int32)
    frequency = jnp.arange(2 * block_count, dtype=jnp.int32)
    cos_table, sin_table = rotation(block_order, frequency, 2 * block_count, 1.0)
    summed = contract("qjk,qkbc->jbc", jnp.stack([cos_table, -sin_table]), data)
    return summed * (1.0 / fft_len)


def per_device(projected, conv_weight, skip_gain, spectrum_real, spectrum_imag):
    channels = conv_weight.shape[1] // 3
    rim_rows = conv_weight.shape[0] - 1
    row_count = projected.shape[0]
    rim = shifted(projected[row_count - rim_rows :], ("ctx", "grp"), 1)
    extended = jnp.concatenate([rim, projected], axis=0)
    short = jnp.zeros((row_count, 3 * channels), jnp.float32)
    for offset in range(rim_rows + 1):
        short = short + conv_weight[offset] * extended[
            rim_rows - offset : rim_rows - offset + row_count
        ].astype(jnp.float32)
    short = short.astype(jnp.bfloat16)
    query = short[:, :channels]
    gated = short[:, channels : 2 * channels].astype(jnp.float32) * short[:, 2 * channels :].astype(
        jnp.float32
    )
    block_count = lax.axis_size("ctx")
    group_count = lax.axis_size("grp")
    block_len = row_count * group_count
    fft_len = 2 * block_len * block_count
    block_index = lax.axis_index("ctx")
    sliver = lax.all_to_all(gated, "grp", split_axis=1, concat_axis=0, tiled=True)
    piece_len = block_len // block_count
    token_index = block_index * piece_len + jnp.arange(piece_len, dtype=jnp.int32)
    front = across_forward(
        lax.all_to_all(sliver[None], "ctx", split_axis=1, concat_axis=0, tiled=True),
        token_index,
        fft_len,
    )
    spectra = within_block(
        lax.all_to_all(front, "ctx", split_axis=1, concat_axis=2, tiled=True), -1.0
    )
    filtered = twist(spectra, spectrum_real.astype(jnp.float32), spectrum_imag.astype(jnp.float32))
    restored = within_block(filtered, 1.0)
    local_freq = spectra.shape[1]
    frequency = block_index * local_freq + jnp.arange(local_freq, dtype=jnp.int32)
    turn_real, turn_imag = rotation(frequency, jnp.arange(block_len, dtype=jnp.int32), fft_len, 1.0)
    restored = twist(restored, turn_real[:, :, None], turn_imag[:, :, None])
    long_blocks = across_inverse(
        lax.all_to_all(restored, "ctx", split_axis=2, concat_axis=1, tiled=True), fft_len
    )
    long_sliver = lax.all_to_all(long_blocks, "ctx", split_axis=0, concat_axis=1, tiled=True)[0]
    long_tokens = lax.all_to_all(long_sliver, "grp", split_axis=0, concat_axis=1, tiled=True)
    mixed = query.astype(jnp.float32) * (long_tokens + skip_gain * gated)
    return mixed.astype(jnp.bfloat16)


def short_convolution(projected, conv_weight):
    channels = conv_weight.shape[1] // 3
    rim_rows = conv_weight.shape[0] - 1
    row_count = projected.shape[0]
    rim = shifted(projected[row_count - rim_rows :], ("ctx", "grp"), 1)
    extended = jnp.concatenate([rim, projected], axis=0)
    short = jnp.zeros((row_count, 3 * channels), jnp.float32)
    for offset in range(rim_rows + 1):
        short = short + conv_weight[offset] * extended[
            rim_rows - offset : rim_rows - offset + row_count
        ].astype(jnp.float32)
    short = short.astype(jnp.bfloat16)
    query = short[:, :channels]
    gated = short[:, channels : 2 * channels].astype(jnp.float32) * short[:, 2 * channels :].astype(
        jnp.float32
    )
    return query, gated


def angle_table(rows_index, cols_index, length):
    product = rows_index[:, None] * cols_index[None, :] % length
    angles = product.astype(jnp.float32) * (TWO_PI / length)
    return jnp.cos(angles), jnp.sin(angles)


def channel_parallel(projected, conv_weight, skip_gain, spectrum_real, spectrum_imag):
    query, gated = short_convolution(projected, conv_weight)
    row_count, channels = gated.shape
    block_count = lax.axis_size("ctx")
    group_count = lax.axis_size("grp")
    devices = block_count * group_count
    block_len = row_count * group_count
    residues = 2 * block_count
    fft_len = residues * block_len
    width = channels // devices
    everyone = ("ctx", "grp")

    outgoing = gated.reshape(row_count, group_count, block_count, width).transpose(0, 2, 1, 3)
    outgoing = outgoing.reshape(row_count, devices, width)
    tokens = lax.all_to_all(outgoing, everyone, split_axis=1, concat_axis=0, tiled=True)
    tokens = tokens.reshape(block_count, block_len, width)

    tokens, spectrum = lax.optimization_barrier((tokens, jnp.stack([spectrum_real, spectrum_imag])))
    spectrum = lax.all_to_all(spectrum, "ctx", split_axis=3, concat_axis=1, tiled=True)
    spectrum = spectrum.transpose(0, 2, 3, 1).astype(jnp.float32)
    filter_real, filter_imag = spectrum[0], spectrum[1]

    residue = jnp.arange(residues, dtype=jnp.int32)
    block_order = jnp.arange(block_count, dtype=jnp.int32)
    position = jnp.arange(block_len, dtype=jnp.int32)

    across_cos, across_sin = angle_table(block_order, residue, residues)
    folded_real = contract("jpc,ja->pca", tokens, across_cos)
    folded_imag = -contract("jpc,ja->pca", tokens, across_sin)
    turn_cos, turn_sin = angle_table(position, residue, fft_len)
    turn_cos, turn_sin = turn_cos[:, None, :], turn_sin[:, None, :]
    twisted_real = folded_real * turn_cos + folded_imag * turn_sin
    twisted_imag = folded_imag * turn_cos - folded_real * turn_sin

    within_cos, within_sin = angle_table(position, position, block_len)
    table = jnp.concatenate(
        [
            jnp.concatenate([within_cos, within_sin], axis=1),
            jnp.concatenate([-within_sin, within_cos], axis=1),
        ],
        axis=0,
    )
    lanes = width * residues
    stacked = jnp.concatenate(
        [twisted_real.reshape(block_len, lanes), twisted_imag.reshape(block_len, lanes)], axis=0
    )
    spectra = jnp.dot(table, stacked, precision=lax.Precision.HIGH, preferred_element_type=jnp.float32)
    spectra_real = spectra[:block_len].reshape(block_len, width, residues)
    spectra_imag = spectra[block_len:].reshape(block_len, width, residues)
    product_real = spectra_real * filter_real - spectra_imag * filter_imag
    product_imag = spectra_real * filter_imag + spectra_imag * filter_real
    stacked = jnp.concatenate(
        [product_real.reshape(block_len, lanes), product_imag.reshape(block_len, lanes)], axis=0
    )
    restored = lax.dot_general(
        table,
        stacked,
        (((0,), (0,)), ((), ())),
        precision=lax.Precision.HIGH,
        preferred_element_type=jnp.float32,
    )
    restored_real = restored[:block_len].reshape(block_len, width, residues)
    restored_imag = restored[block_len:].reshape(block_len, width, residues)
    unturned_real = restored_real * turn_cos - restored_imag * turn_sin
    unturned_imag = restored_real * turn_sin + restored_imag * turn_cos
    long_blocks = contract("ja,pca->jpc", across_cos, unturned_real) - contract(
        "ja,pca->jpc", across_sin, unturned_imag
    )
    long_blocks = (long_blocks * (1.0 / fft_len)).reshape(devices, row_count, width)
    long_blocks = long_blocks.astype(jnp.bfloat16)
    returned = lax.all_to_all(long_blocks, everyone, split_axis=0, concat_axis=0, tiled=True)
    returned = returned.astype(jnp.float32)
    returned = returned.reshape(block_count, group_count, row_count, width).transpose(2, 1, 0, 3)
    long_tokens = returned.reshape(row_count, channels)
    mixed = query.astype(jnp.float32) * (long_tokens + skip_gain * gated)
    return mixed.astype(jnp.bfloat16)


def solution(mesh):
    in_specs = (P(("ctx", "grp"), None), P(), P(), P("ctx", None, "grp"), P("ctx", None, "grp"))
    out_specs = P(("ctx", "grp"), None)
    devices = mesh.shape["ctx"] * mesh.shape["grp"]

    def run(projected, conv_weight, skip_gain, spectrum_real, spectrum_imag):
        channels = conv_weight.shape[1] // 3
        wide = channels % devices == 0 and channels // devices >= 32
        body = channel_parallel if wide else per_device
        return jax.shard_map(
            body, mesh=mesh, in_specs=in_specs, out_specs=out_specs, check_vma=False
        )(projected, conv_weight, skip_gain, spectrum_real, spectrum_imag)

    return run
```

```python
import math

import jax
import jax.numpy as jnp
from jax import lax
from jax.sharding import PartitionSpec as P

TWO_PI = 2.0 * math.pi


def shifted(shard, axis, by):
    devices = lax.axis_size(axis)
    pairs = [(i, i + by) for i in range(devices) if 0 <= i + by < devices]
    return lax.ppermute(shard, axis, pairs)


def rotation(rows_index, cols_index, length, direction):
    product = rows_index[:, None] * cols_index[None, :] % length
    angles = product.astype(jnp.float32) * (TWO_PI / length)
    return (jnp.cos(angles), direction * jnp.sin(angles))


def complex_table(cos_part, sin_part):
    return jnp.stack([jnp.stack([cos_part, -sin_part]), jnp.stack([sin_part, cos_part])])


def contract(form, table, data):
    return jnp.einsum(
        form, table, data, precision=lax.Precision.HIGHEST, preferred_element_type=jnp.float32
    )


def twist(data, turn_real, turn_imag):
    return jnp.stack(
        [data[0] * turn_real - data[1] * turn_imag, data[0] * turn_imag + data[1] * turn_real]
    )


def across_forward(blocks, token_index, fft_len):
    block_count = blocks.shape[0]
    frequency = jnp.arange(2 * block_count, dtype=jnp.int32)
    block_order = jnp.arange(block_count, dtype=jnp.int32)
    cos_table, sin_table = rotation(frequency, block_order, 2 * block_count, -1.0)
    accum = contract("pkj,jbc->pkbc", jnp.stack([cos_table, sin_table]), blocks)
    turn_real, turn_imag = rotation(frequency, token_index, fft_len, -1.0)
    return twist(accum, turn_real[:, :, None], turn_imag[:, :, None])


def within_block(data, direction):
    leading, length, lane_count = (data.shape[1], data.shape[2], data.shape[3])
    first_len = math.gcd(length, 256)
    second_len = length // first_len
    data = data.reshape(2, leading, second_len, first_len, lane_count)
    outer_index = jnp.arange(second_len, dtype=jnp.int32)
    inner_index = jnp.arange(first_len, dtype=jnp.int32)
    table_real, table_imag = rotation(outer_index, outer_index, second_len, direction)
    section = contract("pqkj,qxjbc->pxkbc", complex_table(table_real, table_imag), data)
    turn_real, turn_imag = rotation(outer_index, inner_index, length, direction)
    twisted = twist(section, turn_real[None, :, :, None], turn_imag[None, :, :, None])
    last_real, last_imag = rotation(inner_index, inner_index, first_len, direction)
    result = contract("pqgb,qxkbc->pxgkc", complex_table(last_real, last_imag), twisted)
    return result.reshape(2, leading, length, lane_count)


def across_inverse(data, fft_len):
    block_count = data.shape[1] // 2
    block_order = jnp.arange(block_count, dtype=jnp.int32)
    frequency = jnp.arange(2 * block_count, dtype=jnp.int32)
    cos_table, sin_table = rotation(block_order, frequency, 2 * block_count, 1.0)
    summed = contract("qjk,qkbc->jbc", jnp.stack([cos_table, -sin_table]), data)
    return summed * (1.0 / fft_len)


def per_device(projected, conv_weight, skip_gain, spectrum_real, spectrum_imag):
    channels = conv_weight.shape[1] // 3
    rim_rows = conv_weight.shape[0] - 1
    row_count = projected.shape[0]
    rim = shifted(projected[row_count - rim_rows :], ("ctx", "grp"), 1)
    extended = jnp.concatenate([rim, projected], axis=0)
    short = jnp.zeros((row_count, 3 * channels), jnp.float32)
    for offset in range(rim_rows + 1):
        short = short + conv_weight[offset] * extended[
            rim_rows - offset : rim_rows - offset + row_count
        ].astype(jnp.float32)
    short = short.astype(jnp.bfloat16)
    query = short[:, :channels]
    gated = short[:, channels : 2 * channels].astype(jnp.float32) * short[:, 2 * channels :].astype(
        jnp.float32
    )
    block_count = lax.axis_size("ctx")
    group_count = lax.axis_size("grp")
    block_len = row_count * group_count
    fft_len = 2 * block_len * block_count
    block_index = lax.axis_index("ctx")
    sliver = lax.all_to_all(gated, "grp", split_axis=1, concat_axis=0, tiled=True)
    piece_len = block_len // block_count
    token_index = block_index * piece_len + jnp.arange(piece_len, dtype=jnp.int32)
    front = across_forward(
        lax.all_to_all(sliver[None], "ctx", split_axis=1, concat_axis=0, tiled=True),
        token_index,
        fft_len,
    )
    spectra = within_block(
        lax.all_to_all(front, "ctx", split_axis=1, concat_axis=2, tiled=True), -1.0
    )
    filtered = twist(spectra, spectrum_real.astype(jnp.float32), spectrum_imag.astype(jnp.float32))
    restored = within_block(filtered, 1.0)
    local_freq = spectra.shape[1]
    frequency = block_index * local_freq + jnp.arange(local_freq, dtype=jnp.int32)
    turn_real, turn_imag = rotation(frequency, jnp.arange(block_len, dtype=jnp.int32), fft_len, 1.0)
    restored = twist(restored, turn_real[:, :, None], turn_imag[:, :, None])
    long_blocks = across_inverse(
        lax.all_to_all(restored, "ctx", split_axis=2, concat_axis=1, tiled=True), fft_len
    )
    long_sliver = lax.all_to_all(long_blocks, "ctx", split_axis=0, concat_axis=1, tiled=True)[0]
    long_tokens = lax.all_to_all(long_sliver, "grp", split_axis=0, concat_axis=1, tiled=True)
    mixed = query.astype(jnp.float32) * (long_tokens + skip_gain * gated)
    return mixed.astype(jnp.bfloat16)


def short_convolution(projected, conv_weight):
    channels = conv_weight.shape[1] // 3
    rim_rows = conv_weight.shape[0] - 1
    row_count = projected.shape[0]
    rim = shifted(projected[row_count - rim_rows :], ("ctx", "grp"), 1)
    extended = jnp.concatenate([rim, projected], axis=0)
    short = jnp.zeros((row_count, 3 * channels), jnp.float32)
    for offset in range(rim_rows + 1):
        short = short + conv_weight[offset] * extended[
            rim_rows - offset : rim_rows - offset + row_count
        ].astype(jnp.float32)
    short = short.astype(jnp.bfloat16)
    query = short[:, :channels]
    gated = short[:, channels : 2 * channels].astype(jnp.float32) * short[:, 2 * channels :].astype(
        jnp.float32
    )
    return query, gated


def angle_table(rows_index, cols_index, length):
    product = rows_index[:, None] * cols_index[None, :] % length
    angles = product.astype(jnp.float32) * (TWO_PI / length)
    return jnp.cos(angles), jnp.sin(angles)


def channel_parallel(projected, conv_weight, skip_gain, spectrum_real, spectrum_imag):
    query, gated = short_convolution(projected, conv_weight)
    row_count, channels = gated.shape
    block_count = lax.axis_size("ctx")
    group_count = lax.axis_size("grp")
    devices = block_count * group_count
    block_len = row_count * group_count
    residues = 2 * block_count
    fft_len = residues * block_len
    width = channels // devices
    everyone = ("ctx", "grp")

    outgoing = gated.reshape(row_count, group_count, block_count, width).transpose(0, 2, 1, 3)
    outgoing = outgoing.reshape(row_count, devices, width)
    outgoing = outgoing.astype(jnp.bfloat16)
    tokens = lax.all_to_all(outgoing, everyone, split_axis=1, concat_axis=0, tiled=True)
    tokens = tokens.reshape(block_count, block_len, width).astype(jnp.float32)

    local_residues, spectrum_len, half = spectrum_real.shape
    spectrum = jnp.stack([spectrum_real, spectrum_imag])
    spectrum = spectrum.reshape(2, local_residues, spectrum_len, block_count, width)
    spectrum = spectrum.transpose(3, 0, 1, 2, 4)
    share = 2 * local_residues * spectrum_len * width
    lane = 128 if share % 128 == 0 else width
    spectrum = spectrum.reshape(block_count, share // lane, lane)
    tokens, spectrum = lax.optimization_barrier((tokens, spectrum))
    spectrum = lax.all_to_all(spectrum, "ctx", split_axis=0, concat_axis=0, tiled=True)
    spectrum = spectrum.reshape(block_count, 2, local_residues, spectrum_len, width)
    spectrum = spectrum.transpose(1, 3, 4, 0, 2).reshape(2, spectrum_len, width, residues)
    spectrum = spectrum.astype(jnp.float32)
    filter_real, filter_imag = spectrum[0], spectrum[1]

    residue = jnp.arange(residues, dtype=jnp.int32)
    block_order = jnp.arange(block_count, dtype=jnp.int32)
    position = jnp.arange(block_len, dtype=jnp.int32)

    across_cos, across_sin = angle_table(block_order, residue, residues)
    folded_real = contract("jpc,ja->pca", tokens, across_cos)
    folded_imag = -contract("jpc,ja->pca", tokens, across_sin)
    turn_cos, turn_sin = angle_table(position, residue, fft_len)
    turn_cos, turn_sin = turn_cos[:, None, :], turn_sin[:, None, :]
    twisted_real = folded_real * turn_cos + folded_imag * turn_sin
    twisted_imag = folded_imag * turn_cos - folded_real * turn_sin

    within_cos, within_sin = angle_table(position, position, block_len)
    table = jnp.concatenate(
        [
            jnp.concatenate([within_cos, within_sin], axis=1),
            jnp.concatenate([-within_sin, within_cos], axis=1),
        ],
        axis=0,
    )
    lanes = width * residues
    stacked = jnp.concatenate(
        [twisted_real.reshape(block_len, lanes), twisted_imag.reshape(block_len, lanes)], axis=0
    )
    spectra = jnp.dot(table, stacked, precision=lax.Precision.HIGH, preferred_element_type=jnp.float32)
    spectra_real = spectra[:block_len].reshape(block_len, width, residues)
    spectra_imag = spectra[block_len:].reshape(block_len, width, residues)
    product_real = spectra_real * filter_real - spectra_imag * filter_imag
    product_imag = spectra_real * filter_imag + spectra_imag * filter_real
    stacked = jnp.concatenate(
        [product_real.reshape(block_len, lanes), product_imag.reshape(block_len, lanes)], axis=0
    )
    restored = lax.dot_general(
        table,
        stacked,
        (((0,), (0,)), ((), ())),
        precision=lax.Precision.HIGH,
        preferred_element_type=jnp.float32,
    )
    restored_real = restored[:block_len].reshape(block_len, width, residues)
    restored_imag = restored[block_len:].reshape(block_len, width, residues)
    unturned_real = restored_real * turn_cos - restored_imag * turn_sin
    unturned_imag = restored_real * turn_sin + restored_imag * turn_cos
    long_blocks = contract("ja,pca->jpc", across_cos, unturned_real) - contract(
        "ja,pca->jpc", across_sin, unturned_imag
    )
    long_blocks = (long_blocks * (1.0 / fft_len)).reshape(devices, row_count, width)
    long_blocks = long_blocks.astype(jnp.bfloat16)
    returned = lax.all_to_all(long_blocks, everyone, split_axis=0, concat_axis=0, tiled=True)
    returned = returned.astype(jnp.float32)
    returned = returned.reshape(block_count, group_count, row_count, width).transpose(2, 1, 0, 3)
    long_tokens = returned.reshape(row_count, channels)
    mixed = query.astype(jnp.float32) * (long_tokens + skip_gain * gated)
    return mixed.astype(jnp.bfloat16)


def solution(mesh):
    in_specs = (P(("ctx", "grp"), None), P(), P(), P("ctx", None, "grp"), P("ctx", None, "grp"))
    out_specs = P(("ctx", "grp"), None)
    devices = mesh.shape["ctx"] * mesh.shape["grp"]

    def run(projected, conv_weight, skip_gain, spectrum_real, spectrum_imag):
        channels = conv_weight.shape[1] // 3
        wide = channels % devices == 0 and channels // devices >= 32
        body = channel_parallel if wide else per_device
        return jax.shard_map(
            body, mesh=mesh, in_specs=in_specs, out_specs=out_specs, check_vma=False
        )(projected, conv_weight, skip_gain, spectrum_real, spectrum_imag)

    return run
```

```python
import math

import jax
import jax.numpy as jnp
from jax import lax
from jax.sharding import PartitionSpec as P

TWO_PI = 2.0 * math.pi


def shifted(shard, axis, by):
    devices = lax.axis_size(axis)
    pairs = [(i, i + by) for i in range(devices) if 0 <= i + by < devices]
    return lax.ppermute(shard, axis, pairs)


def rotation(rows_index, cols_index, length, direction):
    product = rows_index[:, None] * cols_index[None, :] % length
    angles = product.astype(jnp.float32) * (TWO_PI / length)
    return (jnp.cos(angles), direction * jnp.sin(angles))


def complex_table(cos_part, sin_part):
    return jnp.stack([jnp.stack([cos_part, -sin_part]), jnp.stack([sin_part, cos_part])])


def contract(form, table, data):
    return jnp.einsum(
        form, table, data, precision=lax.Precision.HIGHEST, preferred_element_type=jnp.float32
    )


def twist(data, turn_real, turn_imag):
    return jnp.stack(
        [data[0] * turn_real - data[1] * turn_imag, data[0] * turn_imag + data[1] * turn_real]
    )


def across_forward(blocks, token_index, fft_len):
    block_count = blocks.shape[0]
    frequency = jnp.arange(2 * block_count, dtype=jnp.int32)
    block_order = jnp.arange(block_count, dtype=jnp.int32)
    cos_table, sin_table = rotation(frequency, block_order, 2 * block_count, -1.0)
    accum = contract("pkj,jbc->pkbc", jnp.stack([cos_table, sin_table]), blocks)
    turn_real, turn_imag = rotation(frequency, token_index, fft_len, -1.0)
    return twist(accum, turn_real[:, :, None], turn_imag[:, :, None])


def within_block(data, direction):
    leading, length, lane_count = (data.shape[1], data.shape[2], data.shape[3])
    first_len = math.gcd(length, 256)
    second_len = length // first_len
    data = data.reshape(2, leading, second_len, first_len, lane_count)
    outer_index = jnp.arange(second_len, dtype=jnp.int32)
    inner_index = jnp.arange(first_len, dtype=jnp.int32)
    table_real, table_imag = rotation(outer_index, outer_index, second_len, direction)
    section = contract("pqkj,qxjbc->pxkbc", complex_table(table_real, table_imag), data)
    turn_real, turn_imag = rotation(outer_index, inner_index, length, direction)
    twisted = twist(section, turn_real[None, :, :, None], turn_imag[None, :, :, None])
    last_real, last_imag = rotation(inner_index, inner_index, first_len, direction)
    result = contract("pqgb,qxkbc->pxgkc", complex_table(last_real, last_imag), twisted)
    return result.reshape(2, leading, length, lane_count)


def across_inverse(data, fft_len):
    block_count = data.shape[1] // 2
    block_order = jnp.arange(block_count, dtype=jnp.int32)
    frequency = jnp.arange(2 * block_count, dtype=jnp.int32)
    cos_table, sin_table = rotation(block_order, frequency, 2 * block_count, 1.0)
    summed = contract("qjk,qkbc->jbc", jnp.stack([cos_table, -sin_table]), data)
    return summed * (1.0 / fft_len)


def per_device(projected, conv_weight, skip_gain, spectrum_real, spectrum_imag):
    channels = conv_weight.shape[1] // 3
    rim_rows = conv_weight.shape[0] - 1
    row_count = projected.shape[0]
    rim = shifted(projected[row_count - rim_rows :], ("ctx", "grp"), 1)
    extended = jnp.concatenate([rim, projected], axis=0)
    short = jnp.zeros((row_count, 3 * channels), jnp.float32)
    for offset in range(rim_rows + 1):
        short = short + conv_weight[offset] * extended[
            rim_rows - offset : rim_rows - offset + row_count
        ].astype(jnp.float32)
    short = short.astype(jnp.bfloat16)
    query = short[:, :channels]
    gated = short[:, channels : 2 * channels].astype(jnp.float32) * short[:, 2 * channels :].astype(
        jnp.float32
    )
    block_count = lax.axis_size("ctx")
    group_count = lax.axis_size("grp")
    block_len = row_count * group_count
    fft_len = 2 * block_len * block_count
    block_index = lax.axis_index("ctx")
    sliver = lax.all_to_all(gated, "grp", split_axis=1, concat_axis=0, tiled=True)
    piece_len = block_len // block_count
    token_index = block_index * piece_len + jnp.arange(piece_len, dtype=jnp.int32)
    front = across_forward(
        lax.all_to_all(sliver[None], "ctx", split_axis=1, concat_axis=0, tiled=True),
        token_index,
        fft_len,
    )
    spectra = within_block(
        lax.all_to_all(front, "ctx", split_axis=1, concat_axis=2, tiled=True), -1.0
    )
    filtered = twist(spectra, spectrum_real.astype(jnp.float32), spectrum_imag.astype(jnp.float32))
    restored = within_block(filtered, 1.0)
    local_freq = spectra.shape[1]
    frequency = block_index * local_freq + jnp.arange(local_freq, dtype=jnp.int32)
    turn_real, turn_imag = rotation(frequency, jnp.arange(block_len, dtype=jnp.int32), fft_len, 1.0)
    restored = twist(restored, turn_real[:, :, None], turn_imag[:, :, None])
    long_blocks = across_inverse(
        lax.all_to_all(restored, "ctx", split_axis=2, concat_axis=1, tiled=True), fft_len
    )
    long_sliver = lax.all_to_all(long_blocks, "ctx", split_axis=0, concat_axis=1, tiled=True)[0]
    long_tokens = lax.all_to_all(long_sliver, "grp", split_axis=0, concat_axis=1, tiled=True)
    mixed = query.astype(jnp.float32) * (long_tokens + skip_gain * gated)
    return mixed.astype(jnp.bfloat16)


def short_convolution(projected, conv_weight):
    channels = conv_weight.shape[1] // 3
    rim_rows = conv_weight.shape[0] - 1
    row_count = projected.shape[0]
    rim = shifted(projected[row_count - rim_rows :], ("ctx", "grp"), 1)
    extended = jnp.concatenate([rim, projected], axis=0)
    short = jnp.zeros((row_count, 3 * channels), jnp.float32)
    for offset in range(rim_rows + 1):
        short = short + conv_weight[offset] * extended[
            rim_rows - offset : rim_rows - offset + row_count
        ].astype(jnp.float32)
    short = short.astype(jnp.bfloat16)
    query = short[:, :channels]
    gated = short[:, channels : 2 * channels].astype(jnp.float32) * short[:, 2 * channels :].astype(
        jnp.float32
    )
    return query, gated


def angle_table(rows_index, cols_index, length):
    product = rows_index[:, None] * cols_index[None, :] % length
    angles = product.astype(jnp.float32) * (TWO_PI / length)
    return jnp.cos(angles), jnp.sin(angles)


def channel_parallel(projected, conv_weight, skip_gain, spectrum_real, spectrum_imag):
    query, gated = short_convolution(projected, conv_weight)
    row_count, channels = gated.shape
    block_count = lax.axis_size("ctx")
    group_count = lax.axis_size("grp")
    devices = block_count * group_count
    block_len = row_count * group_count
    residues = 2 * block_count
    fft_len = residues * block_len
    width = channels // devices
    everyone = ("ctx", "grp")

    outgoing = gated.reshape(row_count, group_count, block_count, width).transpose(0, 2, 1, 3)
    outgoing = outgoing.reshape(row_count, devices, width)
    outgoing = outgoing.astype(jnp.bfloat16)
    tokens = lax.all_to_all(outgoing, everyone, split_axis=1, concat_axis=0, tiled=True)
    tokens = tokens.reshape(block_count, block_len, width).astype(jnp.float32)

    tokens, spectrum = lax.optimization_barrier((tokens, jnp.stack([spectrum_real, spectrum_imag])))
    spectrum = lax.all_to_all(spectrum, "ctx", split_axis=3, concat_axis=1, tiled=True)
    spectrum = spectrum.transpose(0, 2, 3, 1).astype(jnp.float32)
    filter_real, filter_imag = spectrum[0], spectrum[1]

    residue = jnp.arange(residues, dtype=jnp.int32)
    block_order = jnp.arange(block_count, dtype=jnp.int32)
    position = jnp.arange(block_len, dtype=jnp.int32)

    across_cos, across_sin = angle_table(block_order, residue, residues)
    folded_real = contract("jpc,ja->pca", tokens, across_cos)
    folded_imag = -contract("jpc,ja->pca", tokens, across_sin)
    turn_cos, turn_sin = angle_table(position, residue, fft_len)
    turn_cos, turn_sin = turn_cos[:, None, :], turn_sin[:, None, :]
    twisted_real = folded_real * turn_cos + folded_imag * turn_sin
    twisted_imag = folded_imag * turn_cos - folded_real * turn_sin

    within_cos, within_sin = angle_table(position, position, block_len)
    lanes = width * residues

    def times(table_part, data):
        return lax.dot_general(
            table_part,
            data.reshape(block_len, lanes),
            (((1,), (0,)), ((), ())),
            precision=lax.Precision.HIGH,
            preferred_element_type=jnp.float32,
        ).reshape(block_len, width, residues)

    spectra_real = times(within_cos, twisted_real) + times(within_sin, twisted_imag)
    spectra_imag = times(within_cos, twisted_imag) - times(within_sin, twisted_real)
    product_real = spectra_real * filter_real - spectra_imag * filter_imag
    product_imag = spectra_real * filter_imag + spectra_imag * filter_real
    restored_real = times(within_cos, product_real) - times(within_sin, product_imag)
    restored_imag = times(within_cos, product_imag) + times(within_sin, product_real)
    unturned_real = restored_real * turn_cos - restored_imag * turn_sin
    unturned_imag = restored_real * turn_sin + restored_imag * turn_cos
    long_blocks = contract("ja,pca->jpc", across_cos, unturned_real) - contract(
        "ja,pca->jpc", across_sin, unturned_imag
    )
    long_blocks = (long_blocks * (1.0 / fft_len)).reshape(devices, row_count, width)
    long_blocks = long_blocks.astype(jnp.bfloat16)
    returned = lax.all_to_all(long_blocks, everyone, split_axis=0, concat_axis=0, tiled=True)
    returned = returned.astype(jnp.float32)
    returned = returned.reshape(block_count, group_count, row_count, width).transpose(2, 1, 0, 3)
    long_tokens = returned.reshape(row_count, channels)
    mixed = query.astype(jnp.float32) * (long_tokens + skip_gain * gated)
    return mixed.astype(jnp.bfloat16)


def solution(mesh):
    in_specs = (P(("ctx", "grp"), None), P(), P(), P("ctx", None, "grp"), P("ctx", None, "grp"))
    out_specs = P(("ctx", "grp"), None)
    devices = mesh.shape["ctx"] * mesh.shape["grp"]

    def run(projected, conv_weight, skip_gain, spectrum_real, spectrum_imag):
        channels = conv_weight.shape[1] // 3
        wide = channels % devices == 0 and channels // devices >= 32
        body = channel_parallel if wide else per_device
        return jax.shard_map(
            body, mesh=mesh, in_specs=in_specs, out_specs=out_specs, check_vma=False
        )(projected, conv_weight, skip_gain, spectrum_real, spectrum_imag)

    return run
```

```python
import math

import jax
import jax.numpy as jnp
from jax import lax
from jax.sharding import PartitionSpec as P

TWO_PI = 2.0 * math.pi


def shifted(shard, axis, by):
    devices = lax.axis_size(axis)
    pairs = [(i, i + by) for i in range(devices) if 0 <= i + by < devices]
    return lax.ppermute(shard, axis, pairs)


def rotation(rows_index, cols_index, length, direction):
    product = rows_index[:, None] * cols_index[None, :] % length
    angles = product.astype(jnp.float32) * (TWO_PI / length)
    return (jnp.cos(angles), direction * jnp.sin(angles))


def complex_table(cos_part, sin_part):
    return jnp.stack([jnp.stack([cos_part, -sin_part]), jnp.stack([sin_part, cos_part])])


def contract(form, table, data):
    return jnp.einsum(
        form, table, data, precision=lax.Precision.HIGHEST, preferred_element_type=jnp.float32
    )


def twist(data, turn_real, turn_imag):
    return jnp.stack(
        [data[0] * turn_real - data[1] * turn_imag, data[0] * turn_imag + data[1] * turn_real]
    )


def across_forward(blocks, token_index, fft_len):
    block_count = blocks.shape[0]
    frequency = jnp.arange(2 * block_count, dtype=jnp.int32)
    block_order = jnp.arange(block_count, dtype=jnp.int32)
    cos_table, sin_table = rotation(frequency, block_order, 2 * block_count, -1.0)
    accum = contract("pkj,jbc->pkbc", jnp.stack([cos_table, sin_table]), blocks)
    turn_real, turn_imag = rotation(frequency, token_index, fft_len, -1.0)
    return twist(accum, turn_real[:, :, None], turn_imag[:, :, None])


def within_block(data, direction):
    leading, length, lane_count = (data.shape[1], data.shape[2], data.shape[3])
    first_len = math.gcd(length, 256)
    second_len = length // first_len
    data = data.reshape(2, leading, second_len, first_len, lane_count)
    outer_index = jnp.arange(second_len, dtype=jnp.int32)
    inner_index = jnp.arange(first_len, dtype=jnp.int32)
    table_real, table_imag = rotation(outer_index, outer_index, second_len, direction)
    section = contract("pqkj,qxjbc->pxkbc", complex_table(table_real, table_imag), data)
    turn_real, turn_imag = rotation(outer_index, inner_index, length, direction)
    twisted = twist(section, turn_real[None, :, :, None], turn_imag[None, :, :, None])
    last_real, last_imag = rotation(inner_index, inner_index, first_len, direction)
    result = contract("pqgb,qxkbc->pxgkc", complex_table(last_real, last_imag), twisted)
    return result.reshape(2, leading, length, lane_count)


def across_inverse(data, fft_len):
    block_count = data.shape[1] // 2
    block_order = jnp.arange(block_count, dtype=jnp.int32)
    frequency = jnp.arange(2 * block_count, dtype=jnp.int32)
    cos_table, sin_table = rotation(block_order, frequency, 2 * block_count, 1.0)
    summed = contract("qjk,qkbc->jbc", jnp.stack([cos_table, -sin_table]), data)
    return summed * (1.0 / fft_len)


def per_device(projected, conv_weight, skip_gain, spectrum_real, spectrum_imag):
    channels = conv_weight.shape[1] // 3
    rim_rows = conv_weight.shape[0] - 1
    row_count = projected.shape[0]
    rim = shifted(projected[row_count - rim_rows :], ("ctx", "grp"), 1)
    extended = jnp.concatenate([rim, projected], axis=0)
    short = jnp.zeros((row_count, 3 * channels), jnp.float32)
    for offset in range(rim_rows + 1):
        short = short + conv_weight[offset] * extended[
            rim_rows - offset : rim_rows - offset + row_count
        ].astype(jnp.float32)
    short = short.astype(jnp.bfloat16)
    query = short[:, :channels]
    gated = short[:, channels : 2 * channels].astype(jnp.float32) * short[:, 2 * channels :].astype(
        jnp.float32
    )
    block_count = lax.axis_size("ctx")
    group_count = lax.axis_size("grp")
    block_len = row_count * group_count
    fft_len = 2 * block_len * block_count
    block_index = lax.axis_index("ctx")
    sliver = lax.all_to_all(gated, "grp", split_axis=1, concat_axis=0, tiled=True)
    piece_len = block_len // block_count
    token_index = block_index * piece_len + jnp.arange(piece_len, dtype=jnp.int32)
    front = across_forward(
        lax.all_to_all(sliver[None], "ctx", split_axis=1, concat_axis=0, tiled=True),
        token_index,
        fft_len,
    )
    spectra = within_block(
        lax.all_to_all(front, "ctx", split_axis=1, concat_axis=2, tiled=True), -1.0
    )
    filtered = twist(spectra, spectrum_real.astype(jnp.float32), spectrum_imag.astype(jnp.float32))
    restored = within_block(filtered, 1.0)
    local_freq = spectra.shape[1]
    frequency = block_index * local_freq + jnp.arange(local_freq, dtype=jnp.int32)
    turn_real, turn_imag = rotation(frequency, jnp.arange(block_len, dtype=jnp.int32), fft_len, 1.0)
    restored = twist(restored, turn_real[:, :, None], turn_imag[:, :, None])
    long_blocks = across_inverse(
        lax.all_to_all(restored, "ctx", split_axis=2, concat_axis=1, tiled=True), fft_len
    )
    long_sliver = lax.all_to_all(long_blocks, "ctx", split_axis=0, concat_axis=1, tiled=True)[0]
    long_tokens = lax.all_to_all(long_sliver, "grp", split_axis=0, concat_axis=1, tiled=True)
    mixed = query.astype(jnp.float32) * (long_tokens + skip_gain * gated)
    return mixed.astype(jnp.bfloat16)


def short_convolution(projected, conv_weight):
    channels = conv_weight.shape[1] // 3
    rim_rows = conv_weight.shape[0] - 1
    row_count = projected.shape[0]
    rim = shifted(projected[row_count - rim_rows :], ("ctx", "grp"), 1)
    extended = jnp.concatenate([rim, projected], axis=0)
    short = jnp.zeros((row_count, 3 * channels), jnp.float32)
    for offset in range(rim_rows + 1):
        short = short + conv_weight[offset] * extended[
            rim_rows - offset : rim_rows - offset + row_count
        ].astype(jnp.float32)
    short = short.astype(jnp.bfloat16)
    query = short[:, :channels]
    gated = short[:, channels : 2 * channels].astype(jnp.float32) * short[:, 2 * channels :].astype(
        jnp.float32
    )
    return query, gated


def angle_table(rows_index, cols_index, length):
    product = rows_index[:, None] * cols_index[None, :] % length
    angles = product.astype(jnp.float32) * (TWO_PI / length)
    return jnp.cos(angles), jnp.sin(angles)


def channel_parallel(projected, conv_weight, skip_gain, spectrum_real, spectrum_imag):
    query, gated = short_convolution(projected, conv_weight)
    row_count, channels = gated.shape
    block_count = lax.axis_size("ctx")
    group_count = lax.axis_size("grp")
    devices = block_count * group_count
    block_len = row_count * group_count
    residues = 2 * block_count
    fft_len = residues * block_len
    width = channels // devices
    everyone = ("ctx", "grp")

    outgoing = gated.reshape(row_count, group_count, block_count, width).transpose(0, 2, 1, 3)
    outgoing = outgoing.reshape(row_count, devices, width)
    outgoing = outgoing.astype(jnp.bfloat16)
    tokens = lax.all_to_all(outgoing, everyone, split_axis=1, concat_axis=0, tiled=True)
    tokens = tokens.reshape(block_count, block_len, width).astype(jnp.float32)

    tokens, spectrum = lax.optimization_barrier((tokens, jnp.stack([spectrum_real, spectrum_imag])))
    spectrum = lax.all_to_all(spectrum, "ctx", split_axis=3, concat_axis=1, tiled=True)
    spectrum = spectrum.transpose(0, 2, 3, 1).astype(jnp.float32)
    filter_real, filter_imag = spectrum[0], spectrum[1]

    residue = jnp.arange(residues, dtype=jnp.int32)
    block_order = jnp.arange(block_count, dtype=jnp.int32)
    position = jnp.arange(block_len, dtype=jnp.int32)
    middle = residues // 2

    mirror_real = jnp.flip(filter_real[:, :, middle + 1 :], axis=(0, 2))
    mirror_imag = jnp.flip(filter_imag[:, :, middle + 1 :], axis=(0, 2))
    nothing = jnp.zeros_like(filter_real[:, :, :1])
    paired_real = filter_real[:, :, :middle] + jnp.concatenate([nothing, mirror_real], axis=2)
    paired_imag = filter_imag[:, :, :middle] - jnp.concatenate([nothing, mirror_imag], axis=2)
    single_real = filter_real[:, :, middle]
    single_imag = filter_imag[:, :, middle]

    across_cos, across_sin = angle_table(block_order, residue, residues)
    turn_cos, turn_sin = angle_table(position, residue, fft_len)
    within_cos, within_sin = angle_table(position, position, block_len)

    def times(table_part, data):
        return lax.dot_general(
            table_part,
            data.reshape(block_len, -1),
            (((1,), (0,)), ((), ())),
            precision=lax.Precision.HIGH,
            preferred_element_type=jnp.float32,
        ).reshape(data.shape)

    def filtered(twisted_real, twisted_imag, weight_real, weight_imag, unturn_cos, unturn_sin):
        spectra_real = times(within_cos, twisted_real) + times(within_sin, twisted_imag)
        spectra_imag = times(within_cos, twisted_imag) - times(within_sin, twisted_real)
        product_real = spectra_real * weight_real - spectra_imag * weight_imag
        product_imag = spectra_real * weight_imag + spectra_imag * weight_real
        restored_real = times(within_cos, product_real) - times(within_sin, product_imag)
        restored_imag = times(within_cos, product_imag) + times(within_sin, product_real)
        unturned_real = restored_real * unturn_cos - restored_imag * unturn_sin
        unturned_imag = restored_real * unturn_sin + restored_imag * unturn_cos
        return unturned_real, unturned_imag

    paired_cos, paired_sin = across_cos[:, :middle], across_sin[:, :middle]
    folded_real = contract("jpc,ja->pca", tokens, paired_cos)
    folded_imag = -contract("jpc,ja->pca", tokens, paired_sin)
    half_cos, half_sin = turn_cos[:, None, :middle], turn_sin[:, None, :middle]
    unturned_real, unturned_imag = filtered(
        folded_real * half_cos + folded_imag * half_sin,
        folded_imag * half_cos - folded_real * half_sin,
        paired_real,
        paired_imag,
        half_cos,
        half_sin,
    )
    long_blocks = contract("ja,pca->jpc", paired_cos, unturned_real) - contract(
        "ja,pca->jpc", paired_sin, unturned_imag
    )

    alternate = across_cos[:, middle]
    folded_single = contract("jpc,j->pc", tokens, alternate)
    single_cos, single_sin = turn_cos[:, middle : middle + 1], turn_sin[:, middle : middle + 1]
    single_part, _ = filtered(
        folded_single * single_cos,
        -folded_single * single_sin,
        single_real,
        single_imag,
        single_cos,
        single_sin,
    )
    long_blocks = long_blocks + alternate[:, None, None] * single_part[None]
    long_blocks = (long_blocks * (1.0 / fft_len)).reshape(devices, row_count, width)
    long_blocks = long_blocks.astype(jnp.bfloat16)
    returned = lax.all_to_all(long_blocks, everyone, split_axis=0, concat_axis=0, tiled=True)
    returned = returned.astype(jnp.float32)
    returned = returned.reshape(block_count, group_count, row_count, width).transpose(2, 1, 0, 3)
    long_tokens = returned.reshape(row_count, channels)
    mixed = query.astype(jnp.float32) * (long_tokens + skip_gain * gated)
    return mixed.astype(jnp.bfloat16)


def solution(mesh):
    in_specs = (P(("ctx", "grp"), None), P(), P(), P("ctx", None, "grp"), P("ctx", None, "grp"))
    out_specs = P(("ctx", "grp"), None)
    devices = mesh.shape["ctx"] * mesh.shape["grp"]

    def run(projected, conv_weight, skip_gain, spectrum_real, spectrum_imag):
        channels = conv_weight.shape[1] // 3
        wide = channels % devices == 0 and channels // devices >= 32
        body = channel_parallel if wide else per_device
        return jax.shard_map(
            body, mesh=mesh, in_specs=in_specs, out_specs=out_specs, check_vma=False
        )(projected, conv_weight, skip_gain, spectrum_real, spectrum_imag)

    return run
```

```python
import math

import jax
import jax.numpy as jnp
from jax import lax
from jax.sharding import PartitionSpec as P

TWO_PI = 2.0 * math.pi


def shifted(shard, axis, by):
    devices = lax.axis_size(axis)
    pairs = [(i, i + by) for i in range(devices) if 0 <= i + by < devices]
    return lax.ppermute(shard, axis, pairs)


def rotation(rows_index, cols_index, length, direction):
    product = rows_index[:, None] * cols_index[None, :] % length
    angles = product.astype(jnp.float32) * (TWO_PI / length)
    return (jnp.cos(angles), direction * jnp.sin(angles))


def complex_table(cos_part, sin_part):
    return jnp.stack([jnp.stack([cos_part, -sin_part]), jnp.stack([sin_part, cos_part])])


def contract(form, table, data):
    return jnp.einsum(
        form, table, data, precision=lax.Precision.HIGHEST, preferred_element_type=jnp.float32
    )


def twist(data, turn_real, turn_imag):
    return jnp.stack(
        [data[0] * turn_real - data[1] * turn_imag, data[0] * turn_imag + data[1] * turn_real]
    )


def across_forward(blocks, token_index, fft_len):
    block_count = blocks.shape[0]
    frequency = jnp.arange(2 * block_count, dtype=jnp.int32)
    block_order = jnp.arange(block_count, dtype=jnp.int32)
    cos_table, sin_table = rotation(frequency, block_order, 2 * block_count, -1.0)
    accum = contract("pkj,jbc->pkbc", jnp.stack([cos_table, sin_table]), blocks)
    turn_real, turn_imag = rotation(frequency, token_index, fft_len, -1.0)
    return twist(accum, turn_real[:, :, None], turn_imag[:, :, None])


def within_block(data, direction):
    leading, length, lane_count = (data.shape[1], data.shape[2], data.shape[3])
    first_len = math.gcd(length, 256)
    second_len = length // first_len
    data = data.reshape(2, leading, second_len, first_len, lane_count)
    outer_index = jnp.arange(second_len, dtype=jnp.int32)
    inner_index = jnp.arange(first_len, dtype=jnp.int32)
    table_real, table_imag = rotation(outer_index, outer_index, second_len, direction)
    section = contract("pqkj,qxjbc->pxkbc", complex_table(table_real, table_imag), data)
    turn_real, turn_imag = rotation(outer_index, inner_index, length, direction)
    twisted = twist(section, turn_real[None, :, :, None], turn_imag[None, :, :, None])
    last_real, last_imag = rotation(inner_index, inner_index, first_len, direction)
    result = contract("pqgb,qxkbc->pxgkc", complex_table(last_real, last_imag), twisted)
    return result.reshape(2, leading, length, lane_count)


def across_inverse(data, fft_len):
    block_count = data.shape[1] // 2
    block_order = jnp.arange(block_count, dtype=jnp.int32)
    frequency = jnp.arange(2 * block_count, dtype=jnp.int32)
    cos_table, sin_table = rotation(block_order, frequency, 2 * block_count, 1.0)
    summed = contract("qjk,qkbc->jbc", jnp.stack([cos_table, -sin_table]), data)
    return summed * (1.0 / fft_len)


def per_device(projected, conv_weight, skip_gain, spectrum_real, spectrum_imag):
    channels = conv_weight.shape[1] // 3
    rim_rows = conv_weight.shape[0] - 1
    row_count = projected.shape[0]
    rim = shifted(projected[row_count - rim_rows :], ("ctx", "grp"), 1)
    extended = jnp.concatenate([rim, projected], axis=0)
    short = jnp.zeros((row_count, 3 * channels), jnp.float32)
    for offset in range(rim_rows + 1):
        short = short + conv_weight[offset] * extended[
            rim_rows - offset : rim_rows - offset + row_count
        ].astype(jnp.float32)
    short = short.astype(jnp.bfloat16)
    query = short[:, :channels]
    gated = short[:, channels : 2 * channels].astype(jnp.float32) * short[:, 2 * channels :].astype(
        jnp.float32
    )
    block_count = lax.axis_size("ctx")
    group_count = lax.axis_size("grp")
    block_len = row_count * group_count
    fft_len = 2 * block_len * block_count
    block_index = lax.axis_index("ctx")
    sliver = lax.all_to_all(gated, "grp", split_axis=1, concat_axis=0, tiled=True)
    piece_len = block_len // block_count
    token_index = block_index * piece_len + jnp.arange(piece_len, dtype=jnp.int32)
    front = across_forward(
        lax.all_to_all(sliver[None], "ctx", split_axis=1, concat_axis=0, tiled=True),
        token_index,
        fft_len,
    )
    spectra = within_block(
        lax.all_to_all(front, "ctx", split_axis=1, concat_axis=2, tiled=True), -1.0
    )
    filtered = twist(spectra, spectrum_real.astype(jnp.float32), spectrum_imag.astype(jnp.float32))
    restored = within_block(filtered, 1.0)
    local_freq = spectra.shape[1]
    frequency = block_index * local_freq + jnp.arange(local_freq, dtype=jnp.int32)
    turn_real, turn_imag = rotation(frequency, jnp.arange(block_len, dtype=jnp.int32), fft_len, 1.0)
    restored = twist(restored, turn_real[:, :, None], turn_imag[:, :, None])
    long_blocks = across_inverse(
        lax.all_to_all(restored, "ctx", split_axis=2, concat_axis=1, tiled=True), fft_len
    )
    long_sliver = lax.all_to_all(long_blocks, "ctx", split_axis=0, concat_axis=1, tiled=True)[0]
    long_tokens = lax.all_to_all(long_sliver, "grp", split_axis=0, concat_axis=1, tiled=True)
    mixed = query.astype(jnp.float32) * (long_tokens + skip_gain * gated)
    return mixed.astype(jnp.bfloat16)


def short_convolution(projected, conv_weight):
    channels = conv_weight.shape[1] // 3
    rim_rows = conv_weight.shape[0] - 1
    row_count = projected.shape[0]
    rim = shifted(projected[row_count - rim_rows :], ("ctx", "grp"), 1)
    extended = jnp.concatenate([rim, projected], axis=0)
    short = jnp.zeros((row_count, 3 * channels), jnp.float32)
    for offset in range(rim_rows + 1):
        short = short + conv_weight[offset] * extended[
            rim_rows - offset : rim_rows - offset + row_count
        ].astype(jnp.float32)
    short = short.astype(jnp.bfloat16)
    query = short[:, :channels]
    gated = short[:, channels : 2 * channels].astype(jnp.float32) * short[:, 2 * channels :].astype(
        jnp.float32
    )
    return query, gated


def angle_table(rows_index, cols_index, length):
    product = rows_index[:, None] * cols_index[None, :] % length
    angles = product.astype(jnp.float32) * (TWO_PI / length)
    return jnp.cos(angles), jnp.sin(angles)


def channel_parallel(projected, conv_weight, skip_gain, spectrum_real, spectrum_imag):
    query, gated = short_convolution(projected, conv_weight)
    row_count, channels = gated.shape
    block_count = lax.axis_size("ctx")
    group_count = lax.axis_size("grp")
    devices = block_count * group_count
    block_len = row_count * group_count
    residues = 2 * block_count
    fft_len = residues * block_len
    width = channels // devices
    everyone = ("ctx", "grp")

    outgoing = gated.reshape(row_count, group_count, block_count, width).transpose(0, 2, 1, 3)
    outgoing = outgoing.reshape(row_count, devices, width)
    outgoing = outgoing.astype(jnp.bfloat16)
    tokens = lax.all_to_all(outgoing, everyone, split_axis=1, concat_axis=0, tiled=True)
    tokens = tokens.reshape(block_count, block_len, width).astype(jnp.float32)

    tokens, spectrum = lax.optimization_barrier((tokens, jnp.stack([spectrum_real, spectrum_imag])))
    spectrum = lax.all_to_all(spectrum, "ctx", split_axis=3, concat_axis=1, tiled=True)
    spectrum = spectrum.transpose(0, 2, 3, 1).astype(jnp.float32)
    filter_real, filter_imag = spectrum[0], spectrum[1]

    residue = jnp.arange(residues, dtype=jnp.int32)
    block_order = jnp.arange(block_count, dtype=jnp.int32)
    position = jnp.arange(block_len, dtype=jnp.int32)

    across_cos, across_sin = angle_table(block_order, residue, residues)
    folded_real = contract("jpc,ja->pca", tokens, across_cos)
    folded_imag = -contract("jpc,ja->pca", tokens, across_sin)
    turn_cos, turn_sin = angle_table(position, residue, fft_len)
    turn_cos, turn_sin = turn_cos[:, None, :], turn_sin[:, None, :]
    twisted_real = folded_real * turn_cos + folded_imag * turn_sin
    twisted_imag = folded_imag * turn_cos - folded_real * turn_sin

    within_cos, within_sin = angle_table(position, position, block_len)
    lanes = width * residues

    def times(table_part, data, precision=lax.Precision.HIGH):
        return lax.dot_general(
            table_part,
            data.reshape(block_len, lanes),
            (((1,), (0,)), ((), ())),
            precision=precision,
            preferred_element_type=jnp.float32,
        ).reshape(block_len, width, residues)

    def inverse(table_part, data):
        return times(table_part, data, lax.Precision.DEFAULT)

    spectra_real = times(within_cos, twisted_real) + times(within_sin, twisted_imag)
    spectra_imag = times(within_cos, twisted_imag) - times(within_sin, twisted_real)
    product_real = spectra_real * filter_real - spectra_imag * filter_imag
    product_imag = spectra_real * filter_imag + spectra_imag * filter_real
    restored_real = inverse(within_cos, product_real) - inverse(within_sin, product_imag)
    restored_imag = inverse(within_cos, product_imag) + inverse(within_sin, product_real)
    unturned_real = restored_real * turn_cos - restored_imag * turn_sin
    unturned_imag = restored_real * turn_sin + restored_imag * turn_cos
    long_blocks = contract("ja,pca->jpc", across_cos, unturned_real) - contract(
        "ja,pca->jpc", across_sin, unturned_imag
    )
    long_blocks = (long_blocks * (1.0 / fft_len)).reshape(devices, row_count, width)
    long_blocks = long_blocks.astype(jnp.bfloat16)
    returned = lax.all_to_all(long_blocks, everyone, split_axis=0, concat_axis=0, tiled=True)
    returned = returned.astype(jnp.float32)
    returned = returned.reshape(block_count, group_count, row_count, width).transpose(2, 1, 0, 3)
    long_tokens = returned.reshape(row_count, channels)
    mixed = query.astype(jnp.float32) * (long_tokens + skip_gain * gated)
    return mixed.astype(jnp.bfloat16)


def solution(mesh):
    in_specs = (P(("ctx", "grp"), None), P(), P(), P("ctx", None, "grp"), P("ctx", None, "grp"))
    out_specs = P(("ctx", "grp"), None)
    devices = mesh.shape["ctx"] * mesh.shape["grp"]

    def run(projected, conv_weight, skip_gain, spectrum_real, spectrum_imag):
        channels = conv_weight.shape[1] // 3
        wide = channels % devices == 0 and channels // devices >= 32
        body = channel_parallel if wide else per_device
        return jax.shard_map(
            body, mesh=mesh, in_specs=in_specs, out_specs=out_specs, check_vma=False
        )(projected, conv_weight, skip_gain, spectrum_real, spectrum_imag)

    return run
```

```python
import math

import jax
import jax.numpy as jnp
from jax import lax
from jax.sharding import PartitionSpec as P

TWO_PI = 2.0 * math.pi


def shifted(shard, axis, by):
    devices = lax.axis_size(axis)
    pairs = [(i, i + by) for i in range(devices) if 0 <= i + by < devices]
    return lax.ppermute(shard, axis, pairs)


def rotation(rows_index, cols_index, length, direction):
    product = rows_index[:, None] * cols_index[None, :] % length
    angles = product.astype(jnp.float32) * (TWO_PI / length)
    return (jnp.cos(angles), direction * jnp.sin(angles))


def complex_table(cos_part, sin_part):
    return jnp.stack([jnp.stack([cos_part, -sin_part]), jnp.stack([sin_part, cos_part])])


def contract(form, table, data, precision=lax.Precision.HIGHEST):
    return jnp.einsum(form, table, data, precision=precision, preferred_element_type=jnp.float32)


def contract_high(form, table, data):
    return contract(form, table, data, lax.Precision.HIGH)


def twist(data, turn_real, turn_imag):
    return jnp.stack(
        [data[0] * turn_real - data[1] * turn_imag, data[0] * turn_imag + data[1] * turn_real]
    )


def across_forward(blocks, token_index, fft_len):
    block_count = blocks.shape[0]
    frequency = jnp.arange(2 * block_count, dtype=jnp.int32)
    block_order = jnp.arange(block_count, dtype=jnp.int32)
    cos_table, sin_table = rotation(frequency, block_order, 2 * block_count, -1.0)
    accum = contract("pkj,jbc->pkbc", jnp.stack([cos_table, sin_table]), blocks)
    turn_real, turn_imag = rotation(frequency, token_index, fft_len, -1.0)
    return twist(accum, turn_real[:, :, None], turn_imag[:, :, None])


def within_block(data, direction):
    leading, length, lane_count = (data.shape[1], data.shape[2], data.shape[3])
    first_len = math.gcd(length, 256)
    second_len = length // first_len
    data = data.reshape(2, leading, second_len, first_len, lane_count)
    outer_index = jnp.arange(second_len, dtype=jnp.int32)
    inner_index = jnp.arange(first_len, dtype=jnp.int32)
    table_real, table_imag = rotation(outer_index, outer_index, second_len, direction)
    section = contract("pqkj,qxjbc->pxkbc", complex_table(table_real, table_imag), data)
    turn_real, turn_imag = rotation(outer_index, inner_index, length, direction)
    twisted = twist(section, turn_real[None, :, :, None], turn_imag[None, :, :, None])
    last_real, last_imag = rotation(inner_index, inner_index, first_len, direction)
    result = contract("pqgb,qxkbc->pxgkc", complex_table(last_real, last_imag), twisted)
    return result.reshape(2, leading, length, lane_count)


def across_inverse(data, fft_len):
    block_count = data.shape[1] // 2
    block_order = jnp.arange(block_count, dtype=jnp.int32)
    frequency = jnp.arange(2 * block_count, dtype=jnp.int32)
    cos_table, sin_table = rotation(block_order, frequency, 2 * block_count, 1.0)
    summed = contract("qjk,qkbc->jbc", jnp.stack([cos_table, -sin_table]), data)
    return summed * (1.0 / fft_len)


def per_device(projected, conv_weight, skip_gain, spectrum_real, spectrum_imag):
    channels = conv_weight.shape[1] // 3
    rim_rows = conv_weight.shape[0] - 1
    row_count = projected.shape[0]
    rim = shifted(projected[row_count - rim_rows :], ("ctx", "grp"), 1)
    extended = jnp.concatenate([rim, projected], axis=0)
    short = jnp.zeros((row_count, 3 * channels), jnp.float32)
    for offset in range(rim_rows + 1):
        short = short + conv_weight[offset] * extended[
            rim_rows - offset : rim_rows - offset + row_count
        ].astype(jnp.float32)
    short = short.astype(jnp.bfloat16)
    query = short[:, :channels]
    gated = short[:, channels : 2 * channels].astype(jnp.float32) * short[:, 2 * channels :].astype(
        jnp.float32
    )
    block_count = lax.axis_size("ctx")
    group_count = lax.axis_size("grp")
    block_len = row_count * group_count
    fft_len = 2 * block_len * block_count
    block_index = lax.axis_index("ctx")
    sliver = lax.all_to_all(gated, "grp", split_axis=1, concat_axis=0, tiled=True)
    piece_len = block_len // block_count
    token_index = block_index * piece_len + jnp.arange(piece_len, dtype=jnp.int32)
    front = across_forward(
        lax.all_to_all(sliver[None], "ctx", split_axis=1, concat_axis=0, tiled=True),
        token_index,
        fft_len,
    )
    spectra = within_block(
        lax.all_to_all(front, "ctx", split_axis=1, concat_axis=2, tiled=True), -1.0
    )
    filtered = twist(spectra, spectrum_real.astype(jnp.float32), spectrum_imag.astype(jnp.float32))
    restored = within_block(filtered, 1.0)
    local_freq = spectra.shape[1]
    frequency = block_index * local_freq + jnp.arange(local_freq, dtype=jnp.int32)
    turn_real, turn_imag = rotation(frequency, jnp.arange(block_len, dtype=jnp.int32), fft_len, 1.0)
    restored = twist(restored, turn_real[:, :, None], turn_imag[:, :, None])
    long_blocks = across_inverse(
        lax.all_to_all(restored, "ctx", split_axis=2, concat_axis=1, tiled=True), fft_len
    )
    long_sliver = lax.all_to_all(long_blocks, "ctx", split_axis=0, concat_axis=1, tiled=True)[0]
    long_tokens = lax.all_to_all(long_sliver, "grp", split_axis=0, concat_axis=1, tiled=True)
    mixed = query.astype(jnp.float32) * (long_tokens + skip_gain * gated)
    return mixed.astype(jnp.bfloat16)


def short_convolution(projected, conv_weight):
    channels = conv_weight.shape[1] // 3
    rim_rows = conv_weight.shape[0] - 1
    row_count = projected.shape[0]
    rim = shifted(projected[row_count - rim_rows :], ("ctx", "grp"), 1)
    extended = jnp.concatenate([rim, projected], axis=0)
    short = jnp.zeros((row_count, 3 * channels), jnp.float32)
    for offset in range(rim_rows + 1):
        short = short + conv_weight[offset] * extended[
            rim_rows - offset : rim_rows - offset + row_count
        ].astype(jnp.float32)
    short = short.astype(jnp.bfloat16)
    query = short[:, :channels]
    gated = short[:, channels : 2 * channels].astype(jnp.float32) * short[:, 2 * channels :].astype(
        jnp.float32
    )
    return query, gated


def angle_table(rows_index, cols_index, length):
    product = rows_index[:, None] * cols_index[None, :] % length
    angles = product.astype(jnp.float32) * (TWO_PI / length)
    return jnp.cos(angles), jnp.sin(angles)


def channel_parallel(projected, conv_weight, skip_gain, spectrum_real, spectrum_imag):
    query, gated = short_convolution(projected, conv_weight)
    row_count, channels = gated.shape
    block_count = lax.axis_size("ctx")
    group_count = lax.axis_size("grp")
    devices = block_count * group_count
    block_len = row_count * group_count
    residues = 2 * block_count
    fft_len = residues * block_len
    width = channels // devices
    everyone = ("ctx", "grp")

    outgoing = gated.reshape(row_count, group_count, block_count, width).transpose(0, 2, 1, 3)
    outgoing = outgoing.reshape(row_count, devices, width)
    outgoing = outgoing.astype(jnp.bfloat16)
    tokens = lax.all_to_all(outgoing, everyone, split_axis=1, concat_axis=0, tiled=True)
    tokens = tokens.reshape(block_count, block_len, width).astype(jnp.float32)

    tokens, spectrum = lax.optimization_barrier((tokens, jnp.stack([spectrum_real, spectrum_imag])))
    spectrum = lax.all_to_all(spectrum, "ctx", split_axis=3, concat_axis=1, tiled=True)
    spectrum = spectrum.transpose(0, 2, 3, 1).astype(jnp.float32)
    filter_real, filter_imag = spectrum[0], spectrum[1]

    residue = jnp.arange(residues, dtype=jnp.int32)
    block_order = jnp.arange(block_count, dtype=jnp.int32)
    position = jnp.arange(block_len, dtype=jnp.int32)

    across_cos, across_sin = angle_table(block_order, residue, residues)
    folded_real = contract_high("jpc,ja->pca", tokens, across_cos)
    folded_imag = -contract_high("jpc,ja->pca", tokens, across_sin)
    turn_cos, turn_sin = angle_table(position, residue, fft_len)
    turn_cos, turn_sin = turn_cos[:, None, :], turn_sin[:, None, :]
    twisted_real = folded_real * turn_cos + folded_imag * turn_sin
    twisted_imag = folded_imag * turn_cos - folded_real * turn_sin

    within_cos, within_sin = angle_table(position, position, block_len)
    lanes = width * residues

    def times(table_part, data, precision=lax.Precision.HIGH):
        return lax.dot_general(
            table_part,
            data.reshape(block_len, lanes),
            (((1,), (0,)), ((), ())),
            precision=precision,
            preferred_element_type=jnp.float32,
        ).reshape(block_len, width, residues)

    def inverse(table_part, data):
        return times(table_part, data, lax.Precision.DEFAULT)

    spectra_real = times(within_cos, twisted_real) + times(within_sin, twisted_imag)
    spectra_imag = times(within_cos, twisted_imag) - times(within_sin, twisted_real)
    product_real = spectra_real * filter_real - spectra_imag * filter_imag
    product_imag = spectra_real * filter_imag + spectra_imag * filter_real
    restored_real = inverse(within_cos, product_real) - inverse(within_sin, product_imag)
    restored_imag = inverse(within_cos, product_imag) + inverse(within_sin, product_real)
    unturned_real = restored_real * turn_cos - restored_imag * turn_sin
    unturned_imag = restored_real * turn_sin + restored_imag * turn_cos
    long_blocks = contract_high("ja,pca->jpc", across_cos, unturned_real) - contract_high(
        "ja,pca->jpc", across_sin, unturned_imag
    )
    long_blocks = (long_blocks * (1.0 / fft_len)).reshape(devices, row_count, width)
    long_blocks = long_blocks.astype(jnp.bfloat16)
    returned = lax.all_to_all(long_blocks, everyone, split_axis=0, concat_axis=0, tiled=True)
    returned = returned.astype(jnp.float32)
    returned = returned.reshape(block_count, group_count, row_count, width).transpose(2, 1, 0, 3)
    long_tokens = returned.reshape(row_count, channels)
    mixed = query.astype(jnp.float32) * (long_tokens + skip_gain * gated)
    return mixed.astype(jnp.bfloat16)


def solution(mesh):
    in_specs = (P(("ctx", "grp"), None), P(), P(), P("ctx", None, "grp"), P("ctx", None, "grp"))
    out_specs = P(("ctx", "grp"), None)
    devices = mesh.shape["ctx"] * mesh.shape["grp"]

    def run(projected, conv_weight, skip_gain, spectrum_real, spectrum_imag):
        channels = conv_weight.shape[1] // 3
        wide = channels % devices == 0 and channels // devices >= 32
        body = channel_parallel if wide else per_device
        return jax.shard_map(
            body, mesh=mesh, in_specs=in_specs, out_specs=out_specs, check_vma=False
        )(projected, conv_weight, skip_gain, spectrum_real, spectrum_imag)

    return run
```

```python
import math

import jax
import jax.numpy as jnp
from jax import lax
from jax.sharding import PartitionSpec as P

TWO_PI = 2.0 * math.pi


def shifted(shard, axis, by):
    devices = lax.axis_size(axis)
    pairs = [(i, i + by) for i in range(devices) if 0 <= i + by < devices]
    return lax.ppermute(shard, axis, pairs)


def rotation(rows_index, cols_index, length, direction):
    product = rows_index[:, None] * cols_index[None, :] % length
    angles = product.astype(jnp.float32) * (TWO_PI / length)
    return (jnp.cos(angles), direction * jnp.sin(angles))


def complex_table(cos_part, sin_part):
    return jnp.stack([jnp.stack([cos_part, -sin_part]), jnp.stack([sin_part, cos_part])])


def contract(form, table, data, precision=lax.Precision.HIGHEST):
    return jnp.einsum(form, table, data, precision=precision, preferred_element_type=jnp.float32)


def contract_high(form, table, data):
    return contract(form, table, data, lax.Precision.HIGH)


def twist(data, turn_real, turn_imag):
    return jnp.stack(
        [data[0] * turn_real - data[1] * turn_imag, data[0] * turn_imag + data[1] * turn_real]
    )


def across_forward(blocks, token_index, fft_len):
    block_count = blocks.shape[0]
    frequency = jnp.arange(2 * block_count, dtype=jnp.int32)
    block_order = jnp.arange(block_count, dtype=jnp.int32)
    cos_table, sin_table = rotation(frequency, block_order, 2 * block_count, -1.0)
    accum = contract("pkj,jbc->pkbc", jnp.stack([cos_table, sin_table]), blocks)
    turn_real, turn_imag = rotation(frequency, token_index, fft_len, -1.0)
    return twist(accum, turn_real[:, :, None], turn_imag[:, :, None])


def within_block(data, direction):
    leading, length, lane_count = (data.shape[1], data.shape[2], data.shape[3])
    first_len = math.gcd(length, 256)
    second_len = length // first_len
    data = data.reshape(2, leading, second_len, first_len, lane_count)
    outer_index = jnp.arange(second_len, dtype=jnp.int32)
    inner_index = jnp.arange(first_len, dtype=jnp.int32)
    table_real, table_imag = rotation(outer_index, outer_index, second_len, direction)
    section = contract("pqkj,qxjbc->pxkbc", complex_table(table_real, table_imag), data)
    turn_real, turn_imag = rotation(outer_index, inner_index, length, direction)
    twisted = twist(section, turn_real[None, :, :, None], turn_imag[None, :, :, None])
    last_real, last_imag = rotation(inner_index, inner_index, first_len, direction)
    result = contract("pqgb,qxkbc->pxgkc", complex_table(last_real, last_imag), twisted)
    return result.reshape(2, leading, length, lane_count)


def across_inverse(data, fft_len):
    block_count = data.shape[1] // 2
    block_order = jnp.arange(block_count, dtype=jnp.int32)
    frequency = jnp.arange(2 * block_count, dtype=jnp.int32)
    cos_table, sin_table = rotation(block_order, frequency, 2 * block_count, 1.0)
    summed = contract("qjk,qkbc->jbc", jnp.stack([cos_table, -sin_table]), data)
    return summed * (1.0 / fft_len)


def per_device(projected, conv_weight, skip_gain, spectrum_real, spectrum_imag):
    channels = conv_weight.shape[1] // 3
    rim_rows = conv_weight.shape[0] - 1
    row_count = projected.shape[0]
    rim = shifted(projected[row_count - rim_rows :], ("ctx", "grp"), 1)
    extended = jnp.concatenate([rim, projected], axis=0)
    short = jnp.zeros((row_count, 3 * channels), jnp.float32)
    for offset in range(rim_rows + 1):
        short = short + conv_weight[offset] * extended[
            rim_rows - offset : rim_rows - offset + row_count
        ].astype(jnp.float32)
    short = short.astype(jnp.bfloat16)
    query = short[:, :channels]
    gated = short[:, channels : 2 * channels].astype(jnp.float32) * short[:, 2 * channels :].astype(
        jnp.float32
    )
    block_count = lax.axis_size("ctx")
    group_count = lax.axis_size("grp")
    block_len = row_count * group_count
    fft_len = 2 * block_len * block_count
    block_index = lax.axis_index("ctx")
    sliver = lax.all_to_all(gated, "grp", split_axis=1, concat_axis=0, tiled=True)
    piece_len = block_len // block_count
    token_index = block_index * piece_len + jnp.arange(piece_len, dtype=jnp.int32)
    front = across_forward(
        lax.all_to_all(sliver[None], "ctx", split_axis=1, concat_axis=0, tiled=True),
        token_index,
        fft_len,
    )
    spectra = within_block(
        lax.all_to_all(front, "ctx", split_axis=1, concat_axis=2, tiled=True), -1.0
    )
    filtered = twist(spectra, spectrum_real.astype(jnp.float32), spectrum_imag.astype(jnp.float32))
    restored = within_block(filtered, 1.0)
    local_freq = spectra.shape[1]
    frequency = block_index * local_freq + jnp.arange(local_freq, dtype=jnp.int32)
    turn_real, turn_imag = rotation(frequency, jnp.arange(block_len, dtype=jnp.int32), fft_len, 1.0)
    restored = twist(restored, turn_real[:, :, None], turn_imag[:, :, None])
    long_blocks = across_inverse(
        lax.all_to_all(restored, "ctx", split_axis=2, concat_axis=1, tiled=True), fft_len
    )
    long_sliver = lax.all_to_all(long_blocks, "ctx", split_axis=0, concat_axis=1, tiled=True)[0]
    long_tokens = lax.all_to_all(long_sliver, "grp", split_axis=0, concat_axis=1, tiled=True)
    mixed = query.astype(jnp.float32) * (long_tokens + skip_gain * gated)
    return mixed.astype(jnp.bfloat16)


def short_convolution(projected, conv_weight):
    channels = conv_weight.shape[1] // 3
    rim_rows = conv_weight.shape[0] - 1
    row_count = projected.shape[0]
    rim = shifted(projected[row_count - rim_rows :], ("ctx", "grp"), 1)
    extended = jnp.concatenate([rim, projected], axis=0)
    short = jnp.zeros((row_count, 3 * channels), jnp.float32)
    for offset in range(rim_rows + 1):
        short = short + conv_weight[offset] * extended[
            rim_rows - offset : rim_rows - offset + row_count
        ].astype(jnp.float32)
    short = short.astype(jnp.bfloat16)
    query = short[:, :channels]
    gated = short[:, channels : 2 * channels].astype(jnp.float32) * short[:, 2 * channels :].astype(
        jnp.float32
    )
    return query, gated


def angle_table(rows_index, cols_index, length):
    product = rows_index[:, None] * cols_index[None, :] % length
    angles = product.astype(jnp.float32) * (TWO_PI / length)
    return jnp.cos(angles), jnp.sin(angles)


def channel_parallel(projected, conv_weight, skip_gain, spectrum_real, spectrum_imag):
    row_count = projected.shape[0]
    taps, all_channels = conv_weight.shape
    channels = all_channels // 3
    block_count = lax.axis_size("ctx")
    group_count = lax.axis_size("grp")
    devices = block_count * group_count
    block_len = row_count * group_count
    sequence = block_len * block_count
    residues = 2 * block_count
    fft_len = residues * block_len
    width = channels // devices
    everyone = ("ctx", "grp")

    pairs = projected[:, channels:].reshape(row_count, 2, group_count, block_count, width)
    pairs = pairs.transpose(0, 3, 2, 1, 4).reshape(row_count, devices, 2, width)
    pairs = lax.all_to_all(pairs, everyone, split_axis=1, concat_axis=0, tiled=True)
    pairs = pairs.reshape(sequence, 2, width).astype(jnp.float32)
    pair_weight = conv_weight[:, channels:].reshape(taps, 2, group_count, block_count, width)
    pair_weight = lax.dynamic_index_in_dim(pair_weight, lax.axis_index("grp"), 2, keepdims=False)
    pair_weight = lax.dynamic_index_in_dim(pair_weight, lax.axis_index("ctx"), 2, keepdims=False)
    padded = jnp.pad(pairs, ((taps - 1, 0), (0, 0), (0, 0)))
    short = jnp.zeros((sequence, 2, width), jnp.float32)
    for offset in range(taps):
        short = short + pair_weight[offset] * padded[taps - 1 - offset : taps - 1 - offset + sequence]
    short = short.astype(jnp.bfloat16).astype(jnp.float32)
    tokens = (short[:, 0] * short[:, 1]).reshape(block_count, block_len, width)
    query, gated = short_convolution(projected, conv_weight)

    tokens, spectrum = lax.optimization_barrier((tokens, jnp.stack([spectrum_real, spectrum_imag])))
    spectrum = lax.all_to_all(spectrum, "ctx", split_axis=3, concat_axis=1, tiled=True)
    spectrum = spectrum.transpose(0, 2, 3, 1).astype(jnp.float32)
    filter_real, filter_imag = spectrum[0], spectrum[1]

    residue = jnp.arange(residues, dtype=jnp.int32)
    block_order = jnp.arange(block_count, dtype=jnp.int32)
    position = jnp.arange(block_len, dtype=jnp.int32)

    across_cos, across_sin = angle_table(block_order, residue, residues)
    folded_real = contract_high("jpc,ja->pca", tokens, across_cos)
    folded_imag = -contract_high("jpc,ja->pca", tokens, across_sin)
    turn_cos, turn_sin = angle_table(position, residue, fft_len)
    turn_cos, turn_sin = turn_cos[:, None, :], turn_sin[:, None, :]
    twisted_real = folded_real * turn_cos + folded_imag * turn_sin
    twisted_imag = folded_imag * turn_cos - folded_real * turn_sin

    within_cos, within_sin = angle_table(position, position, block_len)
    lanes = width * residues

    def times(table_part, data, precision=lax.Precision.HIGH):
        return lax.dot_general(
            table_part,
            data.reshape(block_len, lanes),
            (((1,), (0,)), ((), ())),
            precision=precision,
            preferred_element_type=jnp.float32,
        ).reshape(block_len, width, residues)

    def inverse(table_part, data):
        return times(table_part, data, lax.Precision.DEFAULT)

    spectra_real = times(within_cos, twisted_real) + times(within_sin, twisted_imag)
    spectra_imag = times(within_cos, twisted_imag) - times(within_sin, twisted_real)
    product_real = spectra_real * filter_real - spectra_imag * filter_imag
    product_imag = spectra_real * filter_imag + spectra_imag * filter_real
    restored_real = inverse(within_cos, product_real) - inverse(within_sin, product_imag)
    restored_imag = inverse(within_cos, product_imag) + inverse(within_sin, product_real)
    unturned_real = restored_real * turn_cos - restored_imag * turn_sin
    unturned_imag = restored_real * turn_sin + restored_imag * turn_cos
    long_blocks = contract_high("ja,pca->jpc", across_cos, unturned_real) - contract_high(
        "ja,pca->jpc", across_sin, unturned_imag
    )
    long_blocks = (long_blocks * (1.0 / fft_len)).reshape(devices, row_count, width)
    long_blocks = long_blocks.astype(jnp.bfloat16)
    returned = lax.all_to_all(long_blocks, everyone, split_axis=0, concat_axis=0, tiled=True)
    returned = returned.astype(jnp.float32)
    returned = returned.reshape(block_count, group_count, row_count, width).transpose(2, 1, 0, 3)
    long_tokens = returned.reshape(row_count, channels)
    mixed = query.astype(jnp.float32) * (long_tokens + skip_gain * gated)
    return mixed.astype(jnp.bfloat16)


def solution(mesh):
    in_specs = (P(("ctx", "grp"), None), P(), P(), P("ctx", None, "grp"), P("ctx", None, "grp"))
    out_specs = P(("ctx", "grp"), None)
    devices = mesh.shape["ctx"] * mesh.shape["grp"]

    def run(projected, conv_weight, skip_gain, spectrum_real, spectrum_imag):
        channels = conv_weight.shape[1] // 3
        wide = channels % devices == 0 and channels // devices >= 32
        body = channel_parallel if wide else per_device
        return jax.shard_map(
            body, mesh=mesh, in_specs=in_specs, out_specs=out_specs, check_vma=False
        )(projected, conv_weight, skip_gain, spectrum_real, spectrum_imag)

    return run
```

```python
import math

import jax
import jax.numpy as jnp
from jax import lax
from jax.sharding import PartitionSpec as P

TWO_PI = 2.0 * math.pi


def shifted(shard, axis, by):
    devices = lax.axis_size(axis)
    pairs = [(i, i + by) for i in range(devices) if 0 <= i + by < devices]
    return lax.ppermute(shard, axis, pairs)


def rotation(rows_index, cols_index, length, direction):
    product = rows_index[:, None] * cols_index[None, :] % length
    angles = product.astype(jnp.float32) * (TWO_PI / length)
    return (jnp.cos(angles), direction * jnp.sin(angles))


def complex_table(cos_part, sin_part):
    return jnp.stack([jnp.stack([cos_part, -sin_part]), jnp.stack([sin_part, cos_part])])


def contract(form, table, data, precision=lax.Precision.HIGHEST):
    return jnp.einsum(form, table, data, precision=precision, preferred_element_type=jnp.float32)


def contract_high(form, table, data):
    return contract(form, table, data, lax.Precision.HIGH)


def twist(data, turn_real, turn_imag):
    return jnp.stack(
        [data[0] * turn_real - data[1] * turn_imag, data[0] * turn_imag + data[1] * turn_real]
    )


def across_forward(blocks, token_index, fft_len):
    block_count = blocks.shape[0]
    frequency = jnp.arange(2 * block_count, dtype=jnp.int32)
    block_order = jnp.arange(block_count, dtype=jnp.int32)
    cos_table, sin_table = rotation(frequency, block_order, 2 * block_count, -1.0)
    accum = contract("pkj,jbc->pkbc", jnp.stack([cos_table, sin_table]), blocks)
    turn_real, turn_imag = rotation(frequency, token_index, fft_len, -1.0)
    return twist(accum, turn_real[:, :, None], turn_imag[:, :, None])


def within_block(data, direction):
    leading, length, lane_count = (data.shape[1], data.shape[2], data.shape[3])
    first_len = math.gcd(length, 256)
    second_len = length // first_len
    data = data.reshape(2, leading, second_len, first_len, lane_count)
    outer_index = jnp.arange(second_len, dtype=jnp.int32)
    inner_index = jnp.arange(first_len, dtype=jnp.int32)
    table_real, table_imag = rotation(outer_index, outer_index, second_len, direction)
    section = contract("pqkj,qxjbc->pxkbc", complex_table(table_real, table_imag), data)
    turn_real, turn_imag = rotation(outer_index, inner_index, length, direction)
    twisted = twist(section, turn_real[None, :, :, None], turn_imag[None, :, :, None])
    last_real, last_imag = rotation(inner_index, inner_index, first_len, direction)
    result = contract("pqgb,qxkbc->pxgkc", complex_table(last_real, last_imag), twisted)
    return result.reshape(2, leading, length, lane_count)


def across_inverse(data, fft_len):
    block_count = data.shape[1] // 2
    block_order = jnp.arange(block_count, dtype=jnp.int32)
    frequency = jnp.arange(2 * block_count, dtype=jnp.int32)
    cos_table, sin_table = rotation(block_order, frequency, 2 * block_count, 1.0)
    summed = contract("qjk,qkbc->jbc", jnp.stack([cos_table, -sin_table]), data)
    return summed * (1.0 / fft_len)


def per_device(projected, conv_weight, skip_gain, spectrum_real, spectrum_imag):
    channels = conv_weight.shape[1] // 3
    rim_rows = conv_weight.shape[0] - 1
    row_count = projected.shape[0]
    rim = shifted(projected[row_count - rim_rows :], ("ctx", "grp"), 1)
    extended = jnp.concatenate([rim, projected], axis=0)
    short = jnp.zeros((row_count, 3 * channels), jnp.float32)
    for offset in range(rim_rows + 1):
        short = short + conv_weight[offset] * extended[
            rim_rows - offset : rim_rows - offset + row_count
        ].astype(jnp.float32)
    short = short.astype(jnp.bfloat16)
    query = short[:, :channels]
    gated = short[:, channels : 2 * channels].astype(jnp.float32) * short[:, 2 * channels :].astype(
        jnp.float32
    )
    block_count = lax.axis_size("ctx")
    group_count = lax.axis_size("grp")
    block_len = row_count * group_count
    fft_len = 2 * block_len * block_count
    block_index = lax.axis_index("ctx")
    sliver = lax.all_to_all(gated, "grp", split_axis=1, concat_axis=0, tiled=True)
    piece_len = block_len // block_count
    token_index = block_index * piece_len + jnp.arange(piece_len, dtype=jnp.int32)
    front = across_forward(
        lax.all_to_all(sliver[None], "ctx", split_axis=1, concat_axis=0, tiled=True),
        token_index,
        fft_len,
    )
    spectra = within_block(
        lax.all_to_all(front, "ctx", split_axis=1, concat_axis=2, tiled=True), -1.0
    )
    filtered = twist(spectra, spectrum_real.astype(jnp.float32), spectrum_imag.astype(jnp.float32))
    restored = within_block(filtered, 1.0)
    local_freq = spectra.shape[1]
    frequency = block_index * local_freq + jnp.arange(local_freq, dtype=jnp.int32)
    turn_real, turn_imag = rotation(frequency, jnp.arange(block_len, dtype=jnp.int32), fft_len, 1.0)
    restored = twist(restored, turn_real[:, :, None], turn_imag[:, :, None])
    long_blocks = across_inverse(
        lax.all_to_all(restored, "ctx", split_axis=2, concat_axis=1, tiled=True), fft_len
    )
    long_sliver = lax.all_to_all(long_blocks, "ctx", split_axis=0, concat_axis=1, tiled=True)[0]
    long_tokens = lax.all_to_all(long_sliver, "grp", split_axis=0, concat_axis=1, tiled=True)
    mixed = query.astype(jnp.float32) * (long_tokens + skip_gain * gated)
    return mixed.astype(jnp.bfloat16)


def short_convolution(projected, conv_weight):
    channels = conv_weight.shape[1] // 3
    rim_rows = conv_weight.shape[0] - 1
    row_count = projected.shape[0]
    rim = shifted(projected[row_count - rim_rows :], ("ctx", "grp"), 1)
    extended = jnp.concatenate([rim, projected], axis=0)
    short = jnp.zeros((row_count, 3 * channels), jnp.float32)
    for offset in range(rim_rows + 1):
        short = short + conv_weight[offset] * extended[
            rim_rows - offset : rim_rows - offset + row_count
        ].astype(jnp.float32)
    short = short.astype(jnp.bfloat16)
    query = short[:, :channels]
    gated = short[:, channels : 2 * channels].astype(jnp.float32) * short[:, 2 * channels :].astype(
        jnp.float32
    )
    return query, gated


def angle_table(rows_index, cols_index, length):
    product = rows_index[:, None] * cols_index[None, :] % length
    angles = product.astype(jnp.float32) * (TWO_PI / length)
    return jnp.cos(angles), jnp.sin(angles)


def channel_parallel(projected, conv_weight, skip_gain, spectrum_real, spectrum_imag):
    query, gated = short_convolution(projected, conv_weight)
    row_count, channels = gated.shape
    block_count = lax.axis_size("ctx")
    group_count = lax.axis_size("grp")
    devices = block_count * group_count
    block_len = row_count * group_count
    residues = 2 * block_count
    fft_len = residues * block_len
    width = channels // devices
    everyone = ("ctx", "grp")

    outgoing = gated.reshape(row_count, group_count, block_count, width).transpose(0, 2, 1, 3)
    outgoing = outgoing.reshape(row_count, devices, width)
    outgoing = outgoing.astype(jnp.bfloat16)
    tokens = lax.all_to_all(outgoing, everyone, split_axis=1, concat_axis=0, tiled=True)
    tokens = tokens.reshape(block_count, block_len, width).astype(jnp.float32)

    local_residues, spectrum_len, half = spectrum_real.shape
    spectrum = jnp.stack([spectrum_real, spectrum_imag])
    spectrum = spectrum.reshape(2, local_residues, spectrum_len, block_count, width).transpose(0, 2, 3, 4, 1)
    tokens, spectrum = lax.optimization_barrier((tokens, spectrum))
    spectrum = lax.all_to_all(spectrum, "ctx", split_axis=2, concat_axis=4, tiled=True)
    spectrum = spectrum.reshape(2, spectrum_len, width, residues).astype(jnp.float32)
    filter_real, filter_imag = spectrum[0], spectrum[1]

    residue = jnp.arange(residues, dtype=jnp.int32)
    block_order = jnp.arange(block_count, dtype=jnp.int32)
    position = jnp.arange(block_len, dtype=jnp.int32)

    across_cos, across_sin = angle_table(block_order, residue, residues)
    folded_real = contract_high("jpc,ja->pca", tokens, across_cos)
    folded_imag = -contract_high("jpc,ja->pca", tokens, across_sin)
    turn_cos, turn_sin = angle_table(position, residue, fft_len)
    turn_cos, turn_sin = turn_cos[:, None, :], turn_sin[:, None, :]
    twisted_real = folded_real * turn_cos + folded_imag * turn_sin
    twisted_imag = folded_imag * turn_cos - folded_real * turn_sin

    within_cos, within_sin = angle_table(position, position, block_len)
    lanes = width * residues

    def times(table_part, data, precision=lax.Precision.HIGH):
        return lax.dot_general(
            table_part,
            data.reshape(block_len, lanes),
            (((1,), (0,)), ((), ())),
            precision=precision,
            preferred_element_type=jnp.float32,
        ).reshape(block_len, width, residues)

    def inverse(table_part, data):
        return times(table_part, data, lax.Precision.DEFAULT)

    spectra_real = times(within_cos, twisted_real) + times(within_sin, twisted_imag)
    spectra_imag = times(within_cos, twisted_imag) - times(within_sin, twisted_real)
    product_real = spectra_real * filter_real - spectra_imag * filter_imag
    product_imag = spectra_real * filter_imag + spectra_imag * filter_real
    restored_real = inverse(within_cos, product_real) - inverse(within_sin, product_imag)
    restored_imag = inverse(within_cos, product_imag) + inverse(within_sin, product_real)
    unturned_real = restored_real * turn_cos - restored_imag * turn_sin
    unturned_imag = restored_real * turn_sin + restored_imag * turn_cos
    long_blocks = contract_high("ja,pca->jpc", across_cos, unturned_real) - contract_high(
        "ja,pca->jpc", across_sin, unturned_imag
    )
    long_blocks = (long_blocks * (1.0 / fft_len)).reshape(devices, row_count, width)
    long_blocks = long_blocks.astype(jnp.bfloat16)
    returned = lax.all_to_all(long_blocks, everyone, split_axis=0, concat_axis=0, tiled=True)
    returned = returned.astype(jnp.float32)
    returned = returned.reshape(block_count, group_count, row_count, width).transpose(2, 1, 0, 3)
    long_tokens = returned.reshape(row_count, channels)
    mixed = query.astype(jnp.float32) * (long_tokens + skip_gain * gated)
    return mixed.astype(jnp.bfloat16)


def solution(mesh):
    in_specs = (P(("ctx", "grp"), None), P(), P(), P("ctx", None, "grp"), P("ctx", None, "grp"))
    out_specs = P(("ctx", "grp"), None)
    devices = mesh.shape["ctx"] * mesh.shape["grp"]

    def run(projected, conv_weight, skip_gain, spectrum_real, spectrum_imag):
        channels = conv_weight.shape[1] // 3
        wide = channels % devices == 0 and channels // devices >= 32
        body = channel_parallel if wide else per_device
        return jax.shard_map(
            body, mesh=mesh, in_specs=in_specs, out_specs=out_specs, check_vma=False
        )(projected, conv_weight, skip_gain, spectrum_real, spectrum_imag)

    return run
```

```python
import math

import jax
import jax.numpy as jnp
from jax import lax
from jax.sharding import PartitionSpec as P

TWO_PI = 2.0 * math.pi


def shifted(shard, axis, by):
    devices = lax.axis_size(axis)
    pairs = [(i, i + by) for i in range(devices) if 0 <= i + by < devices]
    return lax.ppermute(shard, axis, pairs)


def rotation(rows_index, cols_index, length, direction):
    product = rows_index[:, None] * cols_index[None, :] % length
    angles = product.astype(jnp.float32) * (TWO_PI / length)
    return (jnp.cos(angles), direction * jnp.sin(angles))


def complex_table(cos_part, sin_part):
    return jnp.stack([jnp.stack([cos_part, -sin_part]), jnp.stack([sin_part, cos_part])])


def contract(form, table, data, precision=lax.Precision.HIGHEST):
    return jnp.einsum(form, table, data, precision=precision, preferred_element_type=jnp.float32)


def contract_high(form, table, data):
    return contract(form, table, data, lax.Precision.HIGH)


def twist(data, turn_real, turn_imag):
    return jnp.stack(
        [data[0] * turn_real - data[1] * turn_imag, data[0] * turn_imag + data[1] * turn_real]
    )


def across_forward(blocks, token_index, fft_len):
    block_count = blocks.shape[0]
    frequency = jnp.arange(2 * block_count, dtype=jnp.int32)
    block_order = jnp.arange(block_count, dtype=jnp.int32)
    cos_table, sin_table = rotation(frequency, block_order, 2 * block_count, -1.0)
    accum = contract("pkj,jbc->pkbc", jnp.stack([cos_table, sin_table]), blocks)
    turn_real, turn_imag = rotation(frequency, token_index, fft_len, -1.0)
    return twist(accum, turn_real[:, :, None], turn_imag[:, :, None])


def within_block(data, direction):
    leading, length, lane_count = (data.shape[1], data.shape[2], data.shape[3])
    first_len = math.gcd(length, 256)
    second_len = length // first_len
    data = data.reshape(2, leading, second_len, first_len, lane_count)
    outer_index = jnp.arange(second_len, dtype=jnp.int32)
    inner_index = jnp.arange(first_len, dtype=jnp.int32)
    table_real, table_imag = rotation(outer_index, outer_index, second_len, direction)
    section = contract("pqkj,qxjbc->pxkbc", complex_table(table_real, table_imag), data)
    turn_real, turn_imag = rotation(outer_index, inner_index, length, direction)
    twisted = twist(section, turn_real[None, :, :, None], turn_imag[None, :, :, None])
    last_real, last_imag = rotation(inner_index, inner_index, first_len, direction)
    result = contract("pqgb,qxkbc->pxgkc", complex_table(last_real, last_imag), twisted)
    return result.reshape(2, leading, length, lane_count)


def across_inverse(data, fft_len):
    block_count = data.shape[1] // 2
    block_order = jnp.arange(block_count, dtype=jnp.int32)
    frequency = jnp.arange(2 * block_count, dtype=jnp.int32)
    cos_table, sin_table = rotation(block_order, frequency, 2 * block_count, 1.0)
    summed = contract("qjk,qkbc->jbc", jnp.stack([cos_table, -sin_table]), data)
    return summed * (1.0 / fft_len)


def per_device(projected, conv_weight, skip_gain, spectrum_real, spectrum_imag):
    channels = conv_weight.shape[1] // 3
    rim_rows = conv_weight.shape[0] - 1
    row_count = projected.shape[0]
    rim = shifted(projected[row_count - rim_rows :], ("ctx", "grp"), 1)
    extended = jnp.concatenate([rim, projected], axis=0)
    short = jnp.zeros((row_count, 3 * channels), jnp.float32)
    for offset in range(rim_rows + 1):
        short = short + conv_weight[offset] * extended[
            rim_rows - offset : rim_rows - offset + row_count
        ].astype(jnp.float32)
    short = short.astype(jnp.bfloat16)
    query = short[:, :channels]
    gated = short[:, channels : 2 * channels].astype(jnp.float32) * short[:, 2 * channels :].astype(
        jnp.float32
    )
    block_count = lax.axis_size("ctx")
    group_count = lax.axis_size("grp")
    block_len = row_count * group_count
    fft_len = 2 * block_len * block_count
    block_index = lax.axis_index("ctx")
    sliver = lax.all_to_all(gated, "grp", split_axis=1, concat_axis=0, tiled=True)
    piece_len = block_len // block_count
    token_index = block_index * piece_len + jnp.arange(piece_len, dtype=jnp.int32)
    front = across_forward(
        lax.all_to_all(sliver[None], "ctx", split_axis=1, concat_axis=0, tiled=True),
        token_index,
        fft_len,
    )
    spectra = within_block(
        lax.all_to_all(front, "ctx", split_axis=1, concat_axis=2, tiled=True), -1.0
    )
    filtered = twist(spectra, spectrum_real.astype(jnp.float32), spectrum_imag.astype(jnp.float32))
    restored = within_block(filtered, 1.0)
    local_freq = spectra.shape[1]
    frequency = block_index * local_freq + jnp.arange(local_freq, dtype=jnp.int32)
    turn_real, turn_imag = rotation(frequency, jnp.arange(block_len, dtype=jnp.int32), fft_len, 1.0)
    restored = twist(restored, turn_real[:, :, None], turn_imag[:, :, None])
    long_blocks = across_inverse(
        lax.all_to_all(restored, "ctx", split_axis=2, concat_axis=1, tiled=True), fft_len
    )
    long_sliver = lax.all_to_all(long_blocks, "ctx", split_axis=0, concat_axis=1, tiled=True)[0]
    long_tokens = lax.all_to_all(long_sliver, "grp", split_axis=0, concat_axis=1, tiled=True)
    mixed = query.astype(jnp.float32) * (long_tokens + skip_gain * gated)
    return mixed.astype(jnp.bfloat16)


def short_convolution(projected, conv_weight):
    channels = conv_weight.shape[1] // 3
    rim_rows = conv_weight.shape[0] - 1
    row_count = projected.shape[0]
    rim = shifted(projected[row_count - rim_rows :], ("ctx", "grp"), 1)
    extended = jnp.concatenate([rim, projected], axis=0)
    short = jnp.zeros((row_count, 3 * channels), jnp.float32)
    for offset in range(rim_rows + 1):
        short = short + conv_weight[offset] * extended[
            rim_rows - offset : rim_rows - offset + row_count
        ].astype(jnp.float32)
    short = short.astype(jnp.bfloat16)
    query = short[:, :channels]
    gated = short[:, channels : 2 * channels].astype(jnp.float32) * short[:, 2 * channels :].astype(
        jnp.float32
    )
    return query, gated


def angle_table(rows_index, cols_index, length):
    product = rows_index[:, None] * cols_index[None, :] % length
    angles = product.astype(jnp.float32) * (TWO_PI / length)
    return jnp.cos(angles), jnp.sin(angles)


def split_convolution(projected, conv_weight):
    channels = conv_weight.shape[1] // 3
    rim_rows = conv_weight.shape[0] - 1
    row_count = projected.shape[0]
    rim = shifted(projected[row_count - rim_rows :], ("ctx", "grp"), 1)
    extended = jnp.concatenate([rim, projected], axis=0)

    def columns(first, last):
        total = jnp.zeros((row_count, last - first), jnp.float32)
        for offset in range(rim_rows + 1):
            rows = extended[rim_rows - offset : rim_rows - offset + row_count, first:last]
            total = total + conv_weight[offset, first:last] * rows.astype(jnp.float32)
        return total.astype(jnp.bfloat16)

    pairs = columns(channels, 3 * channels).astype(jnp.float32)
    gated = pairs[:, :channels] * pairs[:, channels:]
    return gated, lambda: columns(0, channels)


def channel_parallel(projected, conv_weight, skip_gain, spectrum_real, spectrum_imag):
    gated, query_of = split_convolution(projected, conv_weight)
    row_count, channels = gated.shape
    block_count = lax.axis_size("ctx")
    group_count = lax.axis_size("grp")
    devices = block_count * group_count
    block_len = row_count * group_count
    residues = 2 * block_count
    fft_len = residues * block_len
    width = channels // devices
    everyone = ("ctx", "grp")

    outgoing = gated.reshape(row_count, group_count, block_count, width).transpose(0, 2, 1, 3)
    outgoing = outgoing.reshape(row_count, devices, width)
    outgoing = outgoing.astype(jnp.bfloat16)
    tokens = lax.all_to_all(outgoing, everyone, split_axis=1, concat_axis=0, tiled=True)
    tokens = tokens.reshape(block_count, block_len, width).astype(jnp.float32)

    tokens, spectrum = lax.optimization_barrier((tokens, jnp.stack([spectrum_real, spectrum_imag])))
    spectrum = lax.all_to_all(spectrum, "ctx", split_axis=3, concat_axis=1, tiled=True)
    spectrum = spectrum.transpose(0, 2, 3, 1).astype(jnp.float32)
    filter_real, filter_imag = spectrum[0], spectrum[1]

    residue = jnp.arange(residues, dtype=jnp.int32)
    block_order = jnp.arange(block_count, dtype=jnp.int32)
    position = jnp.arange(block_len, dtype=jnp.int32)

    across_cos, across_sin = angle_table(block_order, residue, residues)
    folded_real = contract_high("jpc,ja->pca", tokens, across_cos)
    folded_imag = -contract_high("jpc,ja->pca", tokens, across_sin)
    turn_cos, turn_sin = angle_table(position, residue, fft_len)
    turn_cos, turn_sin = turn_cos[:, None, :], turn_sin[:, None, :]
    twisted_real = folded_real * turn_cos + folded_imag * turn_sin
    twisted_imag = folded_imag * turn_cos - folded_real * turn_sin

    within_cos, within_sin = angle_table(position, position, block_len)
    lanes = width * residues

    def times(table_part, data, precision=lax.Precision.HIGH):
        return lax.dot_general(
            table_part,
            data.reshape(block_len, lanes),
            (((1,), (0,)), ((), ())),
            precision=precision,
            preferred_element_type=jnp.float32,
        ).reshape(block_len, width, residues)

    def inverse(table_part, data):
        return times(table_part, data, lax.Precision.DEFAULT)

    spectra_real = times(within_cos, twisted_real) + times(within_sin, twisted_imag)
    spectra_imag = times(within_cos, twisted_imag) - times(within_sin, twisted_real)
    query, spectra_real, spectra_imag = lax.optimization_barrier((query_of(), spectra_real, spectra_imag))
    product_real = spectra_real * filter_real - spectra_imag * filter_imag
    product_imag = spectra_real * filter_imag + spectra_imag * filter_real
    restored_real = inverse(within_cos, product_real) - inverse(within_sin, product_imag)
    restored_imag = inverse(within_cos, product_imag) + inverse(within_sin, product_real)
    unturned_real = restored_real * turn_cos - restored_imag * turn_sin
    unturned_imag = restored_real * turn_sin + restored_imag * turn_cos
    long_blocks = contract_high("ja,pca->jpc", across_cos, unturned_real) - contract_high(
        "ja,pca->jpc", across_sin, unturned_imag
    )
    long_blocks = (long_blocks * (1.0 / fft_len)).reshape(devices, row_count, width)
    long_blocks = long_blocks.astype(jnp.bfloat16)
    returned = lax.all_to_all(long_blocks, everyone, split_axis=0, concat_axis=0, tiled=True)
    returned = returned.astype(jnp.float32)
    returned = returned.reshape(block_count, group_count, row_count, width).transpose(2, 1, 0, 3)
    long_tokens = returned.reshape(row_count, channels)
    mixed = query.astype(jnp.float32) * (long_tokens + skip_gain * gated)
    return mixed.astype(jnp.bfloat16)


def solution(mesh):
    in_specs = (P(("ctx", "grp"), None), P(), P(), P("ctx", None, "grp"), P("ctx", None, "grp"))
    out_specs = P(("ctx", "grp"), None)
    devices = mesh.shape["ctx"] * mesh.shape["grp"]

    def run(projected, conv_weight, skip_gain, spectrum_real, spectrum_imag):
        channels = conv_weight.shape[1] // 3
        wide = channels % devices == 0 and channels // devices >= 32
        body = channel_parallel if wide else per_device
        return jax.shard_map(
            body, mesh=mesh, in_specs=in_specs, out_specs=out_specs, check_vma=False
        )(projected, conv_weight, skip_gain, spectrum_real, spectrum_imag)

    return run
```

```python
import math

import jax
import jax.numpy as jnp
from jax import lax
from jax.sharding import PartitionSpec as P

TWO_PI = 2.0 * math.pi


def shifted(shard, axis, by):
    devices = lax.axis_size(axis)
    pairs = [(i, i + by) for i in range(devices) if 0 <= i + by < devices]
    return lax.ppermute(shard, axis, pairs)


def rotation(rows_index, cols_index, length, direction):
    product = rows_index[:, None] * cols_index[None, :] % length
    angles = product.astype(jnp.float32) * (TWO_PI / length)
    return (jnp.cos(angles), direction * jnp.sin(angles))


def complex_table(cos_part, sin_part):
    return jnp.stack([jnp.stack([cos_part, -sin_part]), jnp.stack([sin_part, cos_part])])


def contract(form, table, data, precision=lax.Precision.HIGHEST):
    return jnp.einsum(form, table, data, precision=precision, preferred_element_type=jnp.float32)


def contract_high(form, table, data):
    return contract(form, table, data, lax.Precision.HIGH)


def twist(data, turn_real, turn_imag):
    return jnp.stack(
        [data[0] * turn_real - data[1] * turn_imag, data[0] * turn_imag + data[1] * turn_real]
    )


def across_forward(blocks, token_index, fft_len):
    block_count = blocks.shape[0]
    frequency = jnp.arange(2 * block_count, dtype=jnp.int32)
    block_order = jnp.arange(block_count, dtype=jnp.int32)
    cos_table, sin_table = rotation(frequency, block_order, 2 * block_count, -1.0)
    accum = contract("pkj,jbc->pkbc", jnp.stack([cos_table, sin_table]), blocks)
    turn_real, turn_imag = rotation(frequency, token_index, fft_len, -1.0)
    return twist(accum, turn_real[:, :, None], turn_imag[:, :, None])


def within_block(data, direction):
    leading, length, lane_count = (data.shape[1], data.shape[2], data.shape[3])
    first_len = math.gcd(length, 256)
    second_len = length // first_len
    data = data.reshape(2, leading, second_len, first_len, lane_count)
    outer_index = jnp.arange(second_len, dtype=jnp.int32)
    inner_index = jnp.arange(first_len, dtype=jnp.int32)
    table_real, table_imag = rotation(outer_index, outer_index, second_len, direction)
    section = contract("pqkj,qxjbc->pxkbc", complex_table(table_real, table_imag), data)
    turn_real, turn_imag = rotation(outer_index, inner_index, length, direction)
    twisted = twist(section, turn_real[None, :, :, None], turn_imag[None, :, :, None])
    last_real, last_imag = rotation(inner_index, inner_index, first_len, direction)
    result = contract("pqgb,qxkbc->pxgkc", complex_table(last_real, last_imag), twisted)
    return result.reshape(2, leading, length, lane_count)


def across_inverse(data, fft_len):
    block_count = data.shape[1] // 2
    block_order = jnp.arange(block_count, dtype=jnp.int32)
    frequency = jnp.arange(2 * block_count, dtype=jnp.int32)
    cos_table, sin_table = rotation(block_order, frequency, 2 * block_count, 1.0)
    summed = contract("qjk,qkbc->jbc", jnp.stack([cos_table, -sin_table]), data)
    return summed * (1.0 / fft_len)


def per_device(projected, conv_weight, skip_gain, spectrum_real, spectrum_imag):
    channels = conv_weight.shape[1] // 3
    rim_rows = conv_weight.shape[0] - 1
    row_count = projected.shape[0]
    rim = shifted(projected[row_count - rim_rows :], ("ctx", "grp"), 1)
    extended = jnp.concatenate([rim, projected], axis=0)
    short = jnp.zeros((row_count, 3 * channels), jnp.float32)
    for offset in range(rim_rows + 1):
        short = short + conv_weight[offset] * extended[
            rim_rows - offset : rim_rows - offset + row_count
        ].astype(jnp.float32)
    short = short.astype(jnp.bfloat16)
    query = short[:, :channels]
    gated = short[:, channels : 2 * channels].astype(jnp.float32) * short[:, 2 * channels :].astype(
        jnp.float32
    )
    block_count = lax.axis_size("ctx")
    group_count = lax.axis_size("grp")
    block_len = row_count * group_count
    fft_len = 2 * block_len * block_count
    block_index = lax.axis_index("ctx")
    sliver = lax.all_to_all(gated, "grp", split_axis=1, concat_axis=0, tiled=True)
    piece_len = block_len // block_count
    token_index = block_index * piece_len + jnp.arange(piece_len, dtype=jnp.int32)
    front = across_forward(
        lax.all_to_all(sliver[None], "ctx", split_axis=1, concat_axis=0, tiled=True),
        token_index,
        fft_len,
    )
    spectra = within_block(
        lax.all_to_all(front, "ctx", split_axis=1, concat_axis=2, tiled=True), -1.0
    )
    filtered = twist(spectra, spectrum_real.astype(jnp.float32), spectrum_imag.astype(jnp.float32))
    restored = within_block(filtered, 1.0)
    local_freq = spectra.shape[1]
    frequency = block_index * local_freq + jnp.arange(local_freq, dtype=jnp.int32)
    turn_real, turn_imag = rotation(frequency, jnp.arange(block_len, dtype=jnp.int32), fft_len, 1.0)
    restored = twist(restored, turn_real[:, :, None], turn_imag[:, :, None])
    long_blocks = across_inverse(
        lax.all_to_all(restored, "ctx", split_axis=2, concat_axis=1, tiled=True), fft_len
    )
    long_sliver = lax.all_to_all(long_blocks, "ctx", split_axis=0, concat_axis=1, tiled=True)[0]
    long_tokens = lax.all_to_all(long_sliver, "grp", split_axis=0, concat_axis=1, tiled=True)
    mixed = query.astype(jnp.float32) * (long_tokens + skip_gain * gated)
    return mixed.astype(jnp.bfloat16)


def short_convolution(projected, conv_weight):
    channels = conv_weight.shape[1] // 3
    rim_rows = conv_weight.shape[0] - 1
    row_count = projected.shape[0]
    rim = shifted(projected[row_count - rim_rows :], ("ctx", "grp"), 1)
    extended = jnp.concatenate([rim, projected], axis=0)
    short = jnp.zeros((row_count, 3 * channels), jnp.float32)
    for offset in range(rim_rows + 1):
        short = short + conv_weight[offset] * extended[
            rim_rows - offset : rim_rows - offset + row_count
        ].astype(jnp.float32)
    short = short.astype(jnp.bfloat16)
    query = short[:, :channels]
    gated = short[:, channels : 2 * channels].astype(jnp.float32) * short[:, 2 * channels :].astype(
        jnp.float32
    )
    return query, gated


def angle_table(rows_index, cols_index, length):
    product = rows_index[:, None] * cols_index[None, :] % length
    angles = product.astype(jnp.float32) * (TWO_PI / length)
    return jnp.cos(angles), jnp.sin(angles)


def channel_parallel(projected, conv_weight, skip_gain, spectrum_real, spectrum_imag):
    query, gated = short_convolution(projected, conv_weight)
    row_count, channels = gated.shape
    block_count = lax.axis_size("ctx")
    group_count = lax.axis_size("grp")
    devices = block_count * group_count
    block_len = row_count * group_count
    residues = 2 * block_count
    fft_len = residues * block_len
    width = channels // devices
    everyone = ("ctx", "grp")

    outgoing = gated.reshape(row_count, group_count, block_count, width).transpose(0, 2, 1, 3)
    outgoing = outgoing.reshape(row_count, devices, width)
    outgoing = outgoing.astype(jnp.bfloat16)
    tokens = lax.all_to_all(outgoing, everyone, split_axis=1, concat_axis=0, tiled=True)
    tokens = tokens.reshape(block_count, block_len, width).astype(jnp.float32).transpose(0, 2, 1)

    tokens, spectrum = lax.optimization_barrier((tokens, jnp.stack([spectrum_real, spectrum_imag])))
    spectrum = lax.all_to_all(spectrum, "ctx", split_axis=3, concat_axis=1, tiled=True)
    spectrum = spectrum.transpose(0, 1, 3, 2).astype(jnp.float32)
    filter_real, filter_imag = spectrum[0], spectrum[1]

    residue = jnp.arange(residues, dtype=jnp.int32)
    block_order = jnp.arange(block_count, dtype=jnp.int32)
    position = jnp.arange(block_len, dtype=jnp.int32)

    across_cos, across_sin = angle_table(block_order, residue, residues)
    folded_real = contract_high("ja,jcp->acp", across_cos, tokens)
    folded_imag = -contract_high("ja,jcp->acp", across_sin, tokens)
    turn_cos, turn_sin = angle_table(residue, position, fft_len)
    turn_cos, turn_sin = turn_cos[:, None, :], turn_sin[:, None, :]
    twisted_real = folded_real * turn_cos + folded_imag * turn_sin
    twisted_imag = folded_imag * turn_cos - folded_real * turn_sin

    within_cos, within_sin = angle_table(position, position, block_len)
    rows = residues * width

    def times(table_part, data, precision=lax.Precision.HIGH):
        return lax.dot_general(
            data.reshape(rows, block_len),
            table_part,
            (((1,), (0,)), ((), ())),
            precision=precision,
            preferred_element_type=jnp.float32,
        ).reshape(residues, width, block_len)

    def inverse(table_part, data):
        return times(table_part, data, lax.Precision.DEFAULT)

    spectra_real = times(within_cos, twisted_real) + times(within_sin, twisted_imag)
    spectra_imag = times(within_cos, twisted_imag) - times(within_sin, twisted_real)
    product_real = spectra_real * filter_real - spectra_imag * filter_imag
    product_imag = spectra_real * filter_imag + spectra_imag * filter_real
    restored_real = inverse(within_cos, product_real) - inverse(within_sin, product_imag)
    restored_imag = inverse(within_cos, product_imag) + inverse(within_sin, product_real)
    unturned_real = restored_real * turn_cos - restored_imag * turn_sin
    unturned_imag = restored_real * turn_sin + restored_imag * turn_cos
    long_blocks = contract_high("ja,acp->jcp", across_cos, unturned_real) - contract_high(
        "ja,acp->jcp", across_sin, unturned_imag
    )
    halves = block_len // row_count
    long_blocks = long_blocks.reshape(block_count, width, halves, row_count).transpose(0, 2, 3, 1)
    long_blocks = (long_blocks * (1.0 / fft_len)).reshape(devices, row_count, width)
    long_blocks = long_blocks.astype(jnp.bfloat16)
    returned = lax.all_to_all(long_blocks, everyone, split_axis=0, concat_axis=0, tiled=True)
    returned = returned.astype(jnp.float32)
    returned = returned.reshape(block_count, group_count, row_count, width).transpose(2, 1, 0, 3)
    long_tokens = returned.reshape(row_count, channels)
    mixed = query.astype(jnp.float32) * (long_tokens + skip_gain * gated)
    return mixed.astype(jnp.bfloat16)


def solution(mesh):
    in_specs = (P(("ctx", "grp"), None), P(), P(), P("ctx", None, "grp"), P("ctx", None, "grp"))
    out_specs = P(("ctx", "grp"), None)
    devices = mesh.shape["ctx"] * mesh.shape["grp"]

    def run(projected, conv_weight, skip_gain, spectrum_real, spectrum_imag):
        channels = conv_weight.shape[1] // 3
        wide = channels % devices == 0 and channels // devices >= 32
        body = channel_parallel if wide else per_device
        return jax.shard_map(
            body, mesh=mesh, in_specs=in_specs, out_specs=out_specs, check_vma=False
        )(projected, conv_weight, skip_gain, spectrum_real, spectrum_imag)

    return run
```

```python
import math

import jax
import jax.numpy as jnp
from jax import lax
from jax.sharding import PartitionSpec as P

TWO_PI = 2.0 * math.pi


def shifted(shard, axis, by):
    devices = lax.axis_size(axis)
    pairs = [(i, i + by) for i in range(devices) if 0 <= i + by < devices]
    return lax.ppermute(shard, axis, pairs)


def rotation(rows_index, cols_index, length, direction):
    product = rows_index[:, None] * cols_index[None, :] % length
    angles = product.astype(jnp.float32) * (TWO_PI / length)
    return (jnp.cos(angles), direction * jnp.sin(angles))


def complex_table(cos_part, sin_part):
    return jnp.stack([jnp.stack([cos_part, -sin_part]), jnp.stack([sin_part, cos_part])])


def contract(form, table, data, precision=lax.Precision.HIGHEST):
    return jnp.einsum(form, table, data, precision=precision, preferred_element_type=jnp.float32)


def contract_high(form, table, data):
    return contract(form, table, data, lax.Precision.HIGH)


def twist(data, turn_real, turn_imag):
    return jnp.stack(
        [data[0] * turn_real - data[1] * turn_imag, data[0] * turn_imag + data[1] * turn_real]
    )


def across_forward(blocks, token_index, fft_len):
    block_count = blocks.shape[0]
    frequency = jnp.arange(2 * block_count, dtype=jnp.int32)
    block_order = jnp.arange(block_count, dtype=jnp.int32)
    cos_table, sin_table = rotation(frequency, block_order, 2 * block_count, -1.0)
    accum = contract("pkj,jbc->pkbc", jnp.stack([cos_table, sin_table]), blocks)
    turn_real, turn_imag = rotation(frequency, token_index, fft_len, -1.0)
    return twist(accum, turn_real[:, :, None], turn_imag[:, :, None])


def within_block(data, direction):
    leading, length, lane_count = (data.shape[1], data.shape[2], data.shape[3])
    first_len = math.gcd(length, 256)
    second_len = length // first_len
    data = data.reshape(2, leading, second_len, first_len, lane_count)
    outer_index = jnp.arange(second_len, dtype=jnp.int32)
    inner_index = jnp.arange(first_len, dtype=jnp.int32)
    table_real, table_imag = rotation(outer_index, outer_index, second_len, direction)
    section = contract("pqkj,qxjbc->pxkbc", complex_table(table_real, table_imag), data)
    turn_real, turn_imag = rotation(outer_index, inner_index, length, direction)
    twisted = twist(section, turn_real[None, :, :, None], turn_imag[None, :, :, None])
    last_real, last_imag = rotation(inner_index, inner_index, first_len, direction)
    result = contract("pqgb,qxkbc->pxgkc", complex_table(last_real, last_imag), twisted)
    return result.reshape(2, leading, length, lane_count)


def across_inverse(data, fft_len):
    block_count = data.shape[1] // 2
    block_order = jnp.arange(block_count, dtype=jnp.int32)
    frequency = jnp.arange(2 * block_count, dtype=jnp.int32)
    cos_table, sin_table = rotation(block_order, frequency, 2 * block_count, 1.0)
    summed = contract("qjk,qkbc->jbc", jnp.stack([cos_table, -sin_table]), data)
    return summed * (1.0 / fft_len)


def per_device(projected, conv_weight, skip_gain, spectrum_real, spectrum_imag):
    channels = conv_weight.shape[1] // 3
    rim_rows = conv_weight.shape[0] - 1
    row_count = projected.shape[0]
    rim = shifted(projected[row_count - rim_rows :], ("ctx", "grp"), 1)
    extended = jnp.concatenate([rim, projected], axis=0)
    short = jnp.zeros((row_count, 3 * channels), jnp.float32)
    for offset in range(rim_rows + 1):
        short = short + conv_weight[offset] * extended[
            rim_rows - offset : rim_rows - offset + row_count
        ].astype(jnp.float32)
    short = short.astype(jnp.bfloat16)
    query = short[:, :channels]
    gated = short[:, channels : 2 * channels].astype(jnp.float32) * short[:, 2 * channels :].astype(
        jnp.float32
    )
    block_count = lax.axis_size("ctx")
    group_count = lax.axis_size("grp")
    block_len = row_count * group_count
    fft_len = 2 * block_len * block_count
    block_index = lax.axis_index("ctx")
    sliver = lax.all_to_all(gated, "grp", split_axis=1, concat_axis=0, tiled=True)
    piece_len = block_len // block_count
    token_index = block_index * piece_len + jnp.arange(piece_len, dtype=jnp.int32)
    front = across_forward(
        lax.all_to_all(sliver[None], "ctx", split_axis=1, concat_axis=0, tiled=True),
        token_index,
        fft_len,
    )
    spectra = within_block(
        lax.all_to_all(front, "ctx", split_axis=1, concat_axis=2, tiled=True), -1.0
    )
    filtered = twist(spectra, spectrum_real.astype(jnp.float32), spectrum_imag.astype(jnp.float32))
    restored = within_block(filtered, 1.0)
    local_freq = spectra.shape[1]
    frequency = block_index * local_freq + jnp.arange(local_freq, dtype=jnp.int32)
    turn_real, turn_imag = rotation(frequency, jnp.arange(block_len, dtype=jnp.int32), fft_len, 1.0)
    restored = twist(restored, turn_real[:, :, None], turn_imag[:, :, None])
    long_blocks = across_inverse(
        lax.all_to_all(restored, "ctx", split_axis=2, concat_axis=1, tiled=True), fft_len
    )
    long_sliver = lax.all_to_all(long_blocks, "ctx", split_axis=0, concat_axis=1, tiled=True)[0]
    long_tokens = lax.all_to_all(long_sliver, "grp", split_axis=0, concat_axis=1, tiled=True)
    mixed = query.astype(jnp.float32) * (long_tokens + skip_gain * gated)
    return mixed.astype(jnp.bfloat16)


def short_convolution(projected, conv_weight):
    channels = conv_weight.shape[1] // 3
    rim_rows = conv_weight.shape[0] - 1
    row_count = projected.shape[0]
    rim = shifted(projected[row_count - rim_rows :], ("ctx", "grp"), 1)
    extended = jnp.concatenate([rim, projected], axis=0)
    short = jnp.zeros((row_count, 3 * channels), jnp.float32)
    for offset in range(rim_rows + 1):
        short = short + conv_weight[offset] * extended[
            rim_rows - offset : rim_rows - offset + row_count
        ].astype(jnp.float32)
    short = short.astype(jnp.bfloat16)
    query = short[:, :channels]
    gated = short[:, channels : 2 * channels].astype(jnp.float32) * short[:, 2 * channels :].astype(
        jnp.float32
    )
    return query, gated


def angle_table(rows_index, cols_index, length):
    product = rows_index[:, None] * cols_index[None, :] % length
    angles = product.astype(jnp.float32) * (TWO_PI / length)
    return jnp.cos(angles), jnp.sin(angles)


def channel_parallel(projected, conv_weight, skip_gain, spectrum_real, spectrum_imag):
    query, gated = short_convolution(projected, conv_weight)
    row_count, channels = gated.shape
    block_count = lax.axis_size("ctx")
    group_count = lax.axis_size("grp")
    devices = block_count * group_count
    block_len = row_count * group_count
    residues = 2 * block_count
    fft_len = residues * block_len
    width = channels // devices
    everyone = ("ctx", "grp")

    outgoing = gated.reshape(row_count, group_count, block_count, width).transpose(0, 2, 1, 3)
    outgoing = outgoing.reshape(row_count, devices, width)
    outgoing = outgoing.astype(jnp.bfloat16)
    tokens = lax.all_to_all(outgoing, everyone, split_axis=1, concat_axis=0, tiled=True)
    tokens = tokens.reshape(block_count, block_len, width).astype(jnp.float32).transpose(0, 2, 1)

    middle = residues // 2
    local_residues = spectrum_real.shape[0]
    held = lax.axis_index("ctx") * local_residues + jnp.arange(local_residues, dtype=jnp.int32)
    above = (held > middle)[:, None, None]
    send_real = jnp.where(above, jnp.flip(spectrum_real, axis=1), spectrum_real)
    send_imag = jnp.where(above, -jnp.flip(spectrum_imag, axis=1), spectrum_imag)
    tokens, spectrum = lax.optimization_barrier((tokens, jnp.stack([send_real, send_imag])))
    spectrum = lax.all_to_all(spectrum, "ctx", split_axis=3, concat_axis=1, tiled=True)
    spectrum = spectrum.transpose(0, 1, 3, 2).astype(jnp.float32)

    def paired(part):
        mirrored = part[1:middle] + part[residues - 1 : middle : -1]
        return jnp.concatenate([part[:1], mirrored, part[middle : middle + 1]], axis=0)

    filter_real, filter_imag = paired(spectrum[0]), paired(spectrum[1])
    kept = middle + 1

    residue = jnp.arange(kept, dtype=jnp.int32)
    block_order = jnp.arange(block_count, dtype=jnp.int32)
    position = jnp.arange(block_len, dtype=jnp.int32)

    across_cos, across_sin = angle_table(block_order, residue, residues)
    folded_real = contract_high("ja,jcp->acp", across_cos, tokens)
    folded_imag = -contract_high("ja,jcp->acp", across_sin, tokens)
    turn_cos, turn_sin = angle_table(residue, position, fft_len)
    turn_cos, turn_sin = turn_cos[:, None, :], turn_sin[:, None, :]
    twisted_real = folded_real * turn_cos + folded_imag * turn_sin
    twisted_imag = folded_imag * turn_cos - folded_real * turn_sin

    within_cos, within_sin = angle_table(position, position, block_len)
    rows = kept * width

    def times(table_part, data, precision=lax.Precision.HIGH):
        return lax.dot_general(
            data.reshape(rows, block_len),
            table_part,
            (((1,), (0,)), ((), ())),
            precision=precision,
            preferred_element_type=jnp.float32,
        ).reshape(kept, width, block_len)

    def inverse(table_part, data):
        return times(table_part, data, lax.Precision.DEFAULT)

    spectra_real = times(within_cos, twisted_real) + times(within_sin, twisted_imag)
    spectra_imag = times(within_cos, twisted_imag) - times(within_sin, twisted_real)
    product_real = spectra_real * filter_real - spectra_imag * filter_imag
    product_imag = spectra_real * filter_imag + spectra_imag * filter_real
    restored_real = inverse(within_cos, product_real) - inverse(within_sin, product_imag)
    restored_imag = inverse(within_cos, product_imag) + inverse(within_sin, product_real)
    unturned_real = restored_real * turn_cos - restored_imag * turn_sin
    unturned_imag = restored_real * turn_sin + restored_imag * turn_cos
    long_blocks = contract_high("ja,acp->jcp", across_cos, unturned_real) - contract_high(
        "ja,acp->jcp", across_sin, unturned_imag
    )
    halves = block_len // row_count
    long_blocks = long_blocks.reshape(block_count, width, halves, row_count).transpose(0, 2, 3, 1)
    long_blocks = (long_blocks * (1.0 / fft_len)).reshape(devices, row_count, width)
    long_blocks = long_blocks.astype(jnp.bfloat16)
    returned = lax.all_to_all(long_blocks, everyone, split_axis=0, concat_axis=0, tiled=True)
    returned = returned.astype(jnp.float32)
    returned = returned.reshape(block_count, group_count, row_count, width).transpose(2, 1, 0, 3)
    long_tokens = returned.reshape(row_count, channels)
    mixed = query.astype(jnp.float32) * (long_tokens + skip_gain * gated)
    return mixed.astype(jnp.bfloat16)


def solution(mesh):
    in_specs = (P(("ctx", "grp"), None), P(), P(), P("ctx", None, "grp"), P("ctx", None, "grp"))
    out_specs = P(("ctx", "grp"), None)
    devices = mesh.shape["ctx"] * mesh.shape["grp"]

    def run(projected, conv_weight, skip_gain, spectrum_real, spectrum_imag):
        channels = conv_weight.shape[1] // 3
        wide = channels % devices == 0 and channels // devices >= 32
        body = channel_parallel if wide else per_device
        return jax.shard_map(
            body, mesh=mesh, in_specs=in_specs, out_specs=out_specs, check_vma=False
        )(projected, conv_weight, skip_gain, spectrum_real, spectrum_imag)

    return run
```

```python
import math

import jax
import jax.numpy as jnp
from jax import lax
from jax.sharding import PartitionSpec as P

TWO_PI = 2.0 * math.pi


def shifted(shard, axis, by):
    devices = lax.axis_size(axis)
    pairs = [(i, i + by) for i in range(devices) if 0 <= i + by < devices]
    return lax.ppermute(shard, axis, pairs)


def rotation(rows_index, cols_index, length, direction):
    product = rows_index[:, None] * cols_index[None, :] % length
    angles = product.astype(jnp.float32) * (TWO_PI / length)
    return (jnp.cos(angles), direction * jnp.sin(angles))


def complex_table(cos_part, sin_part):
    return jnp.stack([jnp.stack([cos_part, -sin_part]), jnp.stack([sin_part, cos_part])])


def contract(form, table, data, precision=lax.Precision.HIGHEST):
    return jnp.einsum(form, table, data, precision=precision, preferred_element_type=jnp.float32)


def contract_high(form, table, data):
    return contract(form, table, data, lax.Precision.HIGH)


def twist(data, turn_real, turn_imag):
    return jnp.stack(
        [data[0] * turn_real - data[1] * turn_imag, data[0] * turn_imag + data[1] * turn_real]
    )


def across_forward(blocks, token_index, fft_len):
    block_count = blocks.shape[0]
    frequency = jnp.arange(2 * block_count, dtype=jnp.int32)
    block_order = jnp.arange(block_count, dtype=jnp.int32)
    cos_table, sin_table = rotation(frequency, block_order, 2 * block_count, -1.0)
    accum = contract("pkj,jbc->pkbc", jnp.stack([cos_table, sin_table]), blocks)
    turn_real, turn_imag = rotation(frequency, token_index, fft_len, -1.0)
    return twist(accum, turn_real[:, :, None], turn_imag[:, :, None])


def within_block(data, direction):
    leading, length, lane_count = (data.shape[1], data.shape[2], data.shape[3])
    first_len = math.gcd(length, 256)
    second_len = length // first_len
    data = data.reshape(2, leading, second_len, first_len, lane_count)
    outer_index = jnp.arange(second_len, dtype=jnp.int32)
    inner_index = jnp.arange(first_len, dtype=jnp.int32)
    table_real, table_imag = rotation(outer_index, outer_index, second_len, direction)
    section = contract("pqkj,qxjbc->pxkbc", complex_table(table_real, table_imag), data)
    turn_real, turn_imag = rotation(outer_index, inner_index, length, direction)
    twisted = twist(section, turn_real[None, :, :, None], turn_imag[None, :, :, None])
    last_real, last_imag = rotation(inner_index, inner_index, first_len, direction)
    result = contract("pqgb,qxkbc->pxgkc", complex_table(last_real, last_imag), twisted)
    return result.reshape(2, leading, length, lane_count)


def across_inverse(data, fft_len):
    block_count = data.shape[1] // 2
    block_order = jnp.arange(block_count, dtype=jnp.int32)
    frequency = jnp.arange(2 * block_count, dtype=jnp.int32)
    cos_table, sin_table = rotation(block_order, frequency, 2 * block_count, 1.0)
    summed = contract("qjk,qkbc->jbc", jnp.stack([cos_table, -sin_table]), data)
    return summed * (1.0 / fft_len)


def per_device(projected, conv_weight, skip_gain, spectrum_real, spectrum_imag):
    channels = conv_weight.shape[1] // 3
    rim_rows = conv_weight.shape[0] - 1
    row_count = projected.shape[0]
    rim = shifted(projected[row_count - rim_rows :], ("ctx", "grp"), 1)
    extended = jnp.concatenate([rim, projected], axis=0)
    short = jnp.zeros((row_count, 3 * channels), jnp.float32)
    for offset in range(rim_rows + 1):
        short = short + conv_weight[offset] * extended[
            rim_rows - offset : rim_rows - offset + row_count
        ].astype(jnp.float32)
    short = short.astype(jnp.bfloat16)
    query = short[:, :channels]
    gated = short[:, channels : 2 * channels].astype(jnp.float32) * short[:, 2 * channels :].astype(
        jnp.float32
    )
    block_count = lax.axis_size("ctx")
    group_count = lax.axis_size("grp")
    block_len = row_count * group_count
    fft_len = 2 * block_len * block_count
    block_index = lax.axis_index("ctx")
    sliver = lax.all_to_all(gated, "grp", split_axis=1, concat_axis=0, tiled=True)
    piece_len = block_len // block_count
    token_index = block_index * piece_len + jnp.arange(piece_len, dtype=jnp.int32)
    front = across_forward(
        lax.all_to_all(sliver[None], "ctx", split_axis=1, concat_axis=0, tiled=True),
        token_index,
        fft_len,
    )
    spectra = within_block(
        lax.all_to_all(front, "ctx", split_axis=1, concat_axis=2, tiled=True), -1.0
    )
    filtered = twist(spectra, spectrum_real.astype(jnp.float32), spectrum_imag.astype(jnp.float32))
    restored = within_block(filtered, 1.0)
    local_freq = spectra.shape[1]
    frequency = block_index * local_freq + jnp.arange(local_freq, dtype=jnp.int32)
    turn_real, turn_imag = rotation(frequency, jnp.arange(block_len, dtype=jnp.int32), fft_len, 1.0)
    restored = twist(restored, turn_real[:, :, None], turn_imag[:, :, None])
    long_blocks = across_inverse(
        lax.all_to_all(restored, "ctx", split_axis=2, concat_axis=1, tiled=True), fft_len
    )
    long_sliver = lax.all_to_all(long_blocks, "ctx", split_axis=0, concat_axis=1, tiled=True)[0]
    long_tokens = lax.all_to_all(long_sliver, "grp", split_axis=0, concat_axis=1, tiled=True)
    mixed = query.astype(jnp.float32) * (long_tokens + skip_gain * gated)
    return mixed.astype(jnp.bfloat16)


def short_convolution(projected, conv_weight):
    channels = conv_weight.shape[1] // 3
    rim_rows = conv_weight.shape[0] - 1
    row_count = projected.shape[0]
    rim = shifted(projected[row_count - rim_rows :], ("ctx", "grp"), 1)
    extended = jnp.concatenate([rim, projected], axis=0)
    short = jnp.zeros((row_count, 3 * channels), jnp.float32)
    for offset in range(rim_rows + 1):
        short = short + conv_weight[offset] * extended[
            rim_rows - offset : rim_rows - offset + row_count
        ].astype(jnp.float32)
    short = short.astype(jnp.bfloat16)
    query = short[:, :channels]
    gated = short[:, channels : 2 * channels].astype(jnp.float32) * short[:, 2 * channels :].astype(
        jnp.float32
    )
    return query, gated


def angle_table(rows_index, cols_index, length):
    product = rows_index[:, None] * cols_index[None, :] % length
    angles = product.astype(jnp.float32) * (TWO_PI / length)
    return jnp.cos(angles), jnp.sin(angles)


def channel_parallel(projected, conv_weight, skip_gain, spectrum_real, spectrum_imag):
    query, gated = short_convolution(projected, conv_weight)
    row_count, channels = gated.shape
    block_count = lax.axis_size("ctx")
    group_count = lax.axis_size("grp")
    devices = block_count * group_count
    block_len = row_count * group_count
    residues = 2 * block_count
    fft_len = residues * block_len
    width = channels // devices
    everyone = ("ctx", "grp")

    outgoing = gated.reshape(row_count, group_count, block_count, width).transpose(0, 2, 1, 3)
    outgoing = outgoing.reshape(row_count, devices, width)
    outgoing = outgoing.astype(jnp.bfloat16)

    def spread(part):
        return lax.all_to_all(part, "ctx", split_axis=3, concat_axis=1, tiled=True)

    early = spread(jnp.stack([spectrum_real[0::2], spectrum_imag[0::2]]))
    early, outgoing = lax.optimization_barrier((early, outgoing))
    tokens = lax.all_to_all(outgoing, everyone, split_axis=1, concat_axis=0, tiled=True)
    tokens = tokens.reshape(block_count, block_len, width).astype(jnp.float32)

    tokens, late = lax.optimization_barrier(
        (tokens, jnp.stack([spectrum_real[1::2], spectrum_imag[1::2]]))
    )
    late = spread(late)
    spectrum = jnp.stack([early, late], axis=2).reshape(2, residues, block_len, width)
    spectrum = spectrum.transpose(0, 2, 3, 1).astype(jnp.float32)
    filter_real, filter_imag = spectrum[0], spectrum[1]

    residue = jnp.arange(residues, dtype=jnp.int32)
    block_order = jnp.arange(block_count, dtype=jnp.int32)
    position = jnp.arange(block_len, dtype=jnp.int32)

    across_cos, across_sin = angle_table(block_order, residue, residues)
    folded_real = contract_high("jpc,ja->pca", tokens, across_cos)
    folded_imag = -contract_high("jpc,ja->pca", tokens, across_sin)
    turn_cos, turn_sin = angle_table(position, residue, fft_len)
    turn_cos, turn_sin = turn_cos[:, None, :], turn_sin[:, None, :]
    twisted_real = folded_real * turn_cos + folded_imag * turn_sin
    twisted_imag = folded_imag * turn_cos - folded_real * turn_sin

    within_cos, within_sin = angle_table(position, position, block_len)
    lanes = width * residues

    def times(table_part, data, precision=lax.Precision.HIGH):
        return lax.dot_general(
            table_part,
            data.reshape(block_len, lanes),
            (((1,), (0,)), ((), ())),
            precision=precision,
            preferred_element_type=jnp.float32,
        ).reshape(block_len, width, residues)

    def inverse(table_part, data):
        return times(table_part, data, lax.Precision.DEFAULT)

    spectra_real = times(within_cos, twisted_real) + times(within_sin, twisted_imag)
    spectra_imag = times(within_cos, twisted_imag) - times(within_sin, twisted_real)
    product_real = spectra_real * filter_real - spectra_imag * filter_imag
    product_imag = spectra_real * filter_imag + spectra_imag * filter_real
    restored_real = inverse(within_cos, product_real) - inverse(within_sin, product_imag)
    restored_imag = inverse(within_cos, product_imag) + inverse(within_sin, product_real)
    unturned_real = restored_real * turn_cos - restored_imag * turn_sin
    unturned_imag = restored_real * turn_sin + restored_imag * turn_cos
    long_blocks = contract_high("ja,pca->jpc", across_cos, unturned_real) - contract_high(
        "ja,pca->jpc", across_sin, unturned_imag
    )
    long_blocks = (long_blocks * (1.0 / fft_len)).reshape(devices, row_count, width)
    long_blocks = long_blocks.astype(jnp.bfloat16)
    returned = lax.all_to_all(long_blocks, everyone, split_axis=0, concat_axis=0, tiled=True)
    returned = returned.astype(jnp.float32)
    returned = returned.reshape(block_count, group_count, row_count, width).transpose(2, 1, 0, 3)
    long_tokens = returned.reshape(row_count, channels)
    mixed = query.astype(jnp.float32) * (long_tokens + skip_gain * gated)
    return mixed.astype(jnp.bfloat16)


def solution(mesh):
    in_specs = (P(("ctx", "grp"), None), P(), P(), P("ctx", None, "grp"), P("ctx", None, "grp"))
    out_specs = P(("ctx", "grp"), None)
    devices = mesh.shape["ctx"] * mesh.shape["grp"]

    def run(projected, conv_weight, skip_gain, spectrum_real, spectrum_imag):
        channels = conv_weight.shape[1] // 3
        wide = channels % devices == 0 and channels // devices >= 32
        body = channel_parallel if wide else per_device
        return jax.shard_map(
            body, mesh=mesh, in_specs=in_specs, out_specs=out_specs, check_vma=False
        )(projected, conv_weight, skip_gain, spectrum_real, spectrum_imag)

    return run
```

```python
import math

import jax
import jax.numpy as jnp
from jax import lax
from jax.sharding import PartitionSpec as P

TWO_PI = 2.0 * math.pi


def shifted(shard, axis, by):
    devices = lax.axis_size(axis)
    pairs = [(i, i + by) for i in range(devices) if 0 <= i + by < devices]
    return lax.ppermute(shard, axis, pairs)


def rotation(rows_index, cols_index, length, direction):
    product = rows_index[:, None] * cols_index[None, :] % length
    angles = product.astype(jnp.float32) * (TWO_PI / length)
    return (jnp.cos(angles), direction * jnp.sin(angles))


def complex_table(cos_part, sin_part):
    return jnp.stack([jnp.stack([cos_part, -sin_part]), jnp.stack([sin_part, cos_part])])


def contract(form, table, data, precision=lax.Precision.HIGHEST):
    return jnp.einsum(form, table, data, precision=precision, preferred_element_type=jnp.float32)


def contract_high(form, table, data):
    return contract(form, table, data, lax.Precision.HIGH)


def twist(data, turn_real, turn_imag):
    return jnp.stack(
        [data[0] * turn_real - data[1] * turn_imag, data[0] * turn_imag + data[1] * turn_real]
    )


def across_forward(blocks, token_index, fft_len):
    block_count = blocks.shape[0]
    frequency = jnp.arange(2 * block_count, dtype=jnp.int32)
    block_order = jnp.arange(block_count, dtype=jnp.int32)
    cos_table, sin_table = rotation(frequency, block_order, 2 * block_count, -1.0)
    accum = contract("pkj,jbc->pkbc", jnp.stack([cos_table, sin_table]), blocks)
    turn_real, turn_imag = rotation(frequency, token_index, fft_len, -1.0)
    return twist(accum, turn_real[:, :, None], turn_imag[:, :, None])


def within_block(data, direction):
    leading, length, lane_count = (data.shape[1], data.shape[2], data.shape[3])
    first_len = math.gcd(length, 256)
    second_len = length // first_len
    data = data.reshape(2, leading, second_len, first_len, lane_count)
    outer_index = jnp.arange(second_len, dtype=jnp.int32)
    inner_index = jnp.arange(first_len, dtype=jnp.int32)
    table_real, table_imag = rotation(outer_index, outer_index, second_len, direction)
    section = contract("pqkj,qxjbc->pxkbc", complex_table(table_real, table_imag), data)
    turn_real, turn_imag = rotation(outer_index, inner_index, length, direction)
    twisted = twist(section, turn_real[None, :, :, None], turn_imag[None, :, :, None])
    last_real, last_imag = rotation(inner_index, inner_index, first_len, direction)
    result = contract("pqgb,qxkbc->pxgkc", complex_table(last_real, last_imag), twisted)
    return result.reshape(2, leading, length, lane_count)


def across_inverse(data, fft_len):
    block_count = data.shape[1] // 2
    block_order = jnp.arange(block_count, dtype=jnp.int32)
    frequency = jnp.arange(2 * block_count, dtype=jnp.int32)
    cos_table, sin_table = rotation(block_order, frequency, 2 * block_count, 1.0)
    summed = contract("qjk,qkbc->jbc", jnp.stack([cos_table, -sin_table]), data)
    return summed * (1.0 / fft_len)


def per_device(projected, conv_weight, skip_gain, spectrum_real, spectrum_imag):
    channels = conv_weight.shape[1] // 3
    rim_rows = conv_weight.shape[0] - 1
    row_count = projected.shape[0]
    rim = shifted(projected[row_count - rim_rows :], ("ctx", "grp"), 1)
    extended = jnp.concatenate([rim, projected], axis=0)
    short = jnp.zeros((row_count, 3 * channels), jnp.float32)
    for offset in range(rim_rows + 1):
        short = short + conv_weight[offset] * extended[
            rim_rows - offset : rim_rows - offset + row_count
        ].astype(jnp.float32)
    short = short.astype(jnp.bfloat16)
    query = short[:, :channels]
    gated = short[:, channels : 2 * channels].astype(jnp.float32) * short[:, 2 * channels :].astype(
        jnp.float32
    )
    block_count = lax.axis_size("ctx")
    group_count = lax.axis_size("grp")
    block_len = row_count * group_count
    fft_len = 2 * block_len * block_count
    block_index = lax.axis_index("ctx")
    sliver = lax.all_to_all(gated, "grp", split_axis=1, concat_axis=0, tiled=True)
    piece_len = block_len // block_count
    token_index = block_index * piece_len + jnp.arange(piece_len, dtype=jnp.int32)
    front = across_forward(
        lax.all_to_all(sliver[None], "ctx", split_axis=1, concat_axis=0, tiled=True),
        token_index,
        fft_len,
    )
    spectra = within_block(
        lax.all_to_all(front, "ctx", split_axis=1, concat_axis=2, tiled=True), -1.0
    )
    filtered = twist(spectra, spectrum_real.astype(jnp.float32), spectrum_imag.astype(jnp.float32))
    restored = within_block(filtered, 1.0)
    local_freq = spectra.shape[1]
    frequency = block_index * local_freq + jnp.arange(local_freq, dtype=jnp.int32)
    turn_real, turn_imag = rotation(frequency, jnp.arange(block_len, dtype=jnp.int32), fft_len, 1.0)
    restored = twist(restored, turn_real[:, :, None], turn_imag[:, :, None])
    long_blocks = across_inverse(
        lax.all_to_all(restored, "ctx", split_axis=2, concat_axis=1, tiled=True), fft_len
    )
    long_sliver = lax.all_to_all(long_blocks, "ctx", split_axis=0, concat_axis=1, tiled=True)[0]
    long_tokens = lax.all_to_all(long_sliver, "grp", split_axis=0, concat_axis=1, tiled=True)
    mixed = query.astype(jnp.float32) * (long_tokens + skip_gain * gated)
    return mixed.astype(jnp.bfloat16)


def short_convolution(projected, conv_weight):
    channels = conv_weight.shape[1] // 3
    rim_rows = conv_weight.shape[0] - 1
    row_count = projected.shape[0]
    rim = shifted(projected[row_count - rim_rows :], ("ctx", "grp"), 1)
    extended = jnp.concatenate([rim, projected], axis=0)
    short = jnp.zeros((row_count, 3 * channels), jnp.float32)
    for offset in range(rim_rows + 1):
        short = short + conv_weight[offset] * extended[
            rim_rows - offset : rim_rows - offset + row_count
        ].astype(jnp.float32)
    short = short.astype(jnp.bfloat16)
    query = short[:, :channels]
    gated = short[:, channels : 2 * channels].astype(jnp.float32) * short[:, 2 * channels :].astype(
        jnp.float32
    )
    return query, gated


def angle_table(rows_index, cols_index, length):
    product = rows_index[:, None] * cols_index[None, :] % length
    angles = product.astype(jnp.float32) * (TWO_PI / length)
    return jnp.cos(angles), jnp.sin(angles)


def channel_parallel(projected, conv_weight, skip_gain, spectrum_real, spectrum_imag):
    query, gated = short_convolution(projected, conv_weight)
    row_count, channels = gated.shape
    block_count = lax.axis_size("ctx")
    group_count = lax.axis_size("grp")
    devices = block_count * group_count
    block_len = row_count * group_count
    residues = 2 * block_count
    fft_len = residues * block_len
    width = channels // devices
    everyone = ("ctx", "grp")

    outgoing = gated.reshape(row_count, group_count, block_count, width).transpose(0, 2, 1, 3)
    outgoing = outgoing.reshape(row_count, devices, width)
    outgoing = outgoing.astype(jnp.bfloat16)
    tokens = lax.all_to_all(outgoing, everyone, split_axis=1, concat_axis=0, tiled=True)
    tokens = tokens.reshape(block_count, block_len, width).astype(jnp.float32).transpose(0, 2, 1)

    local_residues, spectrum_len, half = spectrum_real.shape
    spectrum = jnp.stack([spectrum_real, spectrum_imag])
    spectrum = spectrum.reshape(2, local_residues, spectrum_len, block_count, width)
    spectrum = spectrum.transpose(3, 0, 1, 4, 2)
    tokens, spectrum = lax.optimization_barrier((tokens, spectrum))
    spectrum = lax.all_to_all(spectrum, "ctx", split_axis=0, concat_axis=0, tiled=True)
    spectrum = spectrum.transpose(1, 0, 2, 3, 4).reshape(2, residues, width, spectrum_len)
    filter_real, filter_imag = spectrum[0].astype(jnp.float32), spectrum[1].astype(jnp.float32)

    residue = jnp.arange(residues, dtype=jnp.int32)
    block_order = jnp.arange(block_count, dtype=jnp.int32)
    position = jnp.arange(block_len, dtype=jnp.int32)

    across_cos, across_sin = angle_table(block_order, residue, residues)
    folded_real = contract_high("ja,jcp->acp", across_cos, tokens)
    folded_imag = -contract_high("ja,jcp->acp", across_sin, tokens)
    turn_cos, turn_sin = angle_table(residue, position, fft_len)
    turn_cos, turn_sin = turn_cos[:, None, :], turn_sin[:, None, :]
    twisted_real = folded_real * turn_cos + folded_imag * turn_sin
    twisted_imag = folded_imag * turn_cos - folded_real * turn_sin

    within_cos, within_sin = angle_table(position, position, block_len)
    rows = residues * width

    def times(table_part, data, precision=lax.Precision.HIGH):
        return lax.dot_general(
            data.reshape(rows, block_len),
            table_part,
            (((1,), (0,)), ((), ())),
            precision=precision,
            preferred_element_type=jnp.float32,
        ).reshape(residues, width, block_len)

    def inverse(table_part, data):
        return times(table_part, data, lax.Precision.DEFAULT)

    spectra_real = times(within_cos, twisted_real) + times(within_sin, twisted_imag)
    spectra_imag = times(within_cos, twisted_imag) - times(within_sin, twisted_real)
    product_real = spectra_real * filter_real - spectra_imag * filter_imag
    product_imag = spectra_real * filter_imag + spectra_imag * filter_real
    restored_real = inverse(within_cos, product_real) - inverse(within_sin, product_imag)
    restored_imag = inverse(within_cos, product_imag) + inverse(within_sin, product_real)
    unturned_real = restored_real * turn_cos - restored_imag * turn_sin
    unturned_imag = restored_real * turn_sin + restored_imag * turn_cos
    long_blocks = contract_high("ja,acp->jcp", across_cos, unturned_real) - contract_high(
        "ja,acp->jcp", across_sin, unturned_imag
    )
    halves = block_len // row_count
    long_blocks = long_blocks.reshape(block_count, width, halves, row_count).transpose(0, 2, 3, 1)
    long_blocks = (long_blocks * (1.0 / fft_len)).reshape(devices, row_count, width)
    long_blocks = long_blocks.astype(jnp.bfloat16)
    returned = lax.all_to_all(long_blocks, everyone, split_axis=0, concat_axis=0, tiled=True)
    returned = returned.astype(jnp.float32)
    returned = returned.reshape(block_count, group_count, row_count, width).transpose(2, 1, 0, 3)
    long_tokens = returned.reshape(row_count, channels)
    mixed = query.astype(jnp.float32) * (long_tokens + skip_gain * gated)
    return mixed.astype(jnp.bfloat16)


def solution(mesh):
    in_specs = (P(("ctx", "grp"), None), P(), P(), P("ctx", None, "grp"), P("ctx", None, "grp"))
    out_specs = P(("ctx", "grp"), None)
    devices = mesh.shape["ctx"] * mesh.shape["grp"]

    def run(projected, conv_weight, skip_gain, spectrum_real, spectrum_imag):
        channels = conv_weight.shape[1] // 3
        wide = channels % devices == 0 and channels // devices >= 32
        body = channel_parallel if wide else per_device
        return jax.shard_map(
            body, mesh=mesh, in_specs=in_specs, out_specs=out_specs, check_vma=False
        )(projected, conv_weight, skip_gain, spectrum_real, spectrum_imag)

    return run
```

```python
import math

import jax
import jax.numpy as jnp
from jax import lax
from jax.sharding import PartitionSpec as P

TWO_PI = 2.0 * math.pi


def shifted(shard, axis, by):
    devices = lax.axis_size(axis)
    pairs = [(i, i + by) for i in range(devices) if 0 <= i + by < devices]
    return lax.ppermute(shard, axis, pairs)


def rotation(rows_index, cols_index, length, direction):
    product = rows_index[:, None] * cols_index[None, :] % length
    angles = product.astype(jnp.float32) * (TWO_PI / length)
    return (jnp.cos(angles), direction * jnp.sin(angles))


def complex_table(cos_part, sin_part):
    return jnp.stack([jnp.stack([cos_part, -sin_part]), jnp.stack([sin_part, cos_part])])


def contract(form, table, data, precision=lax.Precision.HIGHEST):
    return jnp.einsum(form, table, data, precision=precision, preferred_element_type=jnp.float32)


def contract_high(form, table, data):
    return contract(form, table, data, lax.Precision.HIGH)


def twist(data, turn_real, turn_imag):
    return jnp.stack(
        [data[0] * turn_real - data[1] * turn_imag, data[0] * turn_imag + data[1] * turn_real]
    )


def across_forward(blocks, token_index, fft_len):
    block_count = blocks.shape[0]
    frequency = jnp.arange(2 * block_count, dtype=jnp.int32)
    block_order = jnp.arange(block_count, dtype=jnp.int32)
    cos_table, sin_table = rotation(frequency, block_order, 2 * block_count, -1.0)
    accum = contract("pkj,jbc->pkbc", jnp.stack([cos_table, sin_table]), blocks)
    turn_real, turn_imag = rotation(frequency, token_index, fft_len, -1.0)
    return twist(accum, turn_real[:, :, None], turn_imag[:, :, None])


def within_block(data, direction):
    leading, length, lane_count = (data.shape[1], data.shape[2], data.shape[3])
    first_len = math.gcd(length, 256)
    second_len = length // first_len
    data = data.reshape(2, leading, second_len, first_len, lane_count)
    outer_index = jnp.arange(second_len, dtype=jnp.int32)
    inner_index = jnp.arange(first_len, dtype=jnp.int32)
    table_real, table_imag = rotation(outer_index, outer_index, second_len, direction)
    section = contract("pqkj,qxjbc->pxkbc", complex_table(table_real, table_imag), data)
    turn_real, turn_imag = rotation(outer_index, inner_index, length, direction)
    twisted = twist(section, turn_real[None, :, :, None], turn_imag[None, :, :, None])
    last_real, last_imag = rotation(inner_index, inner_index, first_len, direction)
    result = contract("pqgb,qxkbc->pxgkc", complex_table(last_real, last_imag), twisted)
    return result.reshape(2, leading, length, lane_count)


def across_inverse(data, fft_len):
    block_count = data.shape[1] // 2
    block_order = jnp.arange(block_count, dtype=jnp.int32)
    frequency = jnp.arange(2 * block_count, dtype=jnp.int32)
    cos_table, sin_table = rotation(block_order, frequency, 2 * block_count, 1.0)
    summed = contract("qjk,qkbc->jbc", jnp.stack([cos_table, -sin_table]), data)
    return summed * (1.0 / fft_len)


def per_device(projected, conv_weight, skip_gain, spectrum_real, spectrum_imag):
    channels = conv_weight.shape[1] // 3
    rim_rows = conv_weight.shape[0] - 1
    row_count = projected.shape[0]
    rim = shifted(projected[row_count - rim_rows :], ("ctx", "grp"), 1)
    extended = jnp.concatenate([rim, projected], axis=0)
    short = jnp.zeros((row_count, 3 * channels), jnp.float32)
    for offset in range(rim_rows + 1):
        short = short + conv_weight[offset] * extended[
            rim_rows - offset : rim_rows - offset + row_count
        ].astype(jnp.float32)
    short = short.astype(jnp.bfloat16)
    query = short[:, :channels]
    gated = short[:, channels : 2 * channels].astype(jnp.float32) * short[:, 2 * channels :].astype(
        jnp.float32
    )
    block_count = lax.axis_size("ctx")
    group_count = lax.axis_size("grp")
    block_len = row_count * group_count
    fft_len = 2 * block_len * block_count
    block_index = lax.axis_index("ctx")
    sliver = lax.all_to_all(gated, "grp", split_axis=1, concat_axis=0, tiled=True)
    piece_len = block_len // block_count
    token_index = block_index * piece_len + jnp.arange(piece_len, dtype=jnp.int32)
    front = across_forward(
        lax.all_to_all(sliver[None], "ctx", split_axis=1, concat_axis=0, tiled=True),
        token_index,
        fft_len,
    )
    spectra = within_block(
        lax.all_to_all(front, "ctx", split_axis=1, concat_axis=2, tiled=True), -1.0
    )
    filtered = twist(spectra, spectrum_real.astype(jnp.float32), spectrum_imag.astype(jnp.float32))
    restored = within_block(filtered, 1.0)
    local_freq = spectra.shape[1]
    frequency = block_index * local_freq + jnp.arange(local_freq, dtype=jnp.int32)
    turn_real, turn_imag = rotation(frequency, jnp.arange(block_len, dtype=jnp.int32), fft_len, 1.0)
    restored = twist(restored, turn_real[:, :, None], turn_imag[:, :, None])
    long_blocks = across_inverse(
        lax.all_to_all(restored, "ctx", split_axis=2, concat_axis=1, tiled=True), fft_len
    )
    long_sliver = lax.all_to_all(long_blocks, "ctx", split_axis=0, concat_axis=1, tiled=True)[0]
    long_tokens = lax.all_to_all(long_sliver, "grp", split_axis=0, concat_axis=1, tiled=True)
    mixed = query.astype(jnp.float32) * (long_tokens + skip_gain * gated)
    return mixed.astype(jnp.bfloat16)


def short_convolution(projected, conv_weight):
    channels = conv_weight.shape[1] // 3
    rim_rows = conv_weight.shape[0] - 1
    row_count = projected.shape[0]
    rim = shifted(projected[row_count - rim_rows :], ("ctx", "grp"), 1)
    extended = jnp.concatenate([rim, projected], axis=0)
    short = jnp.zeros((row_count, 3 * channels), jnp.float32)
    for offset in range(rim_rows + 1):
        short = short + conv_weight[offset] * extended[
            rim_rows - offset : rim_rows - offset + row_count
        ].astype(jnp.float32)
    short = short.astype(jnp.bfloat16)
    query = short[:, :channels]
    gated = short[:, channels : 2 * channels].astype(jnp.float32) * short[:, 2 * channels :].astype(
        jnp.float32
    )
    return query, gated


def angle_table(rows_index, cols_index, length):
    product = rows_index[:, None] * cols_index[None, :] % length
    angles = product.astype(jnp.float32) * (TWO_PI / length)
    return jnp.cos(angles), jnp.sin(angles)


def channel_parallel(projected, conv_weight, skip_gain, spectrum_real, spectrum_imag):
    query, gated = short_convolution(projected, conv_weight)
    row_count, channels = gated.shape
    block_count = lax.axis_size("ctx")
    group_count = lax.axis_size("grp")
    devices = block_count * group_count
    block_len = row_count * group_count
    residues = 2 * block_count
    fft_len = residues * block_len
    width = channels // devices
    everyone = ("ctx", "grp")

    outgoing = gated.reshape(row_count, group_count, block_count, width).transpose(0, 2, 1, 3)
    outgoing = outgoing.reshape(row_count, devices, width)
    outgoing = outgoing.astype(jnp.bfloat16)
    tokens = lax.all_to_all(outgoing, everyone, split_axis=1, concat_axis=0, tiled=True)

    local_residues, spectrum_len, half = spectrum_real.shape
    spectrum = jnp.stack([spectrum_real, spectrum_imag])
    spectrum = spectrum.reshape(2, local_residues, spectrum_len, block_count, width)
    spectrum = spectrum.transpose(3, 0, 1, 4, 2)
    tokens, spectrum = lax.optimization_barrier((tokens, spectrum))
    spectrum = lax.all_to_all(spectrum, "ctx", split_axis=0, concat_axis=0, tiled=True)
    spectrum = spectrum.transpose(1, 0, 2, 3, 4).reshape(2, residues, width, spectrum_len)
    filter_real, filter_imag = spectrum[0].astype(jnp.float32), spectrum[1].astype(jnp.float32)
    tokens = tokens.reshape(block_count, block_len, width).astype(jnp.float32).transpose(0, 2, 1)

    residue = jnp.arange(residues, dtype=jnp.int32)
    block_order = jnp.arange(block_count, dtype=jnp.int32)
    position = jnp.arange(block_len, dtype=jnp.int32)

    across_cos, across_sin = angle_table(block_order, residue, residues)
    folded_real = contract_high("ja,jcp->acp", across_cos, tokens)
    folded_imag = -contract_high("ja,jcp->acp", across_sin, tokens)
    turn_cos, turn_sin = angle_table(residue, position, fft_len)
    turn_cos, turn_sin = turn_cos[:, None, :], turn_sin[:, None, :]
    twisted_real = folded_real * turn_cos + folded_imag * turn_sin
    twisted_imag = folded_imag * turn_cos - folded_real * turn_sin

    within_cos, within_sin = angle_table(position, position, block_len)
    rows = residues * width

    def times(table_part, data, precision=lax.Precision.HIGH):
        return lax.dot_general(
            data.reshape(rows, block_len),
            table_part,
            (((1,), (0,)), ((), ())),
            precision=precision,
            preferred_element_type=jnp.float32,
        ).reshape(residues, width, block_len)

    def inverse(table_part, data):
        return times(table_part, data, lax.Precision.DEFAULT)

    spectra_real = times(within_cos, twisted_real) + times(within_sin, twisted_imag)
    spectra_imag = times(within_cos, twisted_imag) - times(within_sin, twisted_real)
    product_real = spectra_real * filter_real - spectra_imag * filter_imag
    product_imag = spectra_real * filter_imag + spectra_imag * filter_real
    restored_real = inverse(within_cos, product_real) - inverse(within_sin, product_imag)
    restored_imag = inverse(within_cos, product_imag) + inverse(within_sin, product_real)
    unturned_real = restored_real * turn_cos - restored_imag * turn_sin
    unturned_imag = restored_real * turn_sin + restored_imag * turn_cos
    long_blocks = contract_high("ja,acp->jcp", across_cos, unturned_real) - contract_high(
        "ja,acp->jcp", across_sin, unturned_imag
    )
    halves = block_len // row_count
    long_blocks = long_blocks.reshape(block_count, width, halves, row_count).transpose(0, 2, 3, 1)
    long_blocks = (long_blocks * (1.0 / fft_len)).reshape(devices, row_count, width)
    long_blocks = long_blocks.astype(jnp.bfloat16)
    returned = lax.all_to_all(long_blocks, everyone, split_axis=0, concat_axis=0, tiled=True)
    returned = returned.astype(jnp.float32)
    returned = returned.reshape(block_count, group_count, row_count, width).transpose(2, 1, 0, 3)
    long_tokens = returned.reshape(row_count, channels)
    mixed = query.astype(jnp.float32) * (long_tokens + skip_gain * gated)
    return mixed.astype(jnp.bfloat16)


def solution(mesh):
    in_specs = (P(("ctx", "grp"), None), P(), P(), P("ctx", None, "grp"), P("ctx", None, "grp"))
    out_specs = P(("ctx", "grp"), None)
    devices = mesh.shape["ctx"] * mesh.shape["grp"]

    def run(projected, conv_weight, skip_gain, spectrum_real, spectrum_imag):
        channels = conv_weight.shape[1] // 3
        wide = channels % devices == 0 and channels // devices >= 32
        body = channel_parallel if wide else per_device
        return jax.shard_map(
            body, mesh=mesh, in_specs=in_specs, out_specs=out_specs, check_vma=False
        )(projected, conv_weight, skip_gain, spectrum_real, spectrum_imag)

    return run
```

```python
import math

import jax
import jax.numpy as jnp
from jax import lax
from jax.sharding import PartitionSpec as P

TWO_PI = 2.0 * math.pi


def shifted(shard, axis, by):
    devices = lax.axis_size(axis)
    pairs = [(i, i + by) for i in range(devices) if 0 <= i + by < devices]
    return lax.ppermute(shard, axis, pairs)


def rotation(rows_index, cols_index, length, direction):
    product = rows_index[:, None] * cols_index[None, :] % length
    angles = product.astype(jnp.float32) * (TWO_PI / length)
    return (jnp.cos(angles), direction * jnp.sin(angles))


def complex_table(cos_part, sin_part):
    return jnp.stack([jnp.stack([cos_part, -sin_part]), jnp.stack([sin_part, cos_part])])


def contract(form, table, data, precision=lax.Precision.HIGHEST):
    return jnp.einsum(form, table, data, precision=precision, preferred_element_type=jnp.float32)


def contract_high(form, table, data):
    return contract(form, table, data, lax.Precision.HIGH)


def twist(data, turn_real, turn_imag):
    return jnp.stack(
        [data[0] * turn_real - data[1] * turn_imag, data[0] * turn_imag + data[1] * turn_real]
    )


def across_forward(blocks, token_index, fft_len):
    block_count = blocks.shape[0]
    frequency = jnp.arange(2 * block_count, dtype=jnp.int32)
    block_order = jnp.arange(block_count, dtype=jnp.int32)
    cos_table, sin_table = rotation(frequency, block_order, 2 * block_count, -1.0)
    accum = contract("pkj,jbc->pkbc", jnp.stack([cos_table, sin_table]), blocks)
    turn_real, turn_imag = rotation(frequency, token_index, fft_len, -1.0)
    return twist(accum, turn_real[:, :, None], turn_imag[:, :, None])


def within_block(data, direction):
    leading, length, lane_count = (data.shape[1], data.shape[2], data.shape[3])
    first_len = math.gcd(length, 256)
    second_len = length // first_len
    data = data.reshape(2, leading, second_len, first_len, lane_count)
    outer_index = jnp.arange(second_len, dtype=jnp.int32)
    inner_index = jnp.arange(first_len, dtype=jnp.int32)
    table_real, table_imag = rotation(outer_index, outer_index, second_len, direction)
    section = contract("pqkj,qxjbc->pxkbc", complex_table(table_real, table_imag), data)
    turn_real, turn_imag = rotation(outer_index, inner_index, length, direction)
    twisted = twist(section, turn_real[None, :, :, None], turn_imag[None, :, :, None])
    last_real, last_imag = rotation(inner_index, inner_index, first_len, direction)
    result = contract("pqgb,qxkbc->pxgkc", complex_table(last_real, last_imag), twisted)
    return result.reshape(2, leading, length, lane_count)


def across_inverse(data, fft_len):
    block_count = data.shape[1] // 2
    block_order = jnp.arange(block_count, dtype=jnp.int32)
    frequency = jnp.arange(2 * block_count, dtype=jnp.int32)
    cos_table, sin_table = rotation(block_order, frequency, 2 * block_count, 1.0)
    summed = contract("qjk,qkbc->jbc", jnp.stack([cos_table, -sin_table]), data)
    return summed * (1.0 / fft_len)


def per_device(projected, conv_weight, skip_gain, spectrum_real, spectrum_imag):
    channels = conv_weight.shape[1] // 3
    rim_rows = conv_weight.shape[0] - 1
    row_count = projected.shape[0]
    rim = shifted(projected[row_count - rim_rows :], ("ctx", "grp"), 1)
    extended = jnp.concatenate([rim, projected], axis=0)
    short = jnp.zeros((row_count, 3 * channels), jnp.float32)
    for offset in range(rim_rows + 1):
        short = short + conv_weight[offset] * extended[
            rim_rows - offset : rim_rows - offset + row_count
        ].astype(jnp.float32)
    short = short.astype(jnp.bfloat16)
    query = short[:, :channels]
    gated = short[:, channels : 2 * channels].astype(jnp.float32) * short[:, 2 * channels :].astype(
        jnp.float32
    )
    block_count = lax.axis_size("ctx")
    group_count = lax.axis_size("grp")
    block_len = row_count * group_count
    fft_len = 2 * block_len * block_count
    block_index = lax.axis_index("ctx")
    sliver = lax.all_to_all(gated, "grp", split_axis=1, concat_axis=0, tiled=True)
    piece_len = block_len // block_count
    token_index = block_index * piece_len + jnp.arange(piece_len, dtype=jnp.int32)
    front = across_forward(
        lax.all_to_all(sliver[None], "ctx", split_axis=1, concat_axis=0, tiled=True),
        token_index,
        fft_len,
    )
    spectra = within_block(
        lax.all_to_all(front, "ctx", split_axis=1, concat_axis=2, tiled=True), -1.0
    )
    filtered = twist(spectra, spectrum_real.astype(jnp.float32), spectrum_imag.astype(jnp.float32))
    restored = within_block(filtered, 1.0)
    local_freq = spectra.shape[1]
    frequency = block_index * local_freq + jnp.arange(local_freq, dtype=jnp.int32)
    turn_real, turn_imag = rotation(frequency, jnp.arange(block_len, dtype=jnp.int32), fft_len, 1.0)
    restored = twist(restored, turn_real[:, :, None], turn_imag[:, :, None])
    long_blocks = across_inverse(
        lax.all_to_all(restored, "ctx", split_axis=2, concat_axis=1, tiled=True), fft_len
    )
    long_sliver = lax.all_to_all(long_blocks, "ctx", split_axis=0, concat_axis=1, tiled=True)[0]
    long_tokens = lax.all_to_all(long_sliver, "grp", split_axis=0, concat_axis=1, tiled=True)
    mixed = query.astype(jnp.float32) * (long_tokens + skip_gain * gated)
    return mixed.astype(jnp.bfloat16)


def short_convolution(projected, conv_weight):
    channels = conv_weight.shape[1] // 3
    rim_rows = conv_weight.shape[0] - 1
    row_count = projected.shape[0]
    rim = shifted(projected[row_count - rim_rows :], ("ctx", "grp"), 1)
    extended = jnp.concatenate([rim, projected], axis=0)
    short = jnp.zeros((row_count, 3 * channels), jnp.float32)
    for offset in range(rim_rows + 1):
        short = short + conv_weight[offset] * extended[
            rim_rows - offset : rim_rows - offset + row_count
        ].astype(jnp.float32)
    short = short.astype(jnp.bfloat16)
    query = short[:, :channels]
    gated = short[:, channels : 2 * channels].astype(jnp.float32) * short[:, 2 * channels :].astype(
        jnp.float32
    )
    return query, gated


def angle_table(rows_index, cols_index, length):
    product = rows_index[:, None] * cols_index[None, :] % length
    angles = product.astype(jnp.float32) * (TWO_PI / length)
    return jnp.cos(angles), jnp.sin(angles)


def channel_parallel(projected, conv_weight, skip_gain, spectrum_real, spectrum_imag):
    query, gated = short_convolution(projected, conv_weight)
    row_count, channels = gated.shape
    block_count = lax.axis_size("ctx")
    group_count = lax.axis_size("grp")
    devices = block_count * group_count
    block_len = row_count * group_count
    residues = 2 * block_count
    fft_len = residues * block_len
    width = channels // devices
    everyone = ("ctx", "grp")

    outgoing = gated.reshape(row_count, group_count, block_count, width).transpose(0, 2, 1, 3)
    outgoing = outgoing.reshape(row_count, devices, width)
    outgoing = outgoing.astype(jnp.bfloat16)
    tokens = lax.all_to_all(outgoing, everyone, split_axis=1, concat_axis=0, tiled=True)
    tokens = tokens.reshape(block_count, block_len, width).astype(jnp.float32)

    tokens, spectrum = lax.optimization_barrier((tokens, jnp.stack([spectrum_real, spectrum_imag])))
    spectrum = lax.all_to_all(spectrum, "ctx", split_axis=3, concat_axis=1, tiled=True)
    spectrum = spectrum.transpose(0, 2, 3, 1).astype(jnp.float32)
    filter_real, filter_imag = spectrum[0], spectrum[1]

    residue = jnp.arange(residues, dtype=jnp.int32)
    block_order = jnp.arange(block_count, dtype=jnp.int32)
    position = jnp.arange(block_len, dtype=jnp.int32)

    across_cos, across_sin = angle_table(block_order, residue, residues)
    folded_real = contract_high("jpc,ja->pca", tokens, across_cos)
    folded_imag = -contract_high("jpc,ja->pca", tokens, across_sin)
    turn_cos, turn_sin = angle_table(position, residue, fft_len)
    turn_cos, turn_sin = turn_cos[:, None, :], turn_sin[:, None, :]
    twisted_real = folded_real * turn_cos + folded_imag * turn_sin
    twisted_imag = folded_imag * turn_cos - folded_real * turn_sin

    within_cos, within_sin = angle_table(position, position, block_len)
    lanes = width * residues

    def times(table_part, data, precision=lax.Precision.HIGH):
        return lax.dot_general(
            table_part,
            data.reshape(block_len, lanes),
            (((1,), (0,)), ((), ())),
            precision=precision,
            preferred_element_type=jnp.float32,
        ).reshape(block_len, width, residues)

    def inverse(table_part, data):
        return times(table_part, data, lax.Precision.DEFAULT)

    spectra_real = times(within_cos, twisted_real) + times(within_sin, twisted_imag)
    spectra_imag = times(within_cos, twisted_imag) - times(within_sin, twisted_real)
    product_real = spectra_real * filter_real - spectra_imag * filter_imag
    product_imag = spectra_real * filter_imag + spectra_imag * filter_real
    product = jnp.stack([product_real, product_imag]).reshape(2 * block_len, lanes)

    def inverse_part(left, right):
        return lax.dot_general(
            jnp.concatenate([left, right], axis=1),
            product,
            (((1,), (0,)), ((), ())),
            precision=lax.Precision.DEFAULT,
            preferred_element_type=jnp.float32,
        ).reshape(block_len, width, residues)

    restored_real = inverse_part(within_cos, -within_sin)
    restored_imag = inverse_part(within_sin, within_cos)
    unturned_real = restored_real * turn_cos - restored_imag * turn_sin
    unturned_imag = restored_real * turn_sin + restored_imag * turn_cos
    long_blocks = contract_high("ja,pca->jpc", across_cos, unturned_real) - contract_high(
        "ja,pca->jpc", across_sin, unturned_imag
    )
    long_blocks = (long_blocks * (1.0 / fft_len)).reshape(devices, row_count, width)
    long_blocks = long_blocks.astype(jnp.bfloat16)
    returned = lax.all_to_all(long_blocks, everyone, split_axis=0, concat_axis=0, tiled=True)
    returned = returned.astype(jnp.float32)
    returned = returned.reshape(block_count, group_count, row_count, width).transpose(2, 1, 0, 3)
    long_tokens = returned.reshape(row_count, channels)
    mixed = query.astype(jnp.float32) * (long_tokens + skip_gain * gated)
    return mixed.astype(jnp.bfloat16)


def solution(mesh):
    in_specs = (P(("ctx", "grp"), None), P(), P(), P("ctx", None, "grp"), P("ctx", None, "grp"))
    out_specs = P(("ctx", "grp"), None)
    devices = mesh.shape["ctx"] * mesh.shape["grp"]

    def run(projected, conv_weight, skip_gain, spectrum_real, spectrum_imag):
        channels = conv_weight.shape[1] // 3
        wide = channels % devices == 0 and channels // devices >= 32
        body = channel_parallel if wide else per_device
        return jax.shard_map(
            body, mesh=mesh, in_specs=in_specs, out_specs=out_specs, check_vma=False
        )(projected, conv_weight, skip_gain, spectrum_real, spectrum_imag)

    return run
```

```python
import math

import jax
import jax.numpy as jnp
from jax import lax
from jax.sharding import PartitionSpec as P

TWO_PI = 2.0 * math.pi


def shifted(shard, axis, by):
    devices = lax.axis_size(axis)
    pairs = [(i, i + by) for i in range(devices) if 0 <= i + by < devices]
    return lax.ppermute(shard, axis, pairs)


def rotation(rows_index, cols_index, length, direction):
    product = rows_index[:, None] * cols_index[None, :] % length
    angles = product.astype(jnp.float32) * (TWO_PI / length)
    return (jnp.cos(angles), direction * jnp.sin(angles))


def complex_table(cos_part, sin_part):
    return jnp.stack([jnp.stack([cos_part, -sin_part]), jnp.stack([sin_part, cos_part])])


def contract(form, table, data, precision=lax.Precision.HIGHEST):
    return jnp.einsum(form, table, data, precision=precision, preferred_element_type=jnp.float32)


def contract_high(form, table, data):
    return contract(form, table, data, lax.Precision.HIGH)


def twist(data, turn_real, turn_imag):
    return jnp.stack(
        [data[0] * turn_real - data[1] * turn_imag, data[0] * turn_imag + data[1] * turn_real]
    )


def across_forward(blocks, token_index, fft_len):
    block_count = blocks.shape[0]
    frequency = jnp.arange(2 * block_count, dtype=jnp.int32)
    block_order = jnp.arange(block_count, dtype=jnp.int32)
    cos_table, sin_table = rotation(frequency, block_order, 2 * block_count, -1.0)
    accum = contract("pkj,jbc->pkbc", jnp.stack([cos_table, sin_table]), blocks)
    turn_real, turn_imag = rotation(frequency, token_index, fft_len, -1.0)
    return twist(accum, turn_real[:, :, None], turn_imag[:, :, None])


def within_block(data, direction):
    leading, length, lane_count = (data.shape[1], data.shape[2], data.shape[3])
    first_len = math.gcd(length, 256)
    second_len = length // first_len
    data = data.reshape(2, leading, second_len, first_len, lane_count)
    outer_index = jnp.arange(second_len, dtype=jnp.int32)
    inner_index = jnp.arange(first_len, dtype=jnp.int32)
    table_real, table_imag = rotation(outer_index, outer_index, second_len, direction)
    section = contract("pqkj,qxjbc->pxkbc", complex_table(table_real, table_imag), data)
    turn_real, turn_imag = rotation(outer_index, inner_index, length, direction)
    twisted = twist(section, turn_real[None, :, :, None], turn_imag[None, :, :, None])
    last_real, last_imag = rotation(inner_index, inner_index, first_len, direction)
    result = contract("pqgb,qxkbc->pxgkc", complex_table(last_real, last_imag), twisted)
    return result.reshape(2, leading, length, lane_count)


def across_inverse(data, fft_len):
    block_count = data.shape[1] // 2
    block_order = jnp.arange(block_count, dtype=jnp.int32)
    frequency = jnp.arange(2 * block_count, dtype=jnp.int32)
    cos_table, sin_table = rotation(block_order, frequency, 2 * block_count, 1.0)
    summed = contract("qjk,qkbc->jbc", jnp.stack([cos_table, -sin_table]), data)
    return summed * (1.0 / fft_len)


def per_device(projected, conv_weight, skip_gain, spectrum_real, spectrum_imag):
    channels = conv_weight.shape[1] // 3
    rim_rows = conv_weight.shape[0] - 1
    row_count = projected.shape[0]
    rim = shifted(projected[row_count - rim_rows :], ("ctx", "grp"), 1)
    extended = jnp.concatenate([rim, projected], axis=0)
    short = jnp.zeros((row_count, 3 * channels), jnp.float32)
    for offset in range(rim_rows + 1):
        short = short + conv_weight[offset] * extended[
            rim_rows - offset : rim_rows - offset + row_count
        ].astype(jnp.float32)
    short = short.astype(jnp.bfloat16)
    query = short[:, :channels]
    gated = short[:, channels : 2 * channels].astype(jnp.float32) * short[:, 2 * channels :].astype(
        jnp.float32
    )
    block_count = lax.axis_size("ctx")
    group_count = lax.axis_size("grp")
    block_len = row_count * group_count
    fft_len = 2 * block_len * block_count
    block_index = lax.axis_index("ctx")
    sliver = lax.all_to_all(gated, "grp", split_axis=1, concat_axis=0, tiled=True)
    piece_len = block_len // block_count
    token_index = block_index * piece_len + jnp.arange(piece_len, dtype=jnp.int32)
    front = across_forward(
        lax.all_to_all(sliver[None], "ctx", split_axis=1, concat_axis=0, tiled=True),
        token_index,
        fft_len,
    )
    spectra = within_block(
        lax.all_to_all(front, "ctx", split_axis=1, concat_axis=2, tiled=True), -1.0
    )
    filtered = twist(spectra, spectrum_real.astype(jnp.float32), spectrum_imag.astype(jnp.float32))
    restored = within_block(filtered, 1.0)
    local_freq = spectra.shape[1]
    frequency = block_index * local_freq + jnp.arange(local_freq, dtype=jnp.int32)
    turn_real, turn_imag = rotation(frequency, jnp.arange(block_len, dtype=jnp.int32), fft_len, 1.0)
    restored = twist(restored, turn_real[:, :, None], turn_imag[:, :, None])
    long_blocks = across_inverse(
        lax.all_to_all(restored, "ctx", split_axis=2, concat_axis=1, tiled=True), fft_len
    )
    long_sliver = lax.all_to_all(long_blocks, "ctx", split_axis=0, concat_axis=1, tiled=True)[0]
    long_tokens = lax.all_to_all(long_sliver, "grp", split_axis=0, concat_axis=1, tiled=True)
    mixed = query.astype(jnp.float32) * (long_tokens + skip_gain * gated)
    return mixed.astype(jnp.bfloat16)


def short_convolution(projected, conv_weight):
    channels = conv_weight.shape[1] // 3
    rim_rows = conv_weight.shape[0] - 1
    row_count = projected.shape[0]
    rim = shifted(projected[row_count - rim_rows :], ("ctx", "grp"), 1)
    extended = jnp.concatenate([rim, projected], axis=0)
    short = jnp.zeros((row_count, 3 * channels), jnp.float32)
    for offset in range(rim_rows + 1):
        short = short + conv_weight[offset] * extended[
            rim_rows - offset : rim_rows - offset + row_count
        ].astype(jnp.float32)
    short = short.astype(jnp.bfloat16)
    query = short[:, :channels]
    gated = short[:, channels : 2 * channels].astype(jnp.float32) * short[:, 2 * channels :].astype(
        jnp.float32
    )
    return query, gated


def angle_table(rows_index, cols_index, length):
    product = rows_index[:, None] * cols_index[None, :] % length
    angles = product.astype(jnp.float32) * (TWO_PI / length)
    return jnp.cos(angles), jnp.sin(angles)


def channel_parallel(projected, conv_weight, skip_gain, spectrum_real, spectrum_imag):
    query, gated = short_convolution(projected, conv_weight)
    row_count, channels = gated.shape
    block_count = lax.axis_size("ctx")
    group_count = lax.axis_size("grp")
    devices = block_count * group_count
    block_len = row_count * group_count
    residues = 2 * block_count
    fft_len = residues * block_len
    width = channels // devices
    everyone = ("ctx", "grp")

    outgoing = gated.reshape(row_count, group_count, block_count, width).transpose(0, 2, 1, 3)
    outgoing = outgoing.reshape(row_count, devices, width)
    outgoing = outgoing.astype(jnp.bfloat16)
    tokens = lax.all_to_all(outgoing, everyone, split_axis=1, concat_axis=0, tiled=True)
    tokens = tokens.reshape(block_count, block_len, width).astype(jnp.float32)

    tokens, spectrum = lax.optimization_barrier((tokens, jnp.stack([spectrum_real, spectrum_imag])))
    spectrum = lax.all_to_all(spectrum, "ctx", split_axis=3, concat_axis=1, tiled=True)
    spectrum = spectrum.transpose(0, 2, 3, 1).astype(jnp.float32)
    filter_real, filter_imag = spectrum[0], spectrum[1]

    residue = jnp.arange(residues, dtype=jnp.int32)
    block_order = jnp.arange(block_count, dtype=jnp.int32)
    position = jnp.arange(block_len, dtype=jnp.int32)

    across_cos, across_sin = angle_table(block_order, residue, residues)
    folded_real = contract_high("jpc,ja->pca", tokens, across_cos)
    folded_imag = -contract_high("jpc,ja->pca", tokens, across_sin)
    turn_cos, turn_sin = angle_table(position, residue, fft_len)
    turn_cos, turn_sin = turn_cos[:, None, :], turn_sin[:, None, :]
    twisted_real = folded_real * turn_cos + folded_imag * turn_sin
    twisted_imag = folded_imag * turn_cos - folded_real * turn_sin

    within_cos, within_sin = angle_table(position, position, block_len)
    lanes = width * residues

    def times(table_part, data, precision=lax.Precision.HIGH):
        return lax.dot_general(
            table_part,
            data.reshape(block_len, lanes),
            (((1,), (0,)), ((), ())),
            precision=precision,
            preferred_element_type=jnp.float32,
        ).reshape(block_len, width, residues)

    def inverse(table_part, data):
        return times(table_part, data, lax.Precision.DEFAULT)

    spectra_real = times(within_cos, twisted_real) + times(within_sin, twisted_imag)
    spectra_imag = times(within_cos, twisted_imag) - times(within_sin, twisted_real)
    product_real = spectra_real * filter_real - spectra_imag * filter_imag
    product_imag = spectra_real * filter_imag + spectra_imag * filter_real
    product = jnp.concatenate(
        [product_real.reshape(block_len, lanes), product_imag.reshape(block_len, lanes)], axis=0
    ).astype(jnp.bfloat16)

    def inverse_part(left, right):
        return lax.dot_general(
            jnp.concatenate([left, right], axis=1),
            product,
            (((1,), (0,)), ((), ())),
            precision=lax.Precision.DEFAULT,
            preferred_element_type=jnp.float32,
        ).reshape(block_len, width, residues)

    restored_real = inverse_part(within_cos, -within_sin)
    restored_imag = inverse_part(within_sin, within_cos)
    unturned_real = restored_real * turn_cos - restored_imag * turn_sin
    unturned_imag = restored_real * turn_sin + restored_imag * turn_cos
    long_blocks = contract_high("ja,pca->jpc", across_cos, unturned_real) - contract_high(
        "ja,pca->jpc", across_sin, unturned_imag
    )
    long_blocks = (long_blocks * (1.0 / fft_len)).reshape(devices, row_count, width)
    long_blocks = long_blocks.astype(jnp.bfloat16)
    returned = lax.all_to_all(long_blocks, everyone, split_axis=0, concat_axis=0, tiled=True)
    returned = returned.astype(jnp.float32)
    returned = returned.reshape(block_count, group_count, row_count, width).transpose(2, 1, 0, 3)
    long_tokens = returned.reshape(row_count, channels)
    mixed = query.astype(jnp.float32) * (long_tokens + skip_gain * gated)
    return mixed.astype(jnp.bfloat16)


def solution(mesh):
    in_specs = (P(("ctx", "grp"), None), P(), P(), P("ctx", None, "grp"), P("ctx", None, "grp"))
    out_specs = P(("ctx", "grp"), None)
    devices = mesh.shape["ctx"] * mesh.shape["grp"]

    def run(projected, conv_weight, skip_gain, spectrum_real, spectrum_imag):
        channels = conv_weight.shape[1] // 3
        wide = channels % devices == 0 and channels // devices >= 32
        body = channel_parallel if wide else per_device
        return jax.shard_map(
            body, mesh=mesh, in_specs=in_specs, out_specs=out_specs, check_vma=False
        )(projected, conv_weight, skip_gain, spectrum_real, spectrum_imag)

    return run
```

```python
import math

import jax
import jax.numpy as jnp
from jax import lax
from jax.sharding import PartitionSpec as P

TWO_PI = 2.0 * math.pi


def shifted(shard, axis, by):
    devices = lax.axis_size(axis)
    pairs = [(i, i + by) for i in range(devices) if 0 <= i + by < devices]
    return lax.ppermute(shard, axis, pairs)


def rotation(rows_index, cols_index, length, direction):
    product = rows_index[:, None] * cols_index[None, :] % length
    angles = product.astype(jnp.float32) * (TWO_PI / length)
    return (jnp.cos(angles), direction * jnp.sin(angles))


def complex_table(cos_part, sin_part):
    return jnp.stack([jnp.stack([cos_part, -sin_part]), jnp.stack([sin_part, cos_part])])


def contract(form, table, data, precision=lax.Precision.HIGHEST):
    return jnp.einsum(form, table, data, precision=precision, preferred_element_type=jnp.float32)


def contract_high(form, table, data):
    return contract(form, table, data, lax.Precision.HIGH)


def twist(data, turn_real, turn_imag):
    return jnp.stack(
        [data[0] * turn_real - data[1] * turn_imag, data[0] * turn_imag + data[1] * turn_real]
    )


def across_forward(blocks, token_index, fft_len):
    block_count = blocks.shape[0]
    frequency = jnp.arange(2 * block_count, dtype=jnp.int32)
    block_order = jnp.arange(block_count, dtype=jnp.int32)
    cos_table, sin_table = rotation(frequency, block_order, 2 * block_count, -1.0)
    accum = contract("pkj,jbc->pkbc", jnp.stack([cos_table, sin_table]), blocks)
    turn_real, turn_imag = rotation(frequency, token_index, fft_len, -1.0)
    return twist(accum, turn_real[:, :, None], turn_imag[:, :, None])


def within_block(data, direction):
    leading, length, lane_count = (data.shape[1], data.shape[2], data.shape[3])
    first_len = math.gcd(length, 256)
    second_len = length // first_len
    data = data.reshape(2, leading, second_len, first_len, lane_count)
    outer_index = jnp.arange(second_len, dtype=jnp.int32)
    inner_index = jnp.arange(first_len, dtype=jnp.int32)
    table_real, table_imag = rotation(outer_index, outer_index, second_len, direction)
    section = contract("pqkj,qxjbc->pxkbc", complex_table(table_real, table_imag), data)
    turn_real, turn_imag = rotation(outer_index, inner_index, length, direction)
    twisted = twist(section, turn_real[None, :, :, None], turn_imag[None, :, :, None])
    last_real, last_imag = rotation(inner_index, inner_index, first_len, direction)
    result = contract("pqgb,qxkbc->pxgkc", complex_table(last_real, last_imag), twisted)
    return result.reshape(2, leading, length, lane_count)


def across_inverse(data, fft_len):
    block_count = data.shape[1] // 2
    block_order = jnp.arange(block_count, dtype=jnp.int32)
    frequency = jnp.arange(2 * block_count, dtype=jnp.int32)
    cos_table, sin_table = rotation(block_order, frequency, 2 * block_count, 1.0)
    summed = contract("qjk,qkbc->jbc", jnp.stack([cos_table, -sin_table]), data)
    return summed * (1.0 / fft_len)


def per_device(projected, conv_weight, skip_gain, spectrum_real, spectrum_imag):
    channels = conv_weight.shape[1] // 3
    rim_rows = conv_weight.shape[0] - 1
    row_count = projected.shape[0]
    rim = shifted(projected[row_count - rim_rows :], ("ctx", "grp"), 1)
    extended = jnp.concatenate([rim, projected], axis=0)
    short = jnp.zeros((row_count, 3 * channels), jnp.float32)
    for offset in range(rim_rows + 1):
        short = short + conv_weight[offset] * extended[
            rim_rows - offset : rim_rows - offset + row_count
        ].astype(jnp.float32)
    short = short.astype(jnp.bfloat16)
    query = short[:, :channels]
    gated = short[:, channels : 2 * channels].astype(jnp.float32) * short[:, 2 * channels :].astype(
        jnp.float32
    )
    block_count = lax.axis_size("ctx")
    group_count = lax.axis_size("grp")
    block_len = row_count * group_count
    fft_len = 2 * block_len * block_count
    block_index = lax.axis_index("ctx")
    sliver = lax.all_to_all(gated, "grp", split_axis=1, concat_axis=0, tiled=True)
    piece_len = block_len // block_count
    token_index = block_index * piece_len + jnp.arange(piece_len, dtype=jnp.int32)
    front = across_forward(
        lax.all_to_all(sliver[None], "ctx", split_axis=1, concat_axis=0, tiled=True),
        token_index,
        fft_len,
    )
    spectra = within_block(
        lax.all_to_all(front, "ctx", split_axis=1, concat_axis=2, tiled=True), -1.0
    )
    filtered = twist(spectra, spectrum_real.astype(jnp.float32), spectrum_imag.astype(jnp.float32))
    restored = within_block(filtered, 1.0)
    local_freq = spectra.shape[1]
    frequency = block_index * local_freq + jnp.arange(local_freq, dtype=jnp.int32)
    turn_real, turn_imag = rotation(frequency, jnp.arange(block_len, dtype=jnp.int32), fft_len, 1.0)
    restored = twist(restored, turn_real[:, :, None], turn_imag[:, :, None])
    long_blocks = across_inverse(
        lax.all_to_all(restored, "ctx", split_axis=2, concat_axis=1, tiled=True), fft_len
    )
    long_sliver = lax.all_to_all(long_blocks, "ctx", split_axis=0, concat_axis=1, tiled=True)[0]
    long_tokens = lax.all_to_all(long_sliver, "grp", split_axis=0, concat_axis=1, tiled=True)
    mixed = query.astype(jnp.float32) * (long_tokens + skip_gain * gated)
    return mixed.astype(jnp.bfloat16)


def short_convolution(projected, conv_weight):
    channels = conv_weight.shape[1] // 3
    rim_rows = conv_weight.shape[0] - 1
    row_count = projected.shape[0]
    rim = shifted(projected[row_count - rim_rows :], ("ctx", "grp"), 1)
    extended = jnp.concatenate([rim, projected], axis=0)
    short = jnp.zeros((row_count, 3 * channels), jnp.float32)
    for offset in range(rim_rows + 1):
        short = short + conv_weight[offset] * extended[
            rim_rows - offset : rim_rows - offset + row_count
        ].astype(jnp.float32)
    short = short.astype(jnp.bfloat16)
    query = short[:, :channels]
    gated = short[:, channels : 2 * channels].astype(jnp.float32) * short[:, 2 * channels :].astype(
        jnp.float32
    )
    return query, gated


def angle_table(rows_index, cols_index, length):
    product = rows_index[:, None] * cols_index[None, :] % length
    angles = product.astype(jnp.float32) * (TWO_PI / length)
    return jnp.cos(angles), jnp.sin(angles)


def channel_parallel(projected, conv_weight, skip_gain, spectrum_real, spectrum_imag):
    query, gated = short_convolution(projected, conv_weight)
    row_count, channels = gated.shape
    block_count = lax.axis_size("ctx")
    group_count = lax.axis_size("grp")
    devices = block_count * group_count
    block_len = row_count * group_count
    residues = 2 * block_count
    fft_len = residues * block_len
    width = channels // devices
    everyone = ("ctx", "grp")

    outgoing = gated.reshape(row_count, group_count, block_count, width).transpose(0, 2, 1, 3)
    outgoing = outgoing.reshape(row_count, devices, width)
    outgoing = outgoing.astype(jnp.bfloat16)
    tokens = lax.all_to_all(outgoing, everyone, split_axis=1, concat_axis=0, tiled=True)
    tokens = tokens.reshape(block_count, block_len, width).astype(jnp.float32)

    tokens, spectrum = lax.optimization_barrier((tokens, jnp.stack([spectrum_real, spectrum_imag])))
    spectrum = lax.all_to_all(spectrum, "ctx", split_axis=3, concat_axis=1, tiled=True)
    spectrum = spectrum.transpose(0, 2, 3, 1)
    filter_real, filter_imag = spectrum[0], spectrum[1]

    residue = jnp.arange(residues, dtype=jnp.int32)
    block_order = jnp.arange(block_count, dtype=jnp.int32)
    position = jnp.arange(block_len, dtype=jnp.int32)

    across_cos, across_sin = angle_table(block_order, residue, residues)
    folded_real = contract_high("jpc,ja->pca", tokens, across_cos)
    folded_imag = -contract_high("jpc,ja->pca", tokens, across_sin)
    turn_cos, turn_sin = angle_table(position, residue, fft_len)
    turn_cos, turn_sin = turn_cos[:, None, :], turn_sin[:, None, :]
    twisted_real = folded_real * turn_cos + folded_imag * turn_sin
    twisted_imag = folded_imag * turn_cos - folded_real * turn_sin

    within_cos, within_sin = angle_table(position, position, block_len)
    lanes = width * residues

    def times(table_part, data, precision=lax.Precision.HIGH):
        return lax.dot_general(
            table_part,
            data.reshape(block_len, lanes),
            (((1,), (0,)), ((), ())),
            precision=precision,
            preferred_element_type=jnp.float32,
        ).reshape(block_len, width, residues)

    def inverse(table_part, data):
        return times(table_part, data, lax.Precision.DEFAULT)

    spectra_real = times(within_cos, twisted_real) + times(within_sin, twisted_imag)
    spectra_imag = times(within_cos, twisted_imag) - times(within_sin, twisted_real)
    filter_real, filter_imag = filter_real.astype(jnp.float32), filter_imag.astype(jnp.float32)
    product_real = spectra_real * filter_real - spectra_imag * filter_imag
    product_imag = spectra_real * filter_imag + spectra_imag * filter_real
    product = jnp.concatenate(
        [product_real.reshape(block_len, lanes), product_imag.reshape(block_len, lanes)], axis=0
    ).astype(jnp.bfloat16)

    def inverse_part(left, right):
        return lax.dot_general(
            jnp.concatenate([left, right], axis=1),
            product,
            (((1,), (0,)), ((), ())),
            precision=lax.Precision.DEFAULT,
            preferred_element_type=jnp.float32,
        ).reshape(block_len, width, residues)

    restored_real = inverse_part(within_cos, -within_sin)
    restored_imag = inverse_part(within_sin, within_cos)
    unturned_real = restored_real * turn_cos - restored_imag * turn_sin
    unturned_imag = restored_real * turn_sin + restored_imag * turn_cos
    long_blocks = contract_high("ja,pca->jpc", across_cos, unturned_real) - contract_high(
        "ja,pca->jpc", across_sin, unturned_imag
    )
    long_blocks = (long_blocks * (1.0 / fft_len)).reshape(devices, row_count, width)
    long_blocks = long_blocks.astype(jnp.bfloat16)
    returned = lax.all_to_all(long_blocks, everyone, split_axis=0, concat_axis=0, tiled=True)
    returned = returned.astype(jnp.float32)
    returned = returned.reshape(block_count, group_count, row_count, width).transpose(2, 1, 0, 3)
    long_tokens = returned.reshape(row_count, channels)
    mixed = query.astype(jnp.float32) * (long_tokens + skip_gain * gated)
    return mixed.astype(jnp.bfloat16)


def solution(mesh):
    in_specs = (P(("ctx", "grp"), None), P(), P(), P("ctx", None, "grp"), P("ctx", None, "grp"))
    out_specs = P(("ctx", "grp"), None)
    devices = mesh.shape["ctx"] * mesh.shape["grp"]

    def run(projected, conv_weight, skip_gain, spectrum_real, spectrum_imag):
        channels = conv_weight.shape[1] // 3
        wide = channels % devices == 0 and channels // devices >= 32
        body = channel_parallel if wide else per_device
        return jax.shard_map(
            body, mesh=mesh, in_specs=in_specs, out_specs=out_specs, check_vma=False
        )(projected, conv_weight, skip_gain, spectrum_real, spectrum_imag)

    return run
```

```python
import math

import jax
import jax.numpy as jnp
from jax import lax
from jax.sharding import PartitionSpec as P

TWO_PI = 2.0 * math.pi


def shifted(shard, axis, by):
    devices = lax.axis_size(axis)
    pairs = [(i, i + by) for i in range(devices) if 0 <= i + by < devices]
    return lax.ppermute(shard, axis, pairs)


def rotation(rows_index, cols_index, length, direction):
    product = rows_index[:, None] * cols_index[None, :] % length
    angles = product.astype(jnp.float32) * (TWO_PI / length)
    return (jnp.cos(angles), direction * jnp.sin(angles))


def complex_table(cos_part, sin_part):
    return jnp.stack([jnp.stack([cos_part, -sin_part]), jnp.stack([sin_part, cos_part])])


def contract(form, table, data, precision=lax.Precision.HIGHEST):
    return jnp.einsum(form, table, data, precision=precision, preferred_element_type=jnp.float32)


def contract_high(form, table, data):
    return contract(form, table, data, lax.Precision.HIGH)


def twist(data, turn_real, turn_imag):
    return jnp.stack(
        [data[0] * turn_real - data[1] * turn_imag, data[0] * turn_imag + data[1] * turn_real]
    )


def across_forward(blocks, token_index, fft_len):
    block_count = blocks.shape[0]
    frequency = jnp.arange(2 * block_count, dtype=jnp.int32)
    block_order = jnp.arange(block_count, dtype=jnp.int32)
    cos_table, sin_table = rotation(frequency, block_order, 2 * block_count, -1.0)
    accum = contract("pkj,jbc->pkbc", jnp.stack([cos_table, sin_table]), blocks)
    turn_real, turn_imag = rotation(frequency, token_index, fft_len, -1.0)
    return twist(accum, turn_real[:, :, None], turn_imag[:, :, None])


def within_block(data, direction):
    leading, length, lane_count = (data.shape[1], data.shape[2], data.shape[3])
    first_len = math.gcd(length, 256)
    second_len = length // first_len
    data = data.reshape(2, leading, second_len, first_len, lane_count)
    outer_index = jnp.arange(second_len, dtype=jnp.int32)
    inner_index = jnp.arange(first_len, dtype=jnp.int32)
    table_real, table_imag = rotation(outer_index, outer_index, second_len, direction)
    section = contract("pqkj,qxjbc->pxkbc", complex_table(table_real, table_imag), data)
    turn_real, turn_imag = rotation(outer_index, inner_index, length, direction)
    twisted = twist(section, turn_real[None, :, :, None], turn_imag[None, :, :, None])
    last_real, last_imag = rotation(inner_index, inner_index, first_len, direction)
    result = contract("pqgb,qxkbc->pxgkc", complex_table(last_real, last_imag), twisted)
    return result.reshape(2, leading, length, lane_count)


def across_inverse(data, fft_len):
    block_count = data.shape[1] // 2
    block_order = jnp.arange(block_count, dtype=jnp.int32)
    frequency = jnp.arange(2 * block_count, dtype=jnp.int32)
    cos_table, sin_table = rotation(block_order, frequency, 2 * block_count, 1.0)
    summed = contract("qjk,qkbc->jbc", jnp.stack([cos_table, -sin_table]), data)
    return summed * (1.0 / fft_len)


def per_device(projected, conv_weight, skip_gain, spectrum_real, spectrum_imag):
    channels = conv_weight.shape[1] // 3
    rim_rows = conv_weight.shape[0] - 1
    row_count = projected.shape[0]
    rim = shifted(projected[row_count - rim_rows :], ("ctx", "grp"), 1)
    extended = jnp.concatenate([rim, projected], axis=0)
    short = jnp.zeros((row_count, 3 * channels), jnp.float32)
    for offset in range(rim_rows + 1):
        short = short + conv_weight[offset] * extended[
            rim_rows - offset : rim_rows - offset + row_count
        ].astype(jnp.float32)
    short = short.astype(jnp.bfloat16)
    query = short[:, :channels]
    gated = short[:, channels : 2 * channels].astype(jnp.float32) * short[:, 2 * channels :].astype(
        jnp.float32
    )
    block_count = lax.axis_size("ctx")
    group_count = lax.axis_size("grp")
    block_len = row_count * group_count
    fft_len = 2 * block_len * block_count
    block_index = lax.axis_index("ctx")
    sliver = lax.all_to_all(gated, "grp", split_axis=1, concat_axis=0, tiled=True)
    piece_len = block_len // block_count
    token_index = block_index * piece_len + jnp.arange(piece_len, dtype=jnp.int32)
    front = across_forward(
        lax.all_to_all(sliver[None], "ctx", split_axis=1, concat_axis=0, tiled=True),
        token_index,
        fft_len,
    )
    spectra = within_block(
        lax.all_to_all(front, "ctx", split_axis=1, concat_axis=2, tiled=True), -1.0
    )
    filtered = twist(spectra, spectrum_real.astype(jnp.float32), spectrum_imag.astype(jnp.float32))
    restored = within_block(filtered, 1.0)
    local_freq = spectra.shape[1]
    frequency = block_index * local_freq + jnp.arange(local_freq, dtype=jnp.int32)
    turn_real, turn_imag = rotation(frequency, jnp.arange(block_len, dtype=jnp.int32), fft_len, 1.0)
    restored = twist(restored, turn_real[:, :, None], turn_imag[:, :, None])
    long_blocks = across_inverse(
        lax.all_to_all(restored, "ctx", split_axis=2, concat_axis=1, tiled=True), fft_len
    )
    long_sliver = lax.all_to_all(long_blocks, "ctx", split_axis=0, concat_axis=1, tiled=True)[0]
    long_tokens = lax.all_to_all(long_sliver, "grp", split_axis=0, concat_axis=1, tiled=True)
    mixed = query.astype(jnp.float32) * (long_tokens + skip_gain * gated)
    return mixed.astype(jnp.bfloat16)


def short_convolution(projected, conv_weight):
    channels = conv_weight.shape[1] // 3
    rim_rows = conv_weight.shape[0] - 1
    row_count = projected.shape[0]
    rim = shifted(projected[row_count - rim_rows :], ("ctx", "grp"), 1)
    extended = jnp.concatenate([rim, projected], axis=0)
    short = jnp.zeros((row_count, 3 * channels), jnp.float32)
    for offset in range(rim_rows + 1):
        short = short + conv_weight[offset] * extended[
            rim_rows - offset : rim_rows - offset + row_count
        ].astype(jnp.float32)
    short = short.astype(jnp.bfloat16)
    query = short[:, :channels]
    gated = short[:, channels : 2 * channels].astype(jnp.float32) * short[:, 2 * channels :].astype(
        jnp.float32
    )
    return query, gated


def angle_table(rows_index, cols_index, length):
    product = rows_index[:, None] * cols_index[None, :] % length
    angles = product.astype(jnp.float32) * (TWO_PI / length)
    return jnp.cos(angles), jnp.sin(angles)


def channel_parallel(projected, conv_weight, skip_gain, spectrum_real, spectrum_imag):
    query, gated = short_convolution(projected, conv_weight)
    row_count, channels = gated.shape
    block_count = lax.axis_size("ctx")
    group_count = lax.axis_size("grp")
    devices = block_count * group_count
    block_len = row_count * group_count
    residues = 2 * block_count
    fft_len = residues * block_len
    width = channels // devices
    everyone = ("ctx", "grp")

    outgoing = gated.reshape(row_count, group_count, block_count, width).transpose(0, 2, 1, 3)
    outgoing = outgoing.reshape(row_count, devices, width)
    outgoing = outgoing.astype(jnp.bfloat16)
    tokens = lax.all_to_all(outgoing, everyone, split_axis=1, concat_axis=0, tiled=True)
    tokens = tokens.reshape(block_count, block_len, width).astype(jnp.float32)

    tokens, spectrum = lax.optimization_barrier((tokens, jnp.stack([spectrum_real, spectrum_imag])))
    spectrum = lax.all_to_all(spectrum, "ctx", split_axis=3, concat_axis=1, tiled=True)
    spectrum = spectrum.transpose(0, 2, 3, 1).astype(jnp.float32)
    filter_real, filter_imag = spectrum[0], spectrum[1]

    residue = jnp.arange(residues, dtype=jnp.int32)
    block_order = jnp.arange(block_count, dtype=jnp.int32)
    position = jnp.arange(block_len, dtype=jnp.int32)

    across_cos, across_sin = angle_table(block_order, residue, residues)
    folded_real = contract_high("jpc,ja->pca", tokens, across_cos)
    folded_imag = -contract_high("jpc,ja->pca", tokens, across_sin)
    turn_cos, turn_sin = angle_table(position, residue, fft_len)
    turn_cos, turn_sin = turn_cos[:, None, :], turn_sin[:, None, :]
    twisted_real = folded_real * turn_cos + folded_imag * turn_sin
    twisted_imag = folded_imag * turn_cos - folded_real * turn_sin

    within_cos, within_sin = angle_table(position, position, block_len)
    lanes = width * residues

    def times(table_part, data, precision=lax.Precision.HIGH):
        return lax.dot_general(
            table_part,
            data.reshape(block_len, lanes),
            (((1,), (0,)), ((), ())),
            precision=precision,
            preferred_element_type=jnp.float32,
        ).reshape(block_len, width, residues)

    def inverse(table_part, data):
        return times(table_part, data, lax.Precision.DEFAULT)

    spectra_real = times(within_cos, twisted_real) + times(within_sin, twisted_imag)
    spectra_imag = times(within_cos, twisted_imag) - times(within_sin, twisted_real)
    product_real = spectra_real * filter_real - spectra_imag * filter_imag
    product_imag = spectra_real * filter_imag + spectra_imag * filter_real
    product = jnp.concatenate(
        [product_real.reshape(block_len, lanes), product_imag.reshape(block_len, lanes)], axis=0
    ).astype(jnp.bfloat16)

    def inverse_part(left, right):
        return lax.dot_general(
            jnp.concatenate([left, right], axis=1),
            product,
            (((1,), (0,)), ((), ())),
            precision=lax.Precision.DEFAULT,
            preferred_element_type=jnp.float32,
        ).reshape(block_len, width, residues)

    restored_real = inverse_part(within_cos, -within_sin)
    restored_imag = inverse_part(within_sin, within_cos)
    unturned_real = restored_real * turn_cos - restored_imag * turn_sin
    unturned_imag = restored_real * turn_sin + restored_imag * turn_cos
    long_blocks = contract("ja,pca->jpc", across_cos, unturned_real, lax.Precision.DEFAULT) - contract(
        "ja,pca->jpc", across_sin, unturned_imag, lax.Precision.DEFAULT
    )
    long_blocks = (long_blocks * (1.0 / fft_len)).reshape(devices, row_count, width)
    long_blocks = long_blocks.astype(jnp.bfloat16)
    returned = lax.all_to_all(long_blocks, everyone, split_axis=0, concat_axis=0, tiled=True)
    returned = returned.astype(jnp.float32)
    returned = returned.reshape(block_count, group_count, row_count, width).transpose(2, 1, 0, 3)
    long_tokens = returned.reshape(row_count, channels)
    mixed = query.astype(jnp.float32) * (long_tokens + skip_gain * gated)
    return mixed.astype(jnp.bfloat16)


def solution(mesh):
    in_specs = (P(("ctx", "grp"), None), P(), P(), P("ctx", None, "grp"), P("ctx", None, "grp"))
    out_specs = P(("ctx", "grp"), None)
    devices = mesh.shape["ctx"] * mesh.shape["grp"]

    def run(projected, conv_weight, skip_gain, spectrum_real, spectrum_imag):
        channels = conv_weight.shape[1] // 3
        wide = channels % devices == 0 and channels // devices >= 32
        body = channel_parallel if wide else per_device
        return jax.shard_map(
            body, mesh=mesh, in_specs=in_specs, out_specs=out_specs, check_vma=False
        )(projected, conv_weight, skip_gain, spectrum_real, spectrum_imag)

    return run
```
